32 devices in a mesh: groups: 2 (over x), seq: 16 (over z, y, core).
Axes of the slice: x: 2, y: 2, z: 4, core: 2. Of those that a mesh axis runs over, the one named last changes fastest.
Arguments:
- query: bfloat16 [4096, 1024], P(('groups', 'seq')), parts along dimension 0, as said below
- keys: bfloat16 [4096, 1024], P(('groups', 'seq')), parts along dimension 0, as said below
- values: bfloat16 [4096, 1024], P(('groups', 'seq')), parts along dimension 0, may hold values from -6 to 6
- out_weight: bfloat16 [1024, 2048], P('seq'), may hold values from -0.1875 to 0.1875
- grad_out: bfloat16 [4096, 2048], P(('groups', 'seq')), parts along dimension 0, may hold values from -6 to 6
- global_blocks: int32 [4], P('groups'), parts along dimension 0, may hold values from 0 to 15
- random_blocks: int32 [32, 3], P(('groups', 'seq')), parts along dimension 0, may hold values from 0 to 15, as said below
Outputs:
- layer_out: bfloat16 [4096, 2048], P(('groups', 'seq')), parts along dimension 0
- grad_query: bfloat16 [4096, 1024], P(('groups', 'seq')), parts along dimension 0
- grad_keys: bfloat16 [4096, 1024], P(('groups', 'seq')), parts along dimension 0
- grad_values: bfloat16 [4096, 1024], P(('groups', 'seq')), parts along dimension 0
- grad_weight: float32 [2048, 2048], P(('groups', 'seq')), parts along dimension 0
The draws below stay inside these ranges and needn't reach their ends.
There are 2 independent parts, one for each index of `groups`. The reference program is written for one: setup_inputs(seed, part) draws one part's arguments, and reference() takes and returns one part's arrays. A program takes and returns all parts, laid end to end along the dimension named above; an argument that names none is the same for every part. Nothing has to cross between parts.
Inputs may be any that keep to these rules, and one draw needn't show every extreme that they name: `random_blocks`: random block r of query block b lies on the device that holds b or on a device beside it: it is at least max(b - 1, 0) * 1 and below min(b + 2, 16). `query`: entries lie between -12 and 12. `keys`: entries lie between -6 and 6.
All inputs are finite; a program needn't handle non-finite values.
Results may differ from the reference program's by a relative error of at most 0.012.
Values may be sent and summed in bfloat16 or wider, within the bound.
No kernel may reach another device: no remote copies, remote signals or barrier semaphores. Data moves between devices by JAX's collectives and lax.ppermute only.
A program may use at most 128 MiB of HBM per device.

```python
import math
import jax
import jax.numpy as jnp
from jax import lax

D = 2048
H = 8
HD = 128
BLK = 128
R = 3
G = 2
TOK_DEV = 128
BLK_DEV = 1
NB = 16
TOKENS = 2048


def drawn_pair(key):
    base = jax.random.fold_in(key, 17)
    query_key, keys_key = jax.random.split(base, 2)
    shape = (TOKENS, H * HD)
    query_draw = 2.0 * jnp.clip(jax.random.normal(query_key, shape, jnp.float32), -6.0, 6.0)
    keys_draw = jnp.clip(jax.random.normal(keys_key, shape, jnp.float32), -6.0, 6.0)
    return (query_draw, keys_draw)


def draw_query(key, part):
    return drawn_pair(key)[0].astype(jnp.bfloat16)


def draw_keys(key, part):
    return drawn_pair(key)[1].astype(jnp.bfloat16)


def draw_random_blocks(key, part):
    block_ids = jnp.arange(NB, dtype=jnp.int32)
    devices_total = NB // BLK_DEV
    device = block_ids // BLK_DEV
    lowest = jnp.maximum(device - 1, 0) * BLK_DEV
    ceiling = jnp.minimum(device + 2, devices_total) * BLK_DEV
    drawn = jax.random.randint(jax.random.fold_in(key, 29), (NB, R), lowest[:, None], ceiling[:, None], jnp.int32)
    drawn = drawn.at[0, 0].set(jnp.int32(0))
    drawn = drawn.at[NB - 1, 0].set(jnp.int32(NB - 1))
    return drawn


def shard_levels(rng, extent, pieces, low, largest):
    def one(dim, parts):
        draws = jax.random.uniform(jax.random.fold_in(jax.random.fold_in(rng, 6), dim), (parts,), jnp.float32, low / len(pieces), largest / len(pieces))
        return jnp.repeat(jnp.exp(draws), extent[dim] // parts).reshape((-1,) + (1,) * (len(extent) - dim - 1))

    loudness = one(*pieces[0])
    for cut in pieces[1:]:
        loudness = loudness * one(*cut)
    return loudness


def centred(key, shape, spread, limit, pieces=(), kind=jnp.bfloat16):
    values = spread * jax.random.normal(key, shape, jnp.float32)
    if pieces:
        values = values * shard_levels(key, shape, pieces, -0.22, 0.18)
    return jnp.clip(values, -limit, limit).astype(kind)


def setup_inputs(seed: int = 0, part: int = 0) -> dict:
    splits = jax.random.split(jax.random.key(seed), 8)
    own_keys = jax.random.split(jax.random.fold_in(splits[7], part), 8)
    query = draw_query(jax.random.fold_in(jax.random.fold_in(splits[7], part), 71), part)
    keys = draw_keys(jax.random.fold_in(jax.random.fold_in(splits[7], part), 71), part)
    values = centred(own_keys[2], (TOKENS, H * HD), 1.0, 6.0, ((0, 16),))
    out_weight = centred(splits[3], (H * HD, D), (H * HD) ** -0.5, 0.1875, ((0, 16),))
    grad_out = centred(own_keys[4], (TOKENS, D), 1.0, 6.0, ((0, 16),))
    global_blocks = jax.random.randint(own_keys[5], (G,), 0, NB).astype(jnp.int32)
    random_blocks = draw_random_blocks(jax.random.fold_in(jax.random.fold_in(splits[7], part), 71), part)
    return dict(query=query, keys=keys, values=values, out_weight=out_weight, grad_out=grad_out, global_blocks=global_blocks, random_blocks=random_blocks)


NEG_FILL = -1e+30

def window_and_random(random_rows, device, blocks_dev, total_blocks):
    local_ids = jnp.arange(blocks_dev, dtype=jnp.int32)
    global_ids = device * blocks_dev + local_ids
    offsets = jnp.array([-1, 0, 1], dtype=jnp.int32)
    neighbour_ids = global_ids[:, None] + offsets[None, :]
    window_index = local_ids[:, None] + blocks_dev + offsets[None, :]
    window_live = (neighbour_ids >= 0) & (neighbour_ids < total_blocks)
    random_index = random_rows.astype(jnp.int32) - (device - 1) * blocks_dev
    ext_index = jnp.concatenate([window_index, random_index.astype(jnp.int32)], axis=1)
    live_local = jnp.concatenate([window_live, jnp.ones(random_rows.shape, dtype=jnp.bool_)], axis=1)
    return (ext_index, live_local)

def choose_blocks(extended, global_kv, ext_index, live_local, blocks_dev):
    feature_count = extended.shape[2]
    ext_blocks = extended.reshape(2, 3 * blocks_dev, BLK, feature_count)
    local_sel = jnp.take(ext_blocks, ext_index, axis=1)
    global_count = global_kv.shape[0]
    global_sel = jnp.broadcast_to(jnp.swapaxes(global_kv, 0, 1)[:, None], (2, blocks_dev, global_count, BLK, feature_count))
    chosen = jnp.concatenate([local_sel, global_sel], axis=2)
    listed = chosen.shape[2]
    chosen = chosen.reshape(2, blocks_dev, listed * BLK, H, feature_count // H)
    live = jnp.concatenate([live_local, jnp.ones((blocks_dev, global_count), dtype=jnp.bool_)], axis=1)
    live_rows = jnp.repeat(live, BLK, axis=1)
    return (chosen[0], chosen[1], live_rows)

def attend_blocks(query_blocks, chosen_keys, chosen_values, live_rows):
    score_scale = 1.0 / math.sqrt(query_blocks.shape[-1])
    scores = jnp.einsum('qihd,qjhd->qhij', query_blocks.astype(jnp.float32), chosen_keys.astype(jnp.float32)) * score_scale
    scores = jnp.where(live_rows[:, None, None, :], scores, NEG_FILL)
    row_top = lax.optimization_barrier(jnp.max(scores, axis=-1, keepdims=True))
    raised = jnp.exp(scores - row_top)
    soft_weights = raised / lax.optimization_barrier(jnp.sum(raised, axis=-1, keepdims=True))
    rounded_weights = soft_weights.astype(jnp.bfloat16)
    mixed_out = jnp.einsum('qhij,qjhd->qihd', rounded_weights.astype(jnp.float32), chosen_values.astype(jnp.float32))
    return (soft_weights, rounded_weights, mixed_out.astype(jnp.bfloat16))

def attend_backward(query_blocks, chosen_keys, chosen_values, soft_weights, rounded_weights, upstream_blocks):
    score_scale = 1.0 / math.sqrt(query_blocks.shape[-1])
    upstream_f = upstream_blocks.astype(jnp.float32)
    grad_chosen_values = jnp.einsum('qhij,qihd->qjhd', rounded_weights.astype(jnp.float32), upstream_f)
    grad_weights = jnp.einsum('qihd,qjhd->qhij', upstream_f, chosen_values.astype(jnp.float32))
    row_delta = lax.optimization_barrier(jnp.sum(soft_weights * grad_weights, axis=-1, keepdims=True))
    grad_scores = (score_scale * soft_weights * (grad_weights - row_delta)).astype(jnp.bfloat16)
    grad_query_blocks = jnp.einsum('qhij,qjhd->qihd', grad_scores.astype(jnp.float32), chosen_keys.astype(jnp.float32))
    grad_chosen_keys = jnp.einsum('qhij,qihd->qjhd', grad_scores.astype(jnp.float32), query_blocks.astype(jnp.float32))
    return (grad_query_blocks, grad_chosen_keys, grad_chosen_values)

def fold_gradients(grad_chosen_keys, grad_chosen_values, ext_index, blocks_dev):
    stacked = jnp.stack([grad_chosen_keys, grad_chosen_values])
    listed_local = ext_index.shape[1]
    feature_count = stacked.shape[3] * stacked.shape[4]
    stacked = stacked.reshape(2, blocks_dev, -1, BLK * feature_count)
    local_part = stacked[:, :, :listed_local].reshape(2, blocks_dev * listed_local, BLK * feature_count)
    one_hot = (ext_index.reshape(-1)[:, None] == jnp.arange(3 * blocks_dev, dtype=jnp.int32)[None, :]).astype(jnp.float32)
    grad_ext = jnp.einsum('sj,ksx->kjx', one_hot, local_part, precision=lax.Precision.HIGHEST)
    grad_ext = grad_ext.reshape(2, 3 * blocks_dev * BLK, feature_count)
    grad_global = lax.optimization_barrier(jnp.sum(stacked[:, :, listed_local:], axis=1)).reshape(2, -1, BLK, feature_count)
    return (grad_ext, grad_global)

def reference(query, keys, values, out_weight, grad_out, global_blocks, random_blocks):
    device_count = NB // BLK_DEV
    feature_count = H * HD
    paired = jnp.stack([keys, values])
    padded = jnp.pad(paired, ((0, 0), (TOK_DEV, TOK_DEV), (0, 0)))
    global_kv = jnp.stack([lax.dynamic_slice_in_dim(paired, (global_blocks[global_slot] * BLK).astype(jnp.int32), BLK, 1) for global_slot in range(G)])
    upstream_all = lax.dot_general(grad_out, out_weight, (((1,), (1,)), ((), ())), preferred_element_type=jnp.float32).astype(jnp.bfloat16)

    def per_device(carry, device):
        grad_padded, global_running = carry
        first_row = (device * TOK_DEV).astype(jnp.int32)
        query_dev = lax.dynamic_slice_in_dim(query, first_row, TOK_DEV, 0)
        upstream_dev = lax.dynamic_slice_in_dim(upstream_all, first_row, TOK_DEV, 0)
        extended = lax.dynamic_slice_in_dim(padded, first_row, 3 * TOK_DEV, 1)
        random_rows = lax.dynamic_slice_in_dim(random_blocks, (device * BLK_DEV).astype(jnp.int32), BLK_DEV, 0)
        ext_index, live_local = window_and_random(random_rows, device, BLK_DEV, NB)
        chosen_keys, chosen_values, live_rows = choose_blocks(extended, global_kv, ext_index, live_local, BLK_DEV)
        query_blocks = query_dev.reshape(BLK_DEV, BLK, H, HD)
        soft_weights, rounded_weights, mixed_out = attend_blocks(query_blocks, chosen_keys, chosen_values, live_rows)
        upstream_blocks = upstream_dev.reshape(BLK_DEV, BLK, H, HD)
        grad_query_blocks, grad_chosen_keys, grad_chosen_values = attend_backward(query_blocks, chosen_keys, chosen_values, soft_weights, rounded_weights, upstream_blocks)
        grad_ext, grad_global = fold_gradients(grad_chosen_keys, grad_chosen_values, ext_index, BLK_DEV)
        left_rim = lax.optimization_barrier(grad_ext[:, :TOK_DEV].astype(jnp.bfloat16)).astype(jnp.float32)
        right_rim = lax.optimization_barrier(grad_ext[:, 2 * TOK_DEV:].astype(jnp.bfloat16)).astype(jnp.float32)
        update = jnp.concatenate([left_rim, grad_ext[:, TOK_DEV:2 * TOK_DEV], right_rim], axis=1)
        current = lax.dynamic_slice_in_dim(grad_padded, first_row, 3 * TOK_DEV, 1)
        grad_padded = lax.dynamic_update_slice_in_dim(grad_padded, current + update, first_row, 1)
        outputs = (mixed_out.reshape(TOK_DEV, feature_count), grad_query_blocks.reshape(TOK_DEV, feature_count).astype(jnp.bfloat16))
        return ((grad_padded, global_running + grad_global), outputs)
    initial = (jnp.zeros((2, TOKENS + 2 * TOK_DEV, feature_count), jnp.float32), jnp.zeros((2, G, BLK, feature_count), jnp.float32))
    (grad_padded, global_running), (attn_parts, query_parts) = lax.scan(per_device, initial, jnp.arange(device_count, dtype=jnp.int32))
    attn_out = attn_parts.reshape(TOKENS, feature_count)
    grad_query = query_parts.reshape(TOKENS, feature_count)
    grad_paired = grad_padded[:, TOK_DEV:TOK_DEV + TOKENS]
    for global_slot in range(G):
        start_row = (global_blocks[global_slot] * BLK).astype(jnp.int32)
        current = lax.dynamic_slice_in_dim(grad_paired, start_row, BLK, 1)
        grad_paired = lax.dynamic_update_slice_in_dim(grad_paired, current + global_running[:, global_slot], start_row, 1)
    grad_paired = grad_paired.astype(jnp.bfloat16)
    layer_out = jnp.dot(attn_out, out_weight, preferred_element_type=jnp.float32).astype(jnp.bfloat16)
    grad_weight = lax.dot_general(attn_out, grad_out, (((0,), (0,)), ((), ())), preferred_element_type=jnp.float32)
    return (layer_out, grad_query, grad_paired[0], grad_paired[1], grad_weight)
```

```python
import math

import jax
import jax.numpy as jnp
from jax import lax
from jax.sharding import Mesh
from jax.sharding import PartitionSpec as P

H = 8
BLK = 128
SEQ = ("chip", "core")


NEG_FILL = -1e30


def flat_index():
    return lax.axis_index("chip") * lax.axis_size("core") + lax.axis_index("core")


def xor_swap(x, level):
    if level == 0:
        n = lax.axis_size("core")
        return lax.ppermute(x, "core", [(i, i ^ 1) for i in range(n)])
    n = lax.axis_size("chip")
    m = 1 << (level - 1)
    return lax.ppermute(x, "chip", [(i, i ^ m) for i in range(n)])


def butterfly_sum(x):
    count = lax.axis_size("chip") * lax.axis_size("core")
    levels = count.bit_length() - 1
    shape = x.shape
    flat = x.reshape(count, -1)
    d = flat_index()
    parts = flat
    for k in range(levels):
        half = parts.shape[0] // 2
        lo, hi = parts[:half], parts[half:]
        upper = ((d >> k) & 1) == 1
        send = jnp.where(upper, lo, hi)
        keep = jnp.where(upper, hi, lo)
        parts = keep + xor_swap(send, k)
    for k in reversed(range(levels)):
        upper = ((d >> k) & 1) == 1
        other = xor_swap(parts, k)
        parts = jnp.where(
            upper, jnp.concatenate([other, parts]), jnp.concatenate([parts, other])
        )
    return parts.reshape(shape)


def halo(shard):
    count = lax.axis_size("chip") * lax.axis_size("core")
    up = [(i, i + 1) for i in range(count - 1)]
    down = [(j, i) for i, j in up]
    before = lax.ppermute(shard, SEQ, up)
    after = lax.ppermute(shard, SEQ, down)
    return before, after


def attend(q, k, v, live, up):
    scale = 1.0 / math.sqrt(q.shape[-1])
    scores = jnp.einsum("ihd,jhd->hij", q, k, preferred_element_type=jnp.float32) * scale
    scores = jnp.where(live[None, None, :], scores, NEG_FILL)
    top = jnp.max(scores, axis=-1, keepdims=True)
    raised = jnp.exp(scores - top)
    probs = raised / jnp.sum(raised, axis=-1, keepdims=True)
    probs_b = probs.astype(jnp.bfloat16)
    attn = jnp.einsum("hij,jhd->ihd", probs_b, v, preferred_element_type=jnp.float32)
    attn = attn.astype(jnp.bfloat16)
    return probs, probs_b, attn


def attend_back(q, k, v, probs, probs_b, up):
    scale = 1.0 / math.sqrt(q.shape[-1])
    dv = jnp.einsum("hij,ihd->jhd", probs_b, up, preferred_element_type=jnp.float32)
    dprobs = jnp.einsum("ihd,jhd->hij", up, v, preferred_element_type=jnp.float32)
    rowdot = jnp.sum(probs * dprobs, axis=-1, keepdims=True)
    dscores = (scale * probs * (dprobs - rowdot)).astype(jnp.bfloat16)
    dq = jnp.einsum("hij,jhd->ihd", dscores, k, preferred_element_type=jnp.float32)
    dk = jnp.einsum("hij,ihd->jhd", dscores, q, preferred_element_type=jnp.float32)
    return dq, dk, dv


def local(query, keys, values, out_weight, grad_out, global_blocks, random_blocks):
    tok_rows, feature_count = query.shape
    hd = feature_count // H
    blocks_dev = tok_rows // BLK
    count = lax.axis_size("chip") * lax.axis_size("core")
    total_blocks = blocks_dev * count
    device = flat_index()

    grad_out_all = lax.all_gather(grad_out, SEQ, axis=0, tiled=True)
    weight_all = lax.all_gather(out_weight, SEQ, axis=0, tiled=True)

    paired = jnp.stack([keys, values])
    before, after = halo(paired)
    extended = jnp.concatenate([before, paired, after], axis=1)

    slots = global_blocks.shape[0]
    owners = global_blocks // blocks_dev
    masked = []
    for g in range(slots):
        start = (global_blocks[g] % blocks_dev) * BLK
        block = lax.dynamic_slice_in_dim(paired, start, BLK, axis=1)
        masked.append(jnp.where(owners[g] == device, block, jnp.zeros_like(block)))
    global_kv = butterfly_sum(jnp.stack(masked))

    local_ids = jnp.arange(blocks_dev, dtype=jnp.int32)
    global_ids = device * blocks_dev + local_ids
    offsets = jnp.array([-1, 0, 1], dtype=jnp.int32)
    neighbour_ids = global_ids[:, None] + offsets[None, :]
    window_index = local_ids[:, None] + blocks_dev + offsets[None, :]
    window_live = (neighbour_ids >= 0) & (neighbour_ids < total_blocks)
    random_index = random_blocks - (device - 1) * blocks_dev
    ext_index = jnp.concatenate([window_index, random_index], axis=1)
    n_local = ext_index.shape[1]
    live = jnp.concatenate(
        [window_live, jnp.ones(random_blocks.shape, jnp.bool_), jnp.ones((blocks_dev, slots), jnp.bool_)],
        axis=1,
    )

    upstream = lax.dot_general(
        grad_out, weight_all, (((1,), (1,)), ((), ())), preferred_element_type=jnp.float32
    ).astype(jnp.bfloat16)

    attn_rows, dq_rows, dk_ext, dv_ext = [], [], [], []
    grad_ext = jnp.zeros((2, 3 * blocks_dev * BLK, feature_count), jnp.float32)
    global_terms = []
    for b in range(blocks_dev):
        chosen = [
            lax.dynamic_slice_in_dim(extended, ext_index[b, j] * BLK, BLK, axis=1)
            for j in range(n_local)
        ]
        chosen += [global_kv[g] for g in range(slots)]
        chosen = jnp.concatenate(chosen, axis=1).reshape(2, -1, H, hd)
        live_rows = jnp.repeat(live[b], BLK)
        q = query[b * BLK : (b + 1) * BLK].reshape(BLK, H, hd)
        up = upstream[b * BLK : (b + 1) * BLK].reshape(BLK, H, hd)
        probs, probs_b, attn = attend(q, chosen[0], chosen[1], live_rows, up)
        dq, dk, dv = attend_back(q, chosen[0], chosen[1], probs, probs_b, up)
        attn_rows.append(attn.reshape(BLK, feature_count))
        dq_rows.append(dq.reshape(BLK, feature_count).astype(jnp.bfloat16))
        dkv = jnp.stack([dk, dv]).reshape(2, -1, BLK, feature_count)
        for j in range(n_local):
            start = ext_index[b, j] * BLK
            cur = lax.dynamic_slice_in_dim(grad_ext, start, BLK, axis=1)
            grad_ext = lax.dynamic_update_slice_in_dim(grad_ext, cur + dkv[:, j], start, axis=1)
        global_terms.append(dkv[:, n_local:])
    global_local = global_terms[0]
    for t in global_terms[1:]:
        global_local = global_local + t
    global_total = butterfly_sum(jnp.swapaxes(global_local, 0, 1))

    attn_out = jnp.concatenate(attn_rows, axis=0)
    layer_out = jnp.dot(attn_out, weight_all, preferred_element_type=jnp.float32).astype(
        jnp.bfloat16
    )
    w_rows = out_weight.shape[0]
    attn_cols = lax.all_to_all(
        attn_out.reshape(tok_rows, count, w_rows), SEQ, 1, 0, tiled=False
    ).reshape(count * tok_rows, w_rows)
    grad_weight = lax.dot_general(
        attn_cols, grad_out_all, (((0,), (0,)), ((), ())), preferred_element_type=jnp.float32
    )

    rims = jnp.concatenate(
        [grad_ext[:, : blocks_dev * BLK], grad_ext[:, 2 * blocks_dev * BLK :]], axis=1
    ).astype(jnp.bfloat16)
    from_prev, from_next = halo(rims)
    own = grad_ext[:, blocks_dev * BLK : 2 * blocks_dev * BLK]
    own = own + from_prev[:, blocks_dev * BLK :].astype(jnp.float32)
    own = own + from_next[:, : blocks_dev * BLK].astype(jnp.float32)
    for g in range(slots):
        start = (global_blocks[g] % blocks_dev) * BLK
        add = jnp.where(owners[g] == device, global_total[g], jnp.zeros_like(global_total[g]))
        cur = lax.dynamic_slice_in_dim(own, start, BLK, axis=1)
        own = lax.dynamic_update_slice_in_dim(own, cur + add, start, axis=1)
    own = own.astype(jnp.bfloat16)
    grad_query = jnp.concatenate(dq_rows, axis=0)
    return (layer_out, grad_query, own[0], own[1], grad_weight)


def solution(mesh):
    groups, seq = mesh.devices.shape
    split = Mesh(mesh.devices.reshape(groups, seq // 2, 2), ("groups",) + SEQ)
    rows = P(("groups",) + SEQ, None)
    placed = (rows, rows, rows, P(SEQ, None), rows, P("groups"), rows)
    return jax.shard_map(
        local,
        mesh=split,
        in_specs=placed,
        out_specs=(rows, rows, rows, rows, rows),
        check_vma=False,
    )
```

```python
import math

import jax
import jax.numpy as jnp
from jax import lax
from jax.sharding import Mesh
from jax.sharding import PartitionSpec as P

H = 8
BLK = 128
SEQ = ("chip", "core")


NEG_FILL = -1e30


def flat_index():
    return lax.axis_index("chip") * lax.axis_size("core") + lax.axis_index("core")


def xor_swap(x, level):
    if level == 0:
        n = lax.axis_size("core")
        return lax.ppermute(x, "core", [(i, i ^ 1) for i in range(n)])
    n = lax.axis_size("chip")
    m = 1 << (level - 1)
    return lax.ppermute(x, "chip", [(i, i ^ m) for i in range(n)])


def butterfly_sum(x, wire=None):
    count = lax.axis_size("chip") * lax.axis_size("core")
    levels = count.bit_length() - 1
    shape = x.shape
    flat = x.reshape(count, -1)
    d = flat_index()
    parts = flat
    for k in range(levels):
        half = parts.shape[0] // 2
        lo, hi = parts[:half], parts[half:]
        upper = ((d >> k) & 1) == 1
        send = jnp.where(upper, lo, hi)
        keep = jnp.where(upper, hi, lo)
        if wire is not None:
            send = send.astype(wire)
        parts = keep + xor_swap(send, k).astype(keep.dtype)
    for k in reversed(range(levels)):
        upper = ((d >> k) & 1) == 1
        if wire is not None and k == levels - 1:
            parts = parts.astype(wire)
        other = xor_swap(parts, k)
        parts = jnp.where(
            upper, jnp.concatenate([other, parts]), jnp.concatenate([parts, other])
        )
    return parts.reshape(shape)


def halo(shard):
    count = lax.axis_size("chip") * lax.axis_size("core")
    up = [(i, i + 1) for i in range(count - 1)]
    down = [(j, i) for i, j in up]
    before = lax.ppermute(shard, SEQ, up)
    after = lax.ppermute(shard, SEQ, down)
    return before, after


def attend(q, k, v, live, up):
    scale = 1.0 / math.sqrt(q.shape[-1])
    scores = jnp.einsum("ihd,jhd->hij", q, k, preferred_element_type=jnp.float32) * scale
    scores = jnp.where(live[None, None, :], scores, NEG_FILL)
    top = jnp.max(scores, axis=-1, keepdims=True)
    raised = jnp.exp(scores - top)
    probs = raised / jnp.sum(raised, axis=-1, keepdims=True)
    probs_b = probs.astype(jnp.bfloat16)
    attn = jnp.einsum("hij,jhd->ihd", probs_b, v, preferred_element_type=jnp.float32)
    attn = attn.astype(jnp.bfloat16)
    return probs, probs_b, attn


def attend_back(q, k, v, probs, probs_b, up):
    scale = 1.0 / math.sqrt(q.shape[-1])
    dv = jnp.einsum("hij,ihd->jhd", probs_b, up, preferred_element_type=jnp.float32)
    dprobs = jnp.einsum("ihd,jhd->hij", up, v, preferred_element_type=jnp.float32)
    rowdot = jnp.sum(probs * dprobs, axis=-1, keepdims=True)
    dscores = (scale * probs * (dprobs - rowdot)).astype(jnp.bfloat16)
    dq = jnp.einsum("hij,jhd->ihd", dscores, k, preferred_element_type=jnp.float32)
    dk = jnp.einsum("hij,ihd->jhd", dscores, q, preferred_element_type=jnp.float32)
    return dq, dk, dv


def local(query, keys, values, out_weight, grad_out, global_blocks, random_blocks):
    tok_rows, feature_count = query.shape
    hd = feature_count // H
    blocks_dev = tok_rows // BLK
    count = lax.axis_size("chip") * lax.axis_size("core")
    total_blocks = blocks_dev * count
    device = flat_index()

    grad_out_all = lax.all_gather(grad_out, SEQ, axis=0, tiled=True)
    weight_all = lax.all_gather(out_weight, SEQ, axis=0, tiled=True)

    paired = jnp.stack([keys, values])
    before, after = halo(paired)
    extended = jnp.concatenate([before, paired, after], axis=1)

    slots = global_blocks.shape[0]
    owners = global_blocks // blocks_dev
    masked = []
    for g in range(slots):
        start = (global_blocks[g] % blocks_dev) * BLK
        block = lax.dynamic_slice_in_dim(paired, start, BLK, axis=1)
        masked.append(jnp.where(owners[g] == device, block, jnp.zeros_like(block)))
    global_kv = butterfly_sum(jnp.stack(masked))

    local_ids = jnp.arange(blocks_dev, dtype=jnp.int32)
    global_ids = device * blocks_dev + local_ids
    offsets = jnp.array([-1, 0, 1], dtype=jnp.int32)
    neighbour_ids = global_ids[:, None] + offsets[None, :]
    window_index = local_ids[:, None] + blocks_dev + offsets[None, :]
    window_live = (neighbour_ids >= 0) & (neighbour_ids < total_blocks)
    random_index = random_blocks - (device - 1) * blocks_dev
    ext_index = jnp.concatenate([window_index, random_index], axis=1)
    n_local = ext_index.shape[1]
    live = jnp.concatenate(
        [window_live, jnp.ones(random_blocks.shape, jnp.bool_), jnp.ones((blocks_dev, slots), jnp.bool_)],
        axis=1,
    )

    w_rows = out_weight.shape[0]
    upstream_cols = lax.dot_general(
        grad_out_all, out_weight, (((1,), (1,)), ((), ())), preferred_element_type=jnp.float32
    ).astype(jnp.bfloat16)
    upstream = lax.all_to_all(
        upstream_cols.reshape(count, tok_rows, w_rows), SEQ, 0, 0, tiled=False
    )
    upstream = jnp.swapaxes(upstream, 0, 1).reshape(tok_rows, feature_count)

    attn_rows, dq_rows, dk_ext, dv_ext = [], [], [], []
    grad_ext = jnp.zeros((2, 3 * blocks_dev * BLK, feature_count), jnp.float32)
    global_terms = []
    for b in range(blocks_dev):
        chosen = [
            lax.dynamic_slice_in_dim(extended, ext_index[b, j] * BLK, BLK, axis=1)
            for j in range(n_local)
        ]
        chosen += [global_kv[g] for g in range(slots)]
        chosen = jnp.concatenate(chosen, axis=1).reshape(2, -1, H, hd)
        live_rows = jnp.repeat(live[b], BLK)
        q = query[b * BLK : (b + 1) * BLK].reshape(BLK, H, hd)
        up = upstream[b * BLK : (b + 1) * BLK].reshape(BLK, H, hd)
        probs, probs_b, attn = attend(q, chosen[0], chosen[1], live_rows, up)
        dq, dk, dv = attend_back(q, chosen[0], chosen[1], probs, probs_b, up)
        attn_rows.append(attn.reshape(BLK, feature_count))
        dq_rows.append(dq.reshape(BLK, feature_count).astype(jnp.bfloat16))
        dkv = jnp.stack([dk, dv]).reshape(2, -1, BLK, feature_count)
        for j in range(n_local):
            start = ext_index[b, j] * BLK
            cur = lax.dynamic_slice_in_dim(grad_ext, start, BLK, axis=1)
            grad_ext = lax.dynamic_update_slice_in_dim(grad_ext, cur + dkv[:, j], start, axis=1)
        global_terms.append(dkv[:, n_local:])
    global_local = global_terms[0]
    for t in global_terms[1:]:
        global_local = global_local + t
    global_total = butterfly_sum(jnp.swapaxes(global_local, 0, 1), jnp.bfloat16)

    attn_out = jnp.concatenate(attn_rows, axis=0)
    layer_out = jnp.dot(attn_out, weight_all, preferred_element_type=jnp.float32).astype(
        jnp.bfloat16
    )
    attn_cols = lax.all_to_all(
        attn_out.reshape(tok_rows, count, w_rows), SEQ, 1, 0, tiled=False
    ).reshape(count * tok_rows, w_rows)
    grad_weight = lax.dot_general(
        attn_cols, grad_out_all, (((0,), (0,)), ((), ())), preferred_element_type=jnp.float32
    )

    rims = jnp.concatenate(
        [grad_ext[:, : blocks_dev * BLK], grad_ext[:, 2 * blocks_dev * BLK :]], axis=1
    ).astype(jnp.bfloat16)
    from_prev, from_next = halo(rims)
    own = grad_ext[:, blocks_dev * BLK : 2 * blocks_dev * BLK]
    own = own + from_prev[:, blocks_dev * BLK :].astype(jnp.float32)
    own = own + from_next[:, : blocks_dev * BLK].astype(jnp.float32)
    for g in range(slots):
        start = (global_blocks[g] % blocks_dev) * BLK
        add = jnp.where(owners[g] == device, global_total[g], jnp.zeros_like(global_total[g]))
        cur = lax.dynamic_slice_in_dim(own, start, BLK, axis=1)
        own = lax.dynamic_update_slice_in_dim(own, cur + add, start, axis=1)
    own = own.astype(jnp.bfloat16)
    grad_query = jnp.concatenate(dq_rows, axis=0)
    return (layer_out, grad_query, own[0], own[1], grad_weight)


def solution(mesh):
    groups, seq = mesh.devices.shape
    split = Mesh(mesh.devices.reshape(groups, seq // 2, 2), ("groups",) + SEQ)
    rows = P(("groups",) + SEQ, None)
    placed = (rows, rows, rows, P(SEQ, None), rows, P("groups"), rows)
    return jax.shard_map(
        local,
        mesh=split,
        in_specs=placed,
        out_specs=(rows, rows, rows, rows, rows),
        check_vma=False,
    )
```

```python
import math

import jax
import jax.numpy as jnp
from jax import lax
from jax.sharding import Mesh
from jax.sharding import PartitionSpec as P

H = 8
BLK = 128
SEQ = ("chip", "core")


NEG_FILL = -1e30


def flat_index():
    return lax.axis_index("chip") * lax.axis_size("core") + lax.axis_index("core")


def xor_swap(x, level):
    if level == 0:
        n = lax.axis_size("core")
        return lax.ppermute(x, "core", [(i, i ^ 1) for i in range(n)])
    n = lax.axis_size("chip")
    m = 1 << (level - 1)
    return lax.ppermute(x, "chip", [(i, i ^ m) for i in range(n)])


def butterfly_sum(x, wire=None):
    count = lax.axis_size("chip") * lax.axis_size("core")
    levels = count.bit_length() - 1
    shape = x.shape
    flat = x.reshape(count, -1)
    d = flat_index()
    parts = flat
    for k in range(levels):
        half = parts.shape[0] // 2
        lo, hi = parts[:half], parts[half:]
        upper = ((d >> k) & 1) == 1
        send = jnp.where(upper, lo, hi)
        keep = jnp.where(upper, hi, lo)
        if wire is not None:
            send = send.astype(wire)
        parts = keep + xor_swap(send, k).astype(keep.dtype)
    for k in reversed(range(levels)):
        upper = ((d >> k) & 1) == 1
        if wire is not None and k == levels - 1:
            parts = parts.astype(wire)
        other = xor_swap(parts, k)
        parts = jnp.where(
            upper, jnp.concatenate([other, parts]), jnp.concatenate([parts, other])
        )
    return parts.reshape(shape)


def halo(shard):
    count = lax.axis_size("chip") * lax.axis_size("core")
    up = [(i, i + 1) for i in range(count - 1)]
    down = [(j, i) for i, j in up]
    before = lax.ppermute(shard, SEQ, up)
    after = lax.ppermute(shard, SEQ, down)
    return before, after


def attend(q, k, v, live, up):
    scale = 1.0 / math.sqrt(q.shape[-1])
    scores = jnp.einsum("ihd,jhd->hij", q, k, preferred_element_type=jnp.float32) * scale
    scores = jnp.where(live[None, None, :], scores, NEG_FILL)
    top = jnp.max(scores, axis=-1, keepdims=True)
    raised = jnp.exp(scores - top)
    probs = raised / jnp.sum(raised, axis=-1, keepdims=True)
    probs_b = probs.astype(jnp.bfloat16)
    attn = jnp.einsum("hij,jhd->ihd", probs_b, v, preferred_element_type=jnp.float32)
    attn = attn.astype(jnp.bfloat16)
    return probs, probs_b, attn


def attend_back(q, k, v, probs, probs_b, up):
    scale = 1.0 / math.sqrt(q.shape[-1])
    dv = jnp.einsum("hij,ihd->jhd", probs_b, up, preferred_element_type=jnp.float32)
    dprobs = jnp.einsum("ihd,jhd->hij", up, v, preferred_element_type=jnp.float32)
    rowdot = jnp.sum(probs * dprobs, axis=-1, keepdims=True)
    dscores = (scale * probs * (dprobs - rowdot)).astype(jnp.bfloat16)
    dq = jnp.einsum("hij,jhd->ihd", dscores, k, preferred_element_type=jnp.float32)
    dk = jnp.einsum("hij,ihd->jhd", dscores, q, preferred_element_type=jnp.float32)
    return dq, dk, dv


def local(query, keys, values, out_weight, grad_out, global_blocks, random_blocks):
    tok_rows, feature_count = query.shape
    hd = feature_count // H
    blocks_dev = tok_rows // BLK
    count = lax.axis_size("chip") * lax.axis_size("core")
    total_blocks = blocks_dev * count
    device = flat_index()

    weight_all = lax.all_gather(out_weight, SEQ, axis=0, tiled=True)
    weight_all, grad_out_after = lax.optimization_barrier((weight_all, grad_out))
    grad_out_all = lax.all_gather(grad_out_after, SEQ, axis=0, tiled=True)

    paired = jnp.stack([keys, values])
    before, after = halo(paired)
    extended = jnp.concatenate([before, paired, after], axis=1)

    slots = global_blocks.shape[0]
    owners = global_blocks // blocks_dev
    masked = []
    for g in range(slots):
        start = (global_blocks[g] % blocks_dev) * BLK
        block = lax.dynamic_slice_in_dim(paired, start, BLK, axis=1)
        masked.append(jnp.where(owners[g] == device, block, jnp.zeros_like(block)))
    global_kv = butterfly_sum(jnp.stack(masked))

    local_ids = jnp.arange(blocks_dev, dtype=jnp.int32)
    global_ids = device * blocks_dev + local_ids
    offsets = jnp.array([-1, 0, 1], dtype=jnp.int32)
    neighbour_ids = global_ids[:, None] + offsets[None, :]
    window_index = local_ids[:, None] + blocks_dev + offsets[None, :]
    window_live = (neighbour_ids >= 0) & (neighbour_ids < total_blocks)
    random_index = random_blocks - (device - 1) * blocks_dev
    ext_index = jnp.concatenate([window_index, random_index], axis=1)
    n_local = ext_index.shape[1]
    live = jnp.concatenate(
        [window_live, jnp.ones(random_blocks.shape, jnp.bool_), jnp.ones((blocks_dev, slots), jnp.bool_)],
        axis=1,
    )

    w_rows = out_weight.shape[0]
    upstream = lax.dot_general(
        grad_out, weight_all, (((1,), (1,)), ((), ())), preferred_element_type=jnp.float32
    ).astype(jnp.bfloat16)

    attn_rows, dq_rows, dk_ext, dv_ext = [], [], [], []
    grad_ext = jnp.zeros((2, 3 * blocks_dev * BLK, feature_count), jnp.float32)
    global_terms = []
    for b in range(blocks_dev):
        chosen = [
            lax.dynamic_slice_in_dim(extended, ext_index[b, j] * BLK, BLK, axis=1)
            for j in range(n_local)
        ]
        chosen += [global_kv[g] for g in range(slots)]
        chosen = jnp.concatenate(chosen, axis=1).reshape(2, -1, H, hd)
        live_rows = jnp.repeat(live[b], BLK)
        q = query[b * BLK : (b + 1) * BLK].reshape(BLK, H, hd)
        up = upstream[b * BLK : (b + 1) * BLK].reshape(BLK, H, hd)
        probs, probs_b, attn = attend(q, chosen[0], chosen[1], live_rows, up)
        dq, dk, dv = attend_back(q, chosen[0], chosen[1], probs, probs_b, up)
        attn_rows.append(attn.reshape(BLK, feature_count))
        dq_rows.append(dq.reshape(BLK, feature_count).astype(jnp.bfloat16))
        dkv = jnp.stack([dk, dv]).reshape(2, -1, BLK, feature_count)
        for j in range(n_local):
            start = ext_index[b, j] * BLK
            cur = lax.dynamic_slice_in_dim(grad_ext, start, BLK, axis=1)
            grad_ext = lax.dynamic_update_slice_in_dim(grad_ext, cur + dkv[:, j], start, axis=1)
        global_terms.append(dkv[:, n_local:])
    global_local = global_terms[0]
    for t in global_terms[1:]:
        global_local = global_local + t
    global_total = butterfly_sum(jnp.swapaxes(global_local, 0, 1), jnp.bfloat16)

    attn_out = jnp.concatenate(attn_rows, axis=0)
    layer_out = jnp.dot(attn_out, weight_all, preferred_element_type=jnp.float32).astype(
        jnp.bfloat16
    )
    attn_cols = lax.all_to_all(
        attn_out.reshape(tok_rows, count, w_rows), SEQ, 1, 0, tiled=False
    ).reshape(count * tok_rows, w_rows)
    grad_weight = lax.dot_general(
        attn_cols, grad_out_all, (((0,), (0,)), ((), ())), preferred_element_type=jnp.float32
    )

    rims = jnp.concatenate(
        [grad_ext[:, : blocks_dev * BLK], grad_ext[:, 2 * blocks_dev * BLK :]], axis=1
    ).astype(jnp.bfloat16)
    from_prev, from_next = halo(rims)
    own = grad_ext[:, blocks_dev * BLK : 2 * blocks_dev * BLK]
    own = own + from_prev[:, blocks_dev * BLK :].astype(jnp.float32)
    own = own + from_next[:, : blocks_dev * BLK].astype(jnp.float32)
    for g in range(slots):
        start = (global_blocks[g] % blocks_dev) * BLK
        add = jnp.where(owners[g] == device, global_total[g], jnp.zeros_like(global_total[g]))
        cur = lax.dynamic_slice_in_dim(own, start, BLK, axis=1)
        own = lax.dynamic_update_slice_in_dim(own, cur + add, start, axis=1)
    own = own.astype(jnp.bfloat16)
    grad_query = jnp.concatenate(dq_rows, axis=0)
    return (layer_out, grad_query, own[0], own[1], grad_weight)


def solution(mesh):
    groups, seq = mesh.devices.shape
    split = Mesh(mesh.devices.reshape(groups, seq // 2, 2), ("groups",) + SEQ)
    rows = P(("groups",) + SEQ, None)
    placed = (rows, rows, rows, P(SEQ, None), rows, P("groups"), rows)
    return jax.shard_map(
        local,
        mesh=split,
        in_specs=placed,
        out_specs=(rows, rows, rows, rows, rows),
        check_vma=False,
    )
```

```python
import math

import jax
import jax.numpy as jnp
from jax import lax
from jax.experimental import pallas as pl
from jax.sharding import Mesh
from jax.sharding import PartitionSpec as P

H = 8
BLK = 128
SEQ = ("chip", "core")


NEG_FILL = -1e30


def flat_index():
    return lax.axis_index("chip") * lax.axis_size("core") + lax.axis_index("core")


def xor_swap(x, level):
    if level == 0:
        n = lax.axis_size("core")
        return lax.ppermute(x, "core", [(i, i ^ 1) for i in range(n)])
    n = lax.axis_size("chip")
    m = 1 << (level - 1)
    return lax.ppermute(x, "chip", [(i, i ^ m) for i in range(n)])


def butterfly_sum(x, wire=None):
    count = lax.axis_size("chip") * lax.axis_size("core")
    levels = count.bit_length() - 1
    shape = x.shape
    flat = x.reshape(count, -1)
    d = flat_index()
    parts = flat
    for k in range(levels):
        half = parts.shape[0] // 2
        lo, hi = parts[:half], parts[half:]
        upper = ((d >> k) & 1) == 1
        send = jnp.where(upper, lo, hi)
        keep = jnp.where(upper, hi, lo)
        if wire is not None:
            send = send.astype(wire)
        parts = keep + xor_swap(send, k).astype(keep.dtype)
    for k in reversed(range(levels)):
        upper = ((d >> k) & 1) == 1
        if wire is not None and k == levels - 1:
            parts = parts.astype(wire)
        other = xor_swap(parts, k)
        parts = jnp.where(
            upper, jnp.concatenate([other, parts]), jnp.concatenate([parts, other])
        )
    return parts.reshape(shape)


def halo(shard):
    count = lax.axis_size("chip") * lax.axis_size("core")
    up = [(i, i + 1) for i in range(count - 1)]
    down = [(j, i) for i, j in up]
    before = lax.ppermute(shard, SEQ, up)
    after = lax.ppermute(shard, SEQ, down)
    return before, after


def _attn_kernel(live_ref, q_ref, k_ref, v_ref, up_ref, attn_ref, dq_ref, dk_ref, dv_ref):
    scale = 1.0 / math.sqrt(q_ref.shape[-1])
    q = q_ref[...]
    k = k_ref[...]
    v = v_ref[...]
    up = up_ref[...]
    nt = (((1,), (1,)), ((), ()))
    tn = (((0,), (0,)), ((), ()))
    scores = lax.dot_general(q, k, nt, preferred_element_type=jnp.float32) * scale
    scores = jnp.where(live_ref[...] > 0, scores, NEG_FILL)
    top = jnp.max(scores, axis=-1, keepdims=True)
    raised = jnp.exp(scores - top)
    probs = raised / jnp.sum(raised, axis=-1, keepdims=True)
    probs_b = probs.astype(jnp.bfloat16)
    attn_ref[...] = jnp.dot(probs_b, v, preferred_element_type=jnp.float32).astype(attn_ref.dtype)
    dv_ref[...] = lax.dot_general(probs_b, up, tn, preferred_element_type=jnp.float32)
    dprobs = lax.dot_general(up, v, nt, preferred_element_type=jnp.float32)
    rowdot = jnp.sum(probs * dprobs, axis=-1, keepdims=True)
    dscores = (scale * probs * (dprobs - rowdot)).astype(jnp.bfloat16)
    dq_ref[...] = jnp.dot(dscores, k, preferred_element_type=jnp.float32).astype(dq_ref.dtype)
    dk_ref[...] = lax.dot_general(dscores, q, tn, preferred_element_type=jnp.float32)

def attention(live, q, k, v, up, heads):
    rows, features = q.shape
    keys_n = k.shape[0]
    hd = features // heads
    qspec = pl.BlockSpec((rows, hd), lambda h: (0, h))
    kspec = pl.BlockSpec((keys_n, hd), lambda h: (0, h))
    return pl.pallas_call(
        _attn_kernel,
        grid=(heads,),
        in_specs=[pl.BlockSpec((1, keys_n), lambda h: (0, 0)), qspec, kspec, kspec, qspec],
        out_specs=[qspec, qspec, kspec, kspec],
        out_shape=[
            jax.ShapeDtypeStruct((rows, features), jnp.bfloat16),
            jax.ShapeDtypeStruct((rows, features), jnp.bfloat16),
            jax.ShapeDtypeStruct((keys_n, features), jnp.float32),
            jax.ShapeDtypeStruct((keys_n, features), jnp.float32),
        ],
    )(live, q, k, v, up)


def local(query, keys, values, out_weight, grad_out, global_blocks, random_blocks):
    tok_rows, feature_count = query.shape
    hd = feature_count // H
    blocks_dev = tok_rows // BLK
    count = lax.axis_size("chip") * lax.axis_size("core")
    total_blocks = blocks_dev * count
    device = flat_index()

    grad_out_all = lax.all_gather(grad_out, SEQ, axis=0, tiled=True)
    weight_all = lax.all_gather(out_weight, SEQ, axis=0, tiled=True)

    paired = jnp.stack([keys, values])
    before, after = halo(paired)
    extended = jnp.concatenate([before, paired, after], axis=1)

    slots = global_blocks.shape[0]
    owners = global_blocks // blocks_dev
    masked = []
    for g in range(slots):
        start = (global_blocks[g] % blocks_dev) * BLK
        block = lax.dynamic_slice_in_dim(paired, start, BLK, axis=1)
        masked.append(jnp.where(owners[g] == device, block, jnp.zeros_like(block)))
    global_kv = butterfly_sum(jnp.stack(masked))

    local_ids = jnp.arange(blocks_dev, dtype=jnp.int32)
    global_ids = device * blocks_dev + local_ids
    offsets = jnp.array([-1, 0, 1], dtype=jnp.int32)
    neighbour_ids = global_ids[:, None] + offsets[None, :]
    window_index = local_ids[:, None] + blocks_dev + offsets[None, :]
    window_live = (neighbour_ids >= 0) & (neighbour_ids < total_blocks)
    random_index = random_blocks - (device - 1) * blocks_dev
    ext_index = jnp.concatenate([window_index, random_index], axis=1)
    n_local = ext_index.shape[1]
    live = jnp.concatenate(
        [window_live, jnp.ones(random_blocks.shape, jnp.bool_), jnp.ones((blocks_dev, slots), jnp.bool_)],
        axis=1,
    )

    w_rows = out_weight.shape[0]
    upstream_cols = lax.dot_general(
        grad_out_all, out_weight, (((1,), (1,)), ((), ())), preferred_element_type=jnp.float32
    ).astype(jnp.bfloat16)
    upstream = lax.all_to_all(
        upstream_cols.reshape(count, tok_rows, w_rows), SEQ, 0, 0, tiled=False
    )
    upstream = jnp.swapaxes(upstream, 0, 1).reshape(tok_rows, feature_count)

    attn_rows, dq_rows = [], []
    grad_ext = [jnp.zeros((3 * blocks_dev * BLK, feature_count), jnp.float32) for _ in range(2)]
    global_local = None
    for b in range(blocks_dev):
        chosen = []
        for side in range(2):
            parts = [
                lax.dynamic_slice_in_dim(extended[side], ext_index[b, j] * BLK, BLK, axis=0)
                for j in range(n_local)
            ]
            parts += [global_kv[g, side] for g in range(slots)]
            chosen.append(jnp.concatenate(parts, axis=0))
        live_rows = jnp.repeat(live[b], BLK).astype(jnp.float32)[None]
        q = query[b * BLK : (b + 1) * BLK]
        up = upstream[b * BLK : (b + 1) * BLK]
        attn, dq, dk, dv = attention(live_rows, q, chosen[0], chosen[1], up, H)
        attn_rows.append(attn)
        dq_rows.append(dq)
        for side, grad in enumerate((dk, dv)):
            for j in range(n_local):
                start = ext_index[b, j] * BLK
                cur = lax.dynamic_slice_in_dim(grad_ext[side], start, BLK, axis=0)
                term = grad[j * BLK : (j + 1) * BLK]
                grad_ext[side] = lax.dynamic_update_slice_in_dim(
                    grad_ext[side], cur + term, start, axis=0
                )
        terms = jnp.stack(
            [dk[n_local * BLK :].reshape(slots, BLK, feature_count),
             dv[n_local * BLK :].reshape(slots, BLK, feature_count)],
            axis=1,
        )
        global_local = terms if global_local is None else global_local + terms
    grad_ext = jnp.stack(grad_ext)
    global_total = butterfly_sum(global_local, jnp.bfloat16)

    attn_out = jnp.concatenate(attn_rows, axis=0)
    layer_out = jnp.dot(attn_out, weight_all, preferred_element_type=jnp.float32).astype(
        jnp.bfloat16
    )
    attn_cols = lax.all_to_all(
        attn_out.reshape(tok_rows, count, w_rows), SEQ, 1, 0, tiled=False
    ).reshape(count * tok_rows, w_rows)
    grad_weight = lax.dot_general(
        attn_cols, grad_out_all, (((0,), (0,)), ((), ())), preferred_element_type=jnp.float32
    )

    rims = jnp.concatenate(
        [grad_ext[:, : blocks_dev * BLK], grad_ext[:, 2 * blocks_dev * BLK :]], axis=1
    ).astype(jnp.bfloat16)
    from_prev, from_next = halo(rims)
    own = grad_ext[:, blocks_dev * BLK : 2 * blocks_dev * BLK]
    own = own + from_prev[:, blocks_dev * BLK :].astype(jnp.float32)
    own = own + from_next[:, : blocks_dev * BLK].astype(jnp.float32)
    for g in range(slots):
        start = (global_blocks[g] % blocks_dev) * BLK
        add = jnp.where(owners[g] == device, global_total[g], jnp.zeros_like(global_total[g]))
        cur = lax.dynamic_slice_in_dim(own, start, BLK, axis=1)
        own = lax.dynamic_update_slice_in_dim(own, cur + add, start, axis=1)
    own = own.astype(jnp.bfloat16)
    grad_query = jnp.concatenate(dq_rows, axis=0)
    return (layer_out, grad_query, own[0], own[1], grad_weight)


def solution(mesh):
    groups, seq = mesh.devices.shape
    split = Mesh(mesh.devices.reshape(groups, seq // 2, 2), ("groups",) + SEQ)
    rows = P(("groups",) + SEQ, None)
    placed = (rows, rows, rows, P(SEQ, None), rows, P("groups"), rows)
    return jax.shard_map(
        local,
        mesh=split,
        in_specs=placed,
        out_specs=(rows, rows, rows, rows, rows),
        check_vma=False,
    )
```

```python
import math

import jax
import jax.numpy as jnp
from jax import lax
from jax.experimental import pallas as pl
from jax.sharding import Mesh
from jax.sharding import PartitionSpec as P

H = 8
BLK = 128
SEQ = ("chip", "core")


NEG_FILL = -1e30


def flat_index():
    return lax.axis_index("chip") * lax.axis_size("core") + lax.axis_index("core")


def xor_swap(x, level):
    if level == 0:
        n = lax.axis_size("core")
        return lax.ppermute(x, "core", [(i, i ^ 1) for i in range(n)])
    n = lax.axis_size("chip")
    m = 1 << (level - 1)
    return lax.ppermute(x, "chip", [(i, i ^ m) for i in range(n)])


def butterfly_sum(x, wire=None):
    count = lax.axis_size("chip") * lax.axis_size("core")
    levels = count.bit_length() - 1
    shape = x.shape
    flat = x.reshape(count, -1)
    d = flat_index()
    parts = flat
    for k in range(levels):
        half = parts.shape[0] // 2
        lo, hi = parts[:half], parts[half:]
        upper = ((d >> k) & 1) == 1
        send = jnp.where(upper, lo, hi)
        keep = jnp.where(upper, hi, lo)
        if wire is not None:
            send = send.astype(wire)
        parts = keep + xor_swap(send, k).astype(keep.dtype)
    for k in reversed(range(levels)):
        upper = ((d >> k) & 1) == 1
        if wire is not None and k == levels - 1:
            parts = parts.astype(wire)
        other = xor_swap(parts, k)
        parts = jnp.where(
            upper, jnp.concatenate([other, parts]), jnp.concatenate([parts, other])
        )
    return parts.reshape(shape)


def halo(shard):
    count = lax.axis_size("chip") * lax.axis_size("core")
    up = [(i, i + 1) for i in range(count - 1)]
    down = [(j, i) for i, j in up]
    before = lax.ppermute(shard, SEQ, up)
    after = lax.ppermute(shard, SEQ, down)
    return before, after


def _probs(live_ref, q, k):
    scale = 1.0 / math.sqrt(q.shape[-1])
    nt = (((1,), (1,)), ((), ()))
    scores = lax.dot_general(q, k, nt, preferred_element_type=jnp.float32) * scale
    scores = jnp.where(live_ref[...] > 0, scores, NEG_FILL)
    top = jnp.max(scores, axis=-1, keepdims=True)
    raised = jnp.exp(scores - top)
    return raised / jnp.sum(raised, axis=-1, keepdims=True)


def _forward_kernel(live_ref, q_ref, k_ref, v_ref, attn_ref):
    probs_b = _probs(live_ref, q_ref[...], k_ref[...]).astype(jnp.bfloat16)
    attn = jnp.dot(probs_b, v_ref[...], preferred_element_type=jnp.float32)
    attn_ref[...] = attn.astype(attn_ref.dtype)


def _backward_kernel(live_ref, q_ref, k_ref, v_ref, up_ref, dq_ref, dk_ref, dv_ref):
    q = q_ref[...]
    k = k_ref[...]
    v = v_ref[...]
    up = up_ref[...]
    scale = 1.0 / math.sqrt(q.shape[-1])
    nt = (((1,), (1,)), ((), ()))
    tn = (((0,), (0,)), ((), ()))
    probs = _probs(live_ref, q, k)
    probs_b = probs.astype(jnp.bfloat16)
    dv_ref[...] = lax.dot_general(probs_b, up, tn, preferred_element_type=jnp.float32)
    dprobs = lax.dot_general(up, v, nt, preferred_element_type=jnp.float32)
    rowdot = jnp.sum(probs * dprobs, axis=-1, keepdims=True)
    dscores = (scale * probs * (dprobs - rowdot)).astype(jnp.bfloat16)
    dq = jnp.dot(dscores, k, preferred_element_type=jnp.float32)
    dq_ref[...] = dq.astype(dq_ref.dtype)
    dk_ref[...] = lax.dot_general(dscores, q, tn, preferred_element_type=jnp.float32)


def _specs(rows, keys_n, hd):
    qspec = pl.BlockSpec((rows, hd), lambda h: (0, h))
    kspec = pl.BlockSpec((keys_n, hd), lambda h: (0, h))
    return pl.BlockSpec((1, keys_n), lambda h: (0, 0)), qspec, kspec


def attention_forward(live, q, k, v, heads):
    rows, features = q.shape
    lspec, qspec, kspec = _specs(rows, k.shape[0], features // heads)
    return pl.pallas_call(
        _forward_kernel,
        grid=(heads,),
        in_specs=[lspec, qspec, kspec, kspec],
        out_specs=qspec,
        out_shape=jax.ShapeDtypeStruct((rows, features), jnp.bfloat16),
    )(live, q, k, v)


def attention_backward(live, q, k, v, up, heads):
    rows, features = q.shape
    keys_n = k.shape[0]
    lspec, qspec, kspec = _specs(rows, keys_n, features // heads)
    return pl.pallas_call(
        _backward_kernel,
        grid=(heads,),
        in_specs=[lspec, qspec, kspec, kspec, qspec],
        out_specs=[qspec, kspec, kspec],
        out_shape=[
            jax.ShapeDtypeStruct((rows, features), jnp.bfloat16),
            jax.ShapeDtypeStruct((keys_n, features), jnp.float32),
            jax.ShapeDtypeStruct((keys_n, features), jnp.float32),
        ],
    )(live, q, k, v, up)


def local(query, keys, values, out_weight, grad_out, global_blocks, random_blocks):
    tok_rows, feature_count = query.shape
    hd = feature_count // H
    blocks_dev = tok_rows // BLK
    count = lax.axis_size("chip") * lax.axis_size("core")
    total_blocks = blocks_dev * count
    device = flat_index()

    grad_out_all = lax.all_gather(grad_out, SEQ, axis=0, tiled=True)
    weight_all = lax.all_gather(out_weight, SEQ, axis=0, tiled=True)

    paired = jnp.stack([keys, values])
    before, after = halo(paired)
    extended = jnp.concatenate([before, paired, after], axis=1)

    slots = global_blocks.shape[0]
    owners = global_blocks // blocks_dev
    masked = []
    for g in range(slots):
        start = (global_blocks[g] % blocks_dev) * BLK
        block = lax.dynamic_slice_in_dim(paired, start, BLK, axis=1)
        masked.append(jnp.where(owners[g] == device, block, jnp.zeros_like(block)))
    global_kv = butterfly_sum(jnp.stack(masked))

    local_ids = jnp.arange(blocks_dev, dtype=jnp.int32)
    global_ids = device * blocks_dev + local_ids
    offsets = jnp.array([-1, 0, 1], dtype=jnp.int32)
    neighbour_ids = global_ids[:, None] + offsets[None, :]
    window_index = local_ids[:, None] + blocks_dev + offsets[None, :]
    window_live = (neighbour_ids >= 0) & (neighbour_ids < total_blocks)
    random_index = random_blocks - (device - 1) * blocks_dev
    ext_index = jnp.concatenate([window_index, random_index], axis=1)
    n_local = ext_index.shape[1]
    live = jnp.concatenate(
        [window_live, jnp.ones(random_blocks.shape, jnp.bool_), jnp.ones((blocks_dev, slots), jnp.bool_)],
        axis=1,
    )

    w_rows = out_weight.shape[0]
    upstream_cols = lax.dot_general(
        grad_out_all, out_weight, (((1,), (1,)), ((), ())), preferred_element_type=jnp.float32
    ).astype(jnp.bfloat16)
    upstream = lax.all_to_all(
        upstream_cols.reshape(count, tok_rows, w_rows), SEQ, 0, 0, tiled=False
    )
    upstream = jnp.swapaxes(upstream, 0, 1).reshape(tok_rows, feature_count)

    attn_rows, dq_rows = [], []
    grad_ext = [jnp.zeros((3 * blocks_dev * BLK, feature_count), jnp.float32) for _ in range(2)]
    global_local = None
    for b in range(blocks_dev):
        chosen = []
        for side in range(2):
            parts = [
                lax.dynamic_slice_in_dim(extended[side], ext_index[b, j] * BLK, BLK, axis=0)
                for j in range(n_local)
            ]
            parts += [global_kv[g, side] for g in range(slots)]
            chosen.append(jnp.concatenate(parts, axis=0))
        live_rows = jnp.repeat(live[b], BLK).astype(jnp.float32)[None]
        q = query[b * BLK : (b + 1) * BLK]
        up = upstream[b * BLK : (b + 1) * BLK]
        attn = attention_forward(live_rows, q, chosen[0], chosen[1], H)
        dq, dk, dv = attention_backward(live_rows, q, chosen[0], chosen[1], up, H)
        attn_rows.append(attn)
        dq_rows.append(dq)
        for side, grad in enumerate((dk, dv)):
            for j in range(n_local):
                start = ext_index[b, j] * BLK
                cur = lax.dynamic_slice_in_dim(grad_ext[side], start, BLK, axis=0)
                term = grad[j * BLK : (j + 1) * BLK]
                grad_ext[side] = lax.dynamic_update_slice_in_dim(
                    grad_ext[side], cur + term, start, axis=0
                )
        terms = jnp.stack(
            [dk[n_local * BLK :].reshape(slots, BLK, feature_count),
             dv[n_local * BLK :].reshape(slots, BLK, feature_count)],
            axis=1,
        )
        global_local = terms if global_local is None else global_local + terms
    grad_ext = jnp.stack(grad_ext)
    global_total = butterfly_sum(global_local, jnp.bfloat16)

    attn_out = jnp.concatenate(attn_rows, axis=0)
    layer_out = jnp.dot(attn_out, weight_all, preferred_element_type=jnp.float32).astype(
        jnp.bfloat16
    )
    attn_cols = lax.all_to_all(
        attn_out.reshape(tok_rows, count, w_rows), SEQ, 1, 0, tiled=False
    ).reshape(count * tok_rows, w_rows)
    grad_weight = lax.dot_general(
        attn_cols, grad_out_all, (((0,), (0,)), ((), ())), preferred_element_type=jnp.float32
    )

    rims = jnp.concatenate(
        [grad_ext[:, : blocks_dev * BLK], grad_ext[:, 2 * blocks_dev * BLK :]], axis=1
    ).astype(jnp.bfloat16)
    from_prev, from_next = halo(rims)
    own = grad_ext[:, blocks_dev * BLK : 2 * blocks_dev * BLK]
    own = own + from_prev[:, blocks_dev * BLK :].astype(jnp.float32)
    own = own + from_next[:, : blocks_dev * BLK].astype(jnp.float32)
    for g in range(slots):
        start = (global_blocks[g] % blocks_dev) * BLK
        add = jnp.where(owners[g] == device, global_total[g], jnp.zeros_like(global_total[g]))
        cur = lax.dynamic_slice_in_dim(own, start, BLK, axis=1)
        own = lax.dynamic_update_slice_in_dim(own, cur + add, start, axis=1)
    own = own.astype(jnp.bfloat16)
    grad_query = jnp.concatenate(dq_rows, axis=0)
    return (layer_out, grad_query, own[0], own[1], grad_weight)


def solution(mesh):
    groups, seq = mesh.devices.shape
    split = Mesh(mesh.devices.reshape(groups, seq // 2, 2), ("groups",) + SEQ)
    rows = P(("groups",) + SEQ, None)
    placed = (rows, rows, rows, P(SEQ, None), rows, P("groups"), rows)
    return jax.shard_map(
        local,
        mesh=split,
        in_specs=placed,
        out_specs=(rows, rows, rows, rows, rows),
        check_vma=False,
    )
```

```python
import math

import jax
import jax.numpy as jnp
from jax import lax
from jax.experimental import pallas as pl
from jax.sharding import Mesh
from jax.sharding import PartitionSpec as P

H = 8
BLK = 128
SEQ = ("chip", "core")


NEG_FILL = -1e30


def flat_index():
    return lax.axis_index("chip") * lax.axis_size("core") + lax.axis_index("core")


def xor_swap(x, level):
    if level == 0:
        n = lax.axis_size("core")
        return lax.ppermute(x, "core", [(i, i ^ 1) for i in range(n)])
    n = lax.axis_size("chip")
    m = 1 << (level - 1)
    return lax.ppermute(x, "chip", [(i, i ^ m) for i in range(n)])


def butterfly_sum(x, wire=None):
    count = lax.axis_size("chip") * lax.axis_size("core")
    levels = count.bit_length() - 1
    shape = x.shape
    flat = x.reshape(count, -1)
    d = flat_index()
    parts = flat
    for k in range(levels):
        half = parts.shape[0] // 2
        lo, hi = parts[:half], parts[half:]
        upper = ((d >> k) & 1) == 1
        send = jnp.where(upper, lo, hi)
        keep = jnp.where(upper, hi, lo)
        if wire is not None:
            send = send.astype(wire)
        parts = keep + xor_swap(send, k).astype(keep.dtype)
    for k in reversed(range(levels)):
        upper = ((d >> k) & 1) == 1
        if wire is not None and k == levels - 1:
            parts = parts.astype(wire)
        other = xor_swap(parts, k)
        parts = jnp.where(
            upper, jnp.concatenate([other, parts]), jnp.concatenate([parts, other])
        )
    return parts.reshape(shape)


def halo(shard):
    count = lax.axis_size("chip") * lax.axis_size("core")
    up = [(i, i + 1) for i in range(count - 1)]
    down = [(j, i) for i, j in up]
    before = lax.ppermute(shard, SEQ, up)
    after = lax.ppermute(shard, SEQ, down)
    return before, after


def _probs(live_ref, q, k):
    scale = 1.0 / math.sqrt(q.shape[-1])
    nt = (((1,), (1,)), ((), ()))
    scores = lax.dot_general(q, k, nt, preferred_element_type=jnp.float32) * scale
    scores = jnp.where(live_ref[...] > 0, scores, NEG_FILL)
    top = jnp.max(scores, axis=-1, keepdims=True)
    raised = jnp.exp(scores - top)
    return raised / jnp.sum(raised, axis=-1, keepdims=True)


def _forward_kernel(live_ref, q_ref, k_ref, v_ref, attn_ref):
    probs_b = _probs(live_ref, q_ref[...], k_ref[...]).astype(jnp.bfloat16)
    attn = jnp.dot(probs_b, v_ref[...], preferred_element_type=jnp.float32)
    attn_ref[...] = attn.astype(attn_ref.dtype)


def _backward_kernel(live_ref, q_ref, k_ref, v_ref, up_ref, dq_ref, dk_ref, dv_ref):
    q = q_ref[...]
    k = k_ref[...]
    v = v_ref[...]
    up = up_ref[...]
    scale = 1.0 / math.sqrt(q.shape[-1])
    nt = (((1,), (1,)), ((), ()))
    tn = (((0,), (0,)), ((), ()))
    probs = _probs(live_ref, q, k)
    probs_b = probs.astype(jnp.bfloat16)
    dv_ref[...] = lax.dot_general(probs_b, up, tn, preferred_element_type=jnp.float32)
    dprobs = lax.dot_general(up, v, nt, preferred_element_type=jnp.float32)
    rowdot = jnp.sum(probs * dprobs, axis=-1, keepdims=True)
    dscores = (scale * probs * (dprobs - rowdot)).astype(jnp.bfloat16)
    dq = jnp.dot(dscores, k, preferred_element_type=jnp.float32)
    dq_ref[...] = dq.astype(dq_ref.dtype)
    dk_ref[...] = lax.dot_general(dscores, q, tn, preferred_element_type=jnp.float32)


def _specs(rows, keys_n, hd):
    qspec = pl.BlockSpec((rows, hd), lambda h: (0, h))
    kspec = pl.BlockSpec((keys_n, hd), lambda h: (0, h))
    return pl.BlockSpec((1, keys_n), lambda h: (0, 0)), qspec, kspec


def attention_forward(live, q, k, v, heads):
    rows, features = q.shape
    lspec, qspec, kspec = _specs(rows, k.shape[0], features // heads)
    return pl.pallas_call(
        _forward_kernel,
        grid=(heads,),
        in_specs=[lspec, qspec, kspec, kspec],
        out_specs=qspec,
        out_shape=jax.ShapeDtypeStruct((rows, features), jnp.bfloat16),
    )(live, q, k, v)


def attention_backward(live, q, k, v, up, heads):
    rows, features = q.shape
    keys_n = k.shape[0]
    lspec, qspec, kspec = _specs(rows, keys_n, features // heads)
    return pl.pallas_call(
        _backward_kernel,
        grid=(heads,),
        in_specs=[lspec, qspec, kspec, kspec, qspec],
        out_specs=[qspec, kspec, kspec],
        out_shape=[
            jax.ShapeDtypeStruct((rows, features), jnp.bfloat16),
            jax.ShapeDtypeStruct((keys_n, features), jnp.float32),
            jax.ShapeDtypeStruct((keys_n, features), jnp.float32),
        ],
    )(live, q, k, v, up)


def local(query, keys, values, out_weight, grad_out, global_blocks, random_blocks):
    tok_rows, feature_count = query.shape
    hd = feature_count // H
    blocks_dev = tok_rows // BLK
    count = lax.axis_size("chip") * lax.axis_size("core")
    total_blocks = blocks_dev * count
    device = flat_index()

    grad_out_all = lax.all_gather(grad_out, SEQ, axis=0, tiled=True)
    grad_out_all, weight_after = lax.optimization_barrier((grad_out_all, out_weight))
    weight_all = lax.all_gather(weight_after, SEQ, axis=0, tiled=True)

    paired = jnp.stack([keys, values])
    before, after = halo(paired)
    extended = jnp.concatenate([before, paired, after], axis=1)

    slots = global_blocks.shape[0]
    owners = global_blocks // blocks_dev
    masked = []
    for g in range(slots):
        start = (global_blocks[g] % blocks_dev) * BLK
        block = lax.dynamic_slice_in_dim(paired, start, BLK, axis=1)
        masked.append(jnp.where(owners[g] == device, block, jnp.zeros_like(block)))
    global_kv = butterfly_sum(jnp.stack(masked))

    local_ids = jnp.arange(blocks_dev, dtype=jnp.int32)
    global_ids = device * blocks_dev + local_ids
    offsets = jnp.array([-1, 0, 1], dtype=jnp.int32)
    neighbour_ids = global_ids[:, None] + offsets[None, :]
    window_index = local_ids[:, None] + blocks_dev + offsets[None, :]
    window_live = (neighbour_ids >= 0) & (neighbour_ids < total_blocks)
    random_index = random_blocks - (device - 1) * blocks_dev
    ext_index = jnp.concatenate([window_index, random_index], axis=1)
    n_local = ext_index.shape[1]
    live = jnp.concatenate(
        [window_live, jnp.ones(random_blocks.shape, jnp.bool_), jnp.ones((blocks_dev, slots), jnp.bool_)],
        axis=1,
    )

    w_rows = out_weight.shape[0]
    upstream_cols = lax.dot_general(
        grad_out_all, out_weight, (((1,), (1,)), ((), ())), preferred_element_type=jnp.float32
    ).astype(jnp.bfloat16)
    upstream = lax.all_to_all(
        upstream_cols.reshape(count, tok_rows, w_rows), SEQ, 0, 0, tiled=False
    )
    upstream = jnp.swapaxes(upstream, 0, 1).reshape(tok_rows, feature_count)

    attn_rows, dq_rows = [], []
    grad_ext = [jnp.zeros((3 * blocks_dev * BLK, feature_count), jnp.float32) for _ in range(2)]
    global_local = None
    for b in range(blocks_dev):
        chosen = []
        for side in range(2):
            parts = [
                lax.dynamic_slice_in_dim(extended[side], ext_index[b, j] * BLK, BLK, axis=0)
                for j in range(n_local)
            ]
            parts += [global_kv[g, side] for g in range(slots)]
            chosen.append(jnp.concatenate(parts, axis=0))
        live_rows = jnp.repeat(live[b], BLK).astype(jnp.float32)[None]
        q = query[b * BLK : (b + 1) * BLK]
        up = upstream[b * BLK : (b + 1) * BLK]
        attn = attention_forward(live_rows, q, chosen[0], chosen[1], H)
        dq, dk, dv = attention_backward(live_rows, q, chosen[0], chosen[1], up, H)
        attn_rows.append(attn)
        dq_rows.append(dq)
        for side, grad in enumerate((dk, dv)):
            for j in range(n_local):
                start = ext_index[b, j] * BLK
                cur = lax.dynamic_slice_in_dim(grad_ext[side], start, BLK, axis=0)
                term = grad[j * BLK : (j + 1) * BLK]
                grad_ext[side] = lax.dynamic_update_slice_in_dim(
                    grad_ext[side], cur + term, start, axis=0
                )
        terms = jnp.stack(
            [dk[n_local * BLK :].reshape(slots, BLK, feature_count),
             dv[n_local * BLK :].reshape(slots, BLK, feature_count)],
            axis=1,
        )
        global_local = terms if global_local is None else global_local + terms
    grad_ext = jnp.stack(grad_ext)
    global_total = butterfly_sum(global_local, jnp.bfloat16)

    attn_out = jnp.concatenate(attn_rows, axis=0)
    layer_out = jnp.dot(attn_out, weight_all, preferred_element_type=jnp.float32).astype(
        jnp.bfloat16
    )
    attn_cols = lax.all_to_all(
        attn_out.reshape(tok_rows, count, w_rows), SEQ, 1, 0, tiled=False
    ).reshape(count * tok_rows, w_rows)
    grad_weight = lax.dot_general(
        attn_cols, grad_out_all, (((0,), (0,)), ((), ())), preferred_element_type=jnp.float32
    )

    rims = jnp.concatenate(
        [grad_ext[:, : blocks_dev * BLK], grad_ext[:, 2 * blocks_dev * BLK :]], axis=1
    ).astype(jnp.bfloat16)
    from_prev, from_next = halo(rims)
    own = grad_ext[:, blocks_dev * BLK : 2 * blocks_dev * BLK]
    own = own + from_prev[:, blocks_dev * BLK :].astype(jnp.float32)
    own = own + from_next[:, : blocks_dev * BLK].astype(jnp.float32)
    for g in range(slots):
        start = (global_blocks[g] % blocks_dev) * BLK
        add = jnp.where(owners[g] == device, global_total[g], jnp.zeros_like(global_total[g]))
        cur = lax.dynamic_slice_in_dim(own, start, BLK, axis=1)
        own = lax.dynamic_update_slice_in_dim(own, cur + add, start, axis=1)
    own = own.astype(jnp.bfloat16)
    grad_query = jnp.concatenate(dq_rows, axis=0)
    return (layer_out, grad_query, own[0], own[1], grad_weight)


def solution(mesh):
    groups, seq = mesh.devices.shape
    split = Mesh(mesh.devices.reshape(groups, seq // 2, 2), ("groups",) + SEQ)
    rows = P(("groups",) + SEQ, None)
    placed = (rows, rows, rows, P(SEQ, None), rows, P("groups"), rows)
    return jax.shard_map(
        local,
        mesh=split,
        in_specs=placed,
        out_specs=(rows, rows, rows, rows, rows),
        check_vma=False,
    )
```

```python
import math

import jax
import jax.numpy as jnp
from jax import lax
from jax.experimental import pallas as pl
from jax.sharding import Mesh
from jax.sharding import PartitionSpec as P

H = 8
BLK = 128
SEQ = ("chip", "core")


NEG_FILL = -1e30


def flat_index():
    return lax.axis_index("chip") * lax.axis_size("core") + lax.axis_index("core")


def xor_swap(x, level):
    if level == 0:
        n = lax.axis_size("core")
        return lax.ppermute(x, "core", [(i, i ^ 1) for i in range(n)])
    n = lax.axis_size("chip")
    m = 1 << (level - 1)
    return lax.ppermute(x, "chip", [(i, i ^ m) for i in range(n)])


def butterfly_sum(x, wire=None):
    count = lax.axis_size("chip") * lax.axis_size("core")
    levels = count.bit_length() - 1
    shape = x.shape
    flat = x.reshape(count, -1)
    d = flat_index()
    parts = flat
    for k in range(levels):
        half = parts.shape[0] // 2
        lo, hi = parts[:half], parts[half:]
        upper = ((d >> k) & 1) == 1
        send = jnp.where(upper, lo, hi)
        keep = jnp.where(upper, hi, lo)
        if wire is not None:
            send = send.astype(wire)
        parts = keep + xor_swap(send, k).astype(keep.dtype)
    for k in reversed(range(levels)):
        upper = ((d >> k) & 1) == 1
        if wire is not None and k == levels - 1:
            parts = parts.astype(wire)
        other = xor_swap(parts, k)
        parts = jnp.where(
            upper, jnp.concatenate([other, parts]), jnp.concatenate([parts, other])
        )
    return parts.reshape(shape)


def core_swap(x):
    n = lax.axis_size("core")
    return lax.ppermute(x, "core", [(i, i ^ 1) for i in range(n)])


def gather_rows_deduped(x):
    core = lax.axis_index("core")
    rows, cols = x.shape
    half = cols // 2
    partner = core_swap(x)
    pair = jnp.where(core == 0, jnp.concatenate([x, partner]), jnp.concatenate([partner, x]))
    mine = lax.dynamic_slice_in_dim(pair, core * half, half, axis=1)
    gathered = lax.all_gather(mine, "chip", axis=0, tiled=True)
    other = core_swap(gathered)
    return jnp.where(
        core == 0,
        jnp.concatenate([gathered, other], axis=1),
        jnp.concatenate([other, gathered], axis=1),
    )


def halo(shard):
    count = lax.axis_size("chip") * lax.axis_size("core")
    up = [(i, i + 1) for i in range(count - 1)]
    down = [(j, i) for i, j in up]
    before = lax.ppermute(shard, SEQ, up)
    after = lax.ppermute(shard, SEQ, down)
    return before, after


def _attn_kernel(live_ref, q_ref, k_ref, v_ref, up_ref, attn_ref, dq_ref, dk_ref, dv_ref):
    scale = 1.0 / math.sqrt(q_ref.shape[-1])
    q = q_ref[...]
    k = k_ref[...]
    v = v_ref[...]
    up = up_ref[...]
    nt = (((1,), (1,)), ((), ()))
    tn = (((0,), (0,)), ((), ()))
    scores = lax.dot_general(q, k, nt, preferred_element_type=jnp.float32) * scale
    scores = jnp.where(live_ref[...] > 0, scores, NEG_FILL)
    top = jnp.max(scores, axis=-1, keepdims=True)
    raised = jnp.exp(scores - top)
    probs = raised / jnp.sum(raised, axis=-1, keepdims=True)
    probs_b = probs.astype(jnp.bfloat16)
    attn_ref[...] = jnp.dot(probs_b, v, preferred_element_type=jnp.float32).astype(attn_ref.dtype)
    dv_ref[...] = lax.dot_general(probs_b, up, tn, preferred_element_type=jnp.float32)
    dprobs = lax.dot_general(up, v, nt, preferred_element_type=jnp.float32)
    rowdot = jnp.sum(probs * dprobs, axis=-1, keepdims=True)
    dscores = (scale * probs * (dprobs - rowdot)).astype(jnp.bfloat16)
    dq_ref[...] = jnp.dot(dscores, k, preferred_element_type=jnp.float32).astype(dq_ref.dtype)
    dk_ref[...] = lax.dot_general(dscores, q, tn, preferred_element_type=jnp.float32)

def attention(live, q, k, v, up, heads):
    rows, features = q.shape
    keys_n = k.shape[0]
    hd = features // heads
    qspec = pl.BlockSpec((rows, hd), lambda h: (0, h))
    kspec = pl.BlockSpec((keys_n, hd), lambda h: (0, h))
    return pl.pallas_call(
        _attn_kernel,
        grid=(heads,),
        in_specs=[pl.BlockSpec((1, keys_n), lambda h: (0, 0)), qspec, kspec, kspec, qspec],
        out_specs=[qspec, qspec, kspec, kspec],
        out_shape=[
            jax.ShapeDtypeStruct((rows, features), jnp.bfloat16),
            jax.ShapeDtypeStruct((rows, features), jnp.bfloat16),
            jax.ShapeDtypeStruct((keys_n, features), jnp.float32),
            jax.ShapeDtypeStruct((keys_n, features), jnp.float32),
        ],
    )(live, q, k, v, up)


def local(query, keys, values, out_weight, grad_out, global_blocks, random_blocks):
    tok_rows, feature_count = query.shape
    hd = feature_count // H
    blocks_dev = tok_rows // BLK
    count = lax.axis_size("chip") * lax.axis_size("core")
    total_blocks = blocks_dev * count
    device = flat_index()

    grad_out_all = gather_rows_deduped(grad_out)
    weight_all = lax.all_gather(out_weight, SEQ, axis=0, tiled=True)

    paired = jnp.stack([keys, values])
    before, after = halo(paired)
    extended = jnp.concatenate([before, paired, after], axis=1)

    slots = global_blocks.shape[0]
    owners = global_blocks // blocks_dev
    masked = []
    for g in range(slots):
        start = (global_blocks[g] % blocks_dev) * BLK
        block = lax.dynamic_slice_in_dim(paired, start, BLK, axis=1)
        masked.append(jnp.where(owners[g] == device, block, jnp.zeros_like(block)))
    global_kv = butterfly_sum(jnp.stack(masked))

    local_ids = jnp.arange(blocks_dev, dtype=jnp.int32)
    global_ids = device * blocks_dev + local_ids
    offsets = jnp.array([-1, 0, 1], dtype=jnp.int32)
    neighbour_ids = global_ids[:, None] + offsets[None, :]
    window_index = local_ids[:, None] + blocks_dev + offsets[None, :]
    window_live = (neighbour_ids >= 0) & (neighbour_ids < total_blocks)
    random_index = random_blocks - (device - 1) * blocks_dev
    ext_index = jnp.concatenate([window_index, random_index], axis=1)
    n_local = ext_index.shape[1]
    live = jnp.concatenate(
        [window_live, jnp.ones(random_blocks.shape, jnp.bool_), jnp.ones((blocks_dev, slots), jnp.bool_)],
        axis=1,
    )

    w_rows = out_weight.shape[0]
    upstream_cols = lax.dot_general(
        grad_out_all, out_weight, (((1,), (1,)), ((), ())), preferred_element_type=jnp.float32
    ).astype(jnp.bfloat16)
    upstream = lax.all_to_all(
        upstream_cols.reshape(count, tok_rows, w_rows), SEQ, 0, 0, tiled=False
    )
    upstream = jnp.swapaxes(upstream, 0, 1).reshape(tok_rows, feature_count)

    attn_rows, dq_rows = [], []
    grad_ext = [jnp.zeros((3 * blocks_dev * BLK, feature_count), jnp.float32) for _ in range(2)]
    global_local = None
    for b in range(blocks_dev):
        chosen = []
        for side in range(2):
            parts = [
                lax.dynamic_slice_in_dim(extended[side], ext_index[b, j] * BLK, BLK, axis=0)
                for j in range(n_local)
            ]
            parts += [global_kv[g, side] for g in range(slots)]
            chosen.append(jnp.concatenate(parts, axis=0))
        live_rows = jnp.repeat(live[b], BLK).astype(jnp.float32)[None]
        q = query[b * BLK : (b + 1) * BLK]
        up = upstream[b * BLK : (b + 1) * BLK]
        attn, dq, dk, dv = attention(live_rows, q, chosen[0], chosen[1], up, H)
        attn_rows.append(attn)
        dq_rows.append(dq)
        for side, grad in enumerate((dk, dv)):
            for j in range(n_local):
                start = ext_index[b, j] * BLK
                cur = lax.dynamic_slice_in_dim(grad_ext[side], start, BLK, axis=0)
                term = grad[j * BLK : (j + 1) * BLK]
                grad_ext[side] = lax.dynamic_update_slice_in_dim(
                    grad_ext[side], cur + term, start, axis=0
                )
        terms = jnp.stack(
            [dk[n_local * BLK :].reshape(slots, BLK, feature_count),
             dv[n_local * BLK :].reshape(slots, BLK, feature_count)],
            axis=1,
        )
        global_local = terms if global_local is None else global_local + terms
    grad_ext = jnp.stack(grad_ext)
    global_total = butterfly_sum(global_local, jnp.bfloat16)

    attn_out = jnp.concatenate(attn_rows, axis=0)
    layer_out = jnp.dot(attn_out, weight_all, preferred_element_type=jnp.float32).astype(
        jnp.bfloat16
    )
    attn_cols = lax.all_to_all(
        attn_out.reshape(tok_rows, count, w_rows), SEQ, 1, 0, tiled=False
    ).reshape(count * tok_rows, w_rows)
    grad_weight = lax.dot_general(
        attn_cols, grad_out_all, (((0,), (0,)), ((), ())), preferred_element_type=jnp.float32
    )

    rims = jnp.concatenate(
        [grad_ext[:, : blocks_dev * BLK], grad_ext[:, 2 * blocks_dev * BLK :]], axis=1
    ).astype(jnp.bfloat16)
    from_prev, from_next = halo(rims)
    own = grad_ext[:, blocks_dev * BLK : 2 * blocks_dev * BLK]
    own = own + from_prev[:, blocks_dev * BLK :].astype(jnp.float32)
    own = own + from_next[:, : blocks_dev * BLK].astype(jnp.float32)
    for g in range(slots):
        start = (global_blocks[g] % blocks_dev) * BLK
        add = jnp.where(owners[g] == device, global_total[g], jnp.zeros_like(global_total[g]))
        cur = lax.dynamic_slice_in_dim(own, start, BLK, axis=1)
        own = lax.dynamic_update_slice_in_dim(own, cur + add, start, axis=1)
    own = own.astype(jnp.bfloat16)
    grad_query = jnp.concatenate(dq_rows, axis=0)
    return (layer_out, grad_query, own[0], own[1], grad_weight)


def solution(mesh):
    groups, seq = mesh.devices.shape
    split = Mesh(mesh.devices.reshape(groups, seq // 2, 2), ("groups",) + SEQ)
    rows = P(("groups",) + SEQ, None)
    placed = (rows, rows, rows, P(SEQ, None), rows, P("groups"), rows)
    return jax.shard_map(
        local,
        mesh=split,
        in_specs=placed,
        out_specs=(rows, rows, rows, rows, rows),
        check_vma=False,
    )
```

```python
import math

import jax
import jax.numpy as jnp
from jax import lax
from jax.experimental import pallas as pl
from jax.sharding import Mesh
from jax.sharding import PartitionSpec as P

H = 8
BLK = 128
SEQ = ("chip", "core")


NEG_FILL = -1e30


def flat_index():
    return lax.axis_index("chip") * lax.axis_size("core") + lax.axis_index("core")


def xor_swap(x, level):
    if level == 0:
        n = lax.axis_size("core")
        return lax.ppermute(x, "core", [(i, i ^ 1) for i in range(n)])
    n = lax.axis_size("chip")
    m = 1 << (level - 1)
    return lax.ppermute(x, "chip", [(i, i ^ m) for i in range(n)])


def butterfly_sum(x, wire=None):
    count = lax.axis_size("chip") * lax.axis_size("core")
    levels = count.bit_length() - 1
    shape = x.shape
    buf = x.reshape(count, -1)
    d = flat_index()
    start, size = 0, count
    for k in range(levels):
        size //= 2
        upper = (d >> k) & 1
        mine = start + upper * size
        theirs = start + (1 - upper) * size
        send = lax.dynamic_slice_in_dim(buf, theirs, size, axis=0)
        if wire is not None:
            send = send.astype(wire)
        got = xor_swap(send, k).astype(buf.dtype)
        keep = lax.dynamic_slice_in_dim(buf, mine, size, axis=0)
        buf = lax.dynamic_update_slice_in_dim(buf, keep + got, mine, axis=0)
        start = mine
    if wire is not None:
        buf = buf.astype(wire)
    for k in reversed(range(levels)):
        upper = (d >> k) & 1
        seg = lax.dynamic_slice_in_dim(buf, start, size, axis=0)
        got = xor_swap(seg, k)
        other = start + (1 - 2 * upper) * size
        buf = lax.dynamic_update_slice_in_dim(buf, got, other, axis=0)
        start = jnp.minimum(start, other)
        size *= 2
    return buf.reshape(shape)


def halo(shard):
    count = lax.axis_size("chip") * lax.axis_size("core")
    up = [(i, i + 1) for i in range(count - 1)]
    down = [(j, i) for i, j in up]
    before = lax.ppermute(shard, SEQ, up)
    after = lax.ppermute(shard, SEQ, down)
    return before, after


def _attn_kernel(live_ref, q_ref, k_ref, v_ref, up_ref, attn_ref, dq_ref, dk_ref, dv_ref):
    scale = 1.0 / math.sqrt(q_ref.shape[-1])
    q = q_ref[...]
    k = k_ref[...]
    v = v_ref[...]
    up = up_ref[...]
    nt = (((1,), (1,)), ((), ()))
    tn = (((0,), (0,)), ((), ()))
    scores = lax.dot_general(q, k, nt, preferred_element_type=jnp.float32) * scale
    scores = jnp.where(live_ref[...] > 0, scores, NEG_FILL)
    top = jnp.max(scores, axis=-1, keepdims=True)
    raised = jnp.exp(scores - top)
    probs = raised / jnp.sum(raised, axis=-1, keepdims=True)
    probs_b = probs.astype(jnp.bfloat16)
    attn_ref[...] = jnp.dot(probs_b, v, preferred_element_type=jnp.float32).astype(attn_ref.dtype)
    dv_ref[...] = lax.dot_general(probs_b, up, tn, preferred_element_type=jnp.float32)
    dprobs = lax.dot_general(up, v, nt, preferred_element_type=jnp.float32)
    rowdot = jnp.sum(probs * dprobs, axis=-1, keepdims=True)
    dscores = (scale * probs * (dprobs - rowdot)).astype(jnp.bfloat16)
    dq_ref[...] = jnp.dot(dscores, k, preferred_element_type=jnp.float32).astype(dq_ref.dtype)
    dk_ref[...] = lax.dot_general(dscores, q, tn, preferred_element_type=jnp.float32)

def attention(live, q, k, v, up, heads):
    rows, features = q.shape
    keys_n = k.shape[0]
    hd = features // heads
    qspec = pl.BlockSpec((rows, hd), lambda h: (0, h))
    kspec = pl.BlockSpec((keys_n, hd), lambda h: (0, h))
    return pl.pallas_call(
        _attn_kernel,
        grid=(heads,),
        in_specs=[pl.BlockSpec((1, keys_n), lambda h: (0, 0)), qspec, kspec, kspec, qspec],
        out_specs=[qspec, qspec, kspec, kspec],
        out_shape=[
            jax.ShapeDtypeStruct((rows, features), jnp.bfloat16),
            jax.ShapeDtypeStruct((rows, features), jnp.bfloat16),
            jax.ShapeDtypeStruct((keys_n, features), jnp.float32),
            jax.ShapeDtypeStruct((keys_n, features), jnp.float32),
        ],
    )(live, q, k, v, up)


def local(query, keys, values, out_weight, grad_out, global_blocks, random_blocks):
    tok_rows, feature_count = query.shape
    hd = feature_count // H
    blocks_dev = tok_rows // BLK
    count = lax.axis_size("chip") * lax.axis_size("core")
    total_blocks = blocks_dev * count
    device = flat_index()

    grad_out_all = lax.all_gather(grad_out, SEQ, axis=0, tiled=True)
    weight_all = lax.all_gather(out_weight, SEQ, axis=0, tiled=True)

    paired = jnp.stack([keys, values])
    before, after = halo(paired)
    extended = jnp.concatenate([before, paired, after], axis=1)

    slots = global_blocks.shape[0]
    owners = global_blocks // blocks_dev
    masked = []
    for g in range(slots):
        start = (global_blocks[g] % blocks_dev) * BLK
        block = lax.dynamic_slice_in_dim(paired, start, BLK, axis=1)
        masked.append(jnp.where(owners[g] == device, block, jnp.zeros_like(block)))
    global_kv = butterfly_sum(jnp.stack(masked))

    local_ids = jnp.arange(blocks_dev, dtype=jnp.int32)
    global_ids = device * blocks_dev + local_ids
    offsets = jnp.array([-1, 0, 1], dtype=jnp.int32)
    neighbour_ids = global_ids[:, None] + offsets[None, :]
    window_index = local_ids[:, None] + blocks_dev + offsets[None, :]
    window_live = (neighbour_ids >= 0) & (neighbour_ids < total_blocks)
    random_index = random_blocks - (device - 1) * blocks_dev
    ext_index = jnp.concatenate([window_index, random_index], axis=1)
    n_local = ext_index.shape[1]
    live = jnp.concatenate(
        [window_live, jnp.ones(random_blocks.shape, jnp.bool_), jnp.ones((blocks_dev, slots), jnp.bool_)],
        axis=1,
    )

    w_rows = out_weight.shape[0]
    upstream_cols = lax.dot_general(
        grad_out_all, out_weight, (((1,), (1,)), ((), ())), preferred_element_type=jnp.float32
    ).astype(jnp.bfloat16)
    upstream = lax.all_to_all(
        upstream_cols.reshape(count, tok_rows, w_rows), SEQ, 0, 0, tiled=False
    )
    upstream = jnp.swapaxes(upstream, 0, 1).reshape(tok_rows, feature_count)

    attn_rows, dq_rows = [], []
    grad_ext = [jnp.zeros((3 * blocks_dev * BLK, feature_count), jnp.float32) for _ in range(2)]
    global_local = None
    for b in range(blocks_dev):
        chosen = []
        for side in range(2):
            parts = [
                lax.dynamic_slice_in_dim(extended[side], ext_index[b, j] * BLK, BLK, axis=0)
                for j in range(n_local)
            ]
            parts += [global_kv[g, side] for g in range(slots)]
            chosen.append(jnp.concatenate(parts, axis=0))
        live_rows = jnp.repeat(live[b], BLK).astype(jnp.float32)[None]
        q = query[b * BLK : (b + 1) * BLK]
        up = upstream[b * BLK : (b + 1) * BLK]
        attn, dq, dk, dv = attention(live_rows, q, chosen[0], chosen[1], up, H)
        attn_rows.append(attn)
        dq_rows.append(dq)
        for side, grad in enumerate((dk, dv)):
            for j in range(n_local):
                start = ext_index[b, j] * BLK
                cur = lax.dynamic_slice_in_dim(grad_ext[side], start, BLK, axis=0)
                term = grad[j * BLK : (j + 1) * BLK]
                grad_ext[side] = lax.dynamic_update_slice_in_dim(
                    grad_ext[side], cur + term, start, axis=0
                )
        terms = jnp.stack(
            [dk[n_local * BLK :].reshape(slots, BLK, feature_count),
             dv[n_local * BLK :].reshape(slots, BLK, feature_count)],
            axis=1,
        )
        global_local = terms if global_local is None else global_local + terms
    grad_ext = jnp.stack(grad_ext)
    global_total = butterfly_sum(global_local, jnp.bfloat16)

    attn_out = jnp.concatenate(attn_rows, axis=0)
    layer_out = jnp.dot(attn_out, weight_all, preferred_element_type=jnp.float32).astype(
        jnp.bfloat16
    )
    attn_cols = lax.all_to_all(
        attn_out.reshape(tok_rows, count, w_rows), SEQ, 1, 0, tiled=False
    ).reshape(count * tok_rows, w_rows)
    grad_weight = lax.dot_general(
        attn_cols, grad_out_all, (((0,), (0,)), ((), ())), preferred_element_type=jnp.float32
    )

    rims = jnp.concatenate(
        [grad_ext[:, : blocks_dev * BLK], grad_ext[:, 2 * blocks_dev * BLK :]], axis=1
    ).astype(jnp.bfloat16)
    from_prev, from_next = halo(rims)
    finished = []
    for side in range(2):
        own = grad_ext[side, blocks_dev * BLK : 2 * blocks_dev * BLK]
        own = own + from_prev[side, blocks_dev * BLK :].astype(jnp.float32)
        own = own + from_next[side, : blocks_dev * BLK].astype(jnp.float32)
        for g in range(slots):
            start = (global_blocks[g] % blocks_dev) * BLK
            total = global_total[g, side].astype(jnp.float32)
            add = jnp.where(owners[g] == device, total, jnp.zeros_like(total))
            cur = lax.dynamic_slice_in_dim(own, start, BLK, axis=0)
            own = lax.dynamic_update_slice_in_dim(own, cur + add, start, axis=0)
        finished.append(own.astype(jnp.bfloat16))
    grad_query = jnp.concatenate(dq_rows, axis=0)
    return (layer_out, grad_query, finished[0], finished[1], grad_weight)


def solution(mesh):
    groups, seq = mesh.devices.shape
    split = Mesh(mesh.devices.reshape(groups, seq // 2, 2), ("groups",) + SEQ)
    rows = P(("groups",) + SEQ, None)
    placed = (rows, rows, rows, P(SEQ, None), rows, P("groups"), rows)
    return jax.shard_map(
        local,
        mesh=split,
        in_specs=placed,
        out_specs=(rows, rows, rows, rows, rows),
        check_vma=False,
    )
```

```python
import math

import jax
import jax.numpy as jnp
from jax import lax
from jax.experimental import pallas as pl
from jax.sharding import Mesh
from jax.sharding import PartitionSpec as P

H = 8
BLK = 128
SEQ = ("chip", "core")


NEG_FILL = -1e30


def flat_index():
    return lax.axis_index("chip") * lax.axis_size("core") + lax.axis_index("core")


def xor_swap(x, level):
    if level == 0:
        n = lax.axis_size("core")
        return lax.ppermute(x, "core", [(i, i ^ 1) for i in range(n)])
    n = lax.axis_size("chip")
    m = 1 << (level - 1)
    return lax.ppermute(x, "chip", [(i, i ^ m) for i in range(n)])


def butterfly_sum(x, wire=None):
    count = lax.axis_size("chip") * lax.axis_size("core")
    levels = count.bit_length() - 1
    shape = x.shape
    flat = x.reshape(count, -1)
    d = flat_index()
    parts = flat
    for k in range(levels):
        half = parts.shape[0] // 2
        lo, hi = parts[:half], parts[half:]
        upper = ((d >> k) & 1) == 1
        send = jnp.where(upper, lo, hi)
        keep = jnp.where(upper, hi, lo)
        if wire is not None:
            send = send.astype(wire)
        parts = keep + xor_swap(send, k).astype(keep.dtype)
    for k in reversed(range(levels)):
        upper = ((d >> k) & 1) == 1
        if wire is not None and k == levels - 1:
            parts = parts.astype(wire)
        other = xor_swap(parts, k)
        parts = jnp.where(
            upper, jnp.concatenate([other, parts]), jnp.concatenate([parts, other])
        )
    return parts.reshape(shape)


def halo(shard):
    count = lax.axis_size("chip") * lax.axis_size("core")
    up = [(i, i + 1) for i in range(count - 1)]
    down = [(j, i) for i, j in up]
    before = lax.ppermute(shard, SEQ, up)
    after = lax.ppermute(shard, SEQ, down)
    return before, after


def _attn_kernel(live_ref, q_ref, k_ref, v_ref, up_ref, attn_ref, dq_ref, dk_ref, dv_ref):
    scale = 1.0 / math.sqrt(q_ref.shape[-1])
    q = q_ref[...]
    k = k_ref[...]
    v = v_ref[...]
    up = up_ref[...]
    nt = (((1,), (1,)), ((), ()))
    tn = (((0,), (0,)), ((), ()))
    scores = lax.dot_general(q, k, nt, preferred_element_type=jnp.float32) * scale
    scores = jnp.where(live_ref[...] > 0, scores, NEG_FILL)
    top = jnp.max(scores, axis=-1, keepdims=True)
    raised = jnp.exp(scores - top)
    probs = raised / jnp.sum(raised, axis=-1, keepdims=True)
    probs_b = probs.astype(jnp.bfloat16)
    attn_ref[...] = jnp.dot(probs_b, v, preferred_element_type=jnp.float32).astype(attn_ref.dtype)
    dv_ref[...] = lax.dot_general(probs_b, up, tn, preferred_element_type=jnp.float32)
    dprobs = lax.dot_general(up, v, nt, preferred_element_type=jnp.float32)
    rowdot = jnp.sum(probs * dprobs, axis=-1, keepdims=True)
    dscores = (scale * probs * (dprobs - rowdot)).astype(jnp.bfloat16)
    dq_ref[...] = jnp.dot(dscores, k, preferred_element_type=jnp.float32).astype(dq_ref.dtype)
    dk_ref[...] = lax.dot_general(dscores, q, tn, preferred_element_type=jnp.float32)

def attention(live, q, k, v, up, heads):
    rows, features = q.shape
    keys_n = k.shape[0]
    hd = features // heads
    qspec = pl.BlockSpec((rows, hd), lambda h: (0, h))
    kspec = pl.BlockSpec((keys_n, hd), lambda h: (0, h))
    return pl.pallas_call(
        _attn_kernel,
        grid=(heads,),
        in_specs=[pl.BlockSpec((1, keys_n), lambda h: (0, 0)), qspec, kspec, kspec, qspec],
        out_specs=[qspec, qspec, kspec, kspec],
        out_shape=[
            jax.ShapeDtypeStruct((rows, features), jnp.bfloat16),
            jax.ShapeDtypeStruct((rows, features), jnp.bfloat16),
            jax.ShapeDtypeStruct((keys_n, features), jnp.float32),
            jax.ShapeDtypeStruct((keys_n, features), jnp.float32),
        ],
    )(live, q, k, v, up)


def local(query, keys, values, out_weight, grad_out, global_blocks, random_blocks):
    tok_rows, feature_count = query.shape
    hd = feature_count // H
    blocks_dev = tok_rows // BLK
    count = lax.axis_size("chip") * lax.axis_size("core")
    total_blocks = blocks_dev * count
    device = flat_index()

    weight_all = lax.all_gather(out_weight, SEQ, axis=0, tiled=True)

    paired = jnp.stack([keys, values])
    before, after = halo(paired)
    extended = jnp.concatenate([before, paired, after], axis=1)

    slots = global_blocks.shape[0]
    owners = global_blocks // blocks_dev
    masked = []
    for g in range(slots):
        start = (global_blocks[g] % blocks_dev) * BLK
        block = lax.dynamic_slice_in_dim(paired, start, BLK, axis=1)
        masked.append(jnp.where(owners[g] == device, block, jnp.zeros_like(block)))
    global_kv = butterfly_sum(jnp.stack(masked))

    local_ids = jnp.arange(blocks_dev, dtype=jnp.int32)
    global_ids = device * blocks_dev + local_ids
    offsets = jnp.array([-1, 0, 1], dtype=jnp.int32)
    neighbour_ids = global_ids[:, None] + offsets[None, :]
    window_index = local_ids[:, None] + blocks_dev + offsets[None, :]
    window_live = (neighbour_ids >= 0) & (neighbour_ids < total_blocks)
    random_index = random_blocks - (device - 1) * blocks_dev
    ext_index = jnp.concatenate([window_index, random_index], axis=1)
    n_local = ext_index.shape[1]
    live = jnp.concatenate(
        [window_live, jnp.ones(random_blocks.shape, jnp.bool_), jnp.ones((blocks_dev, slots), jnp.bool_)],
        axis=1,
    )

    upstream = lax.dot_general(
        grad_out, weight_all, (((1,), (1,)), ((), ())), preferred_element_type=jnp.float32
    ).astype(jnp.bfloat16)

    attn_rows, dq_rows = [], []
    grad_ext = [jnp.zeros((3 * blocks_dev * BLK, feature_count), jnp.float32) for _ in range(2)]
    global_local = None
    for b in range(blocks_dev):
        chosen = []
        for side in range(2):
            parts = [
                lax.dynamic_slice_in_dim(extended[side], ext_index[b, j] * BLK, BLK, axis=0)
                for j in range(n_local)
            ]
            parts += [global_kv[g, side] for g in range(slots)]
            chosen.append(jnp.concatenate(parts, axis=0))
        live_rows = jnp.repeat(live[b], BLK).astype(jnp.float32)[None]
        q = query[b * BLK : (b + 1) * BLK]
        up = upstream[b * BLK : (b + 1) * BLK]
        attn, dq, dk, dv = attention(live_rows, q, chosen[0], chosen[1], up, H)
        attn_rows.append(attn)
        dq_rows.append(dq)
        for side, grad in enumerate((dk, dv)):
            for j in range(n_local):
                start = ext_index[b, j] * BLK
                cur = lax.dynamic_slice_in_dim(grad_ext[side], start, BLK, axis=0)
                term = grad[j * BLK : (j + 1) * BLK]
                grad_ext[side] = lax.dynamic_update_slice_in_dim(
                    grad_ext[side], cur + term, start, axis=0
                )
        terms = jnp.stack(
            [dk[n_local * BLK :].reshape(slots, BLK, feature_count),
             dv[n_local * BLK :].reshape(slots, BLK, feature_count)],
            axis=1,
        )
        global_local = terms if global_local is None else global_local + terms
    grad_ext = jnp.stack(grad_ext)
    global_total = butterfly_sum(global_local, jnp.bfloat16)

    attn_out = jnp.concatenate(attn_rows, axis=0)
    layer_out = jnp.dot(attn_out, weight_all, preferred_element_type=jnp.float32).astype(
        jnp.bfloat16
    )
    partial = lax.dot_general(
        attn_out, grad_out, (((0,), (0,)), ((), ())), preferred_element_type=jnp.float32
    )
    grad_weight = lax.psum_scatter(
        partial.astype(jnp.bfloat16), SEQ, scatter_dimension=0, tiled=True
    ).astype(jnp.float32)

    rims = jnp.concatenate(
        [grad_ext[:, : blocks_dev * BLK], grad_ext[:, 2 * blocks_dev * BLK :]], axis=1
    ).astype(jnp.bfloat16)
    from_prev, from_next = halo(rims)
    own = grad_ext[:, blocks_dev * BLK : 2 * blocks_dev * BLK]
    own = own + from_prev[:, blocks_dev * BLK :].astype(jnp.float32)
    own = own + from_next[:, : blocks_dev * BLK].astype(jnp.float32)
    for g in range(slots):
        start = (global_blocks[g] % blocks_dev) * BLK
        add = jnp.where(owners[g] == device, global_total[g], jnp.zeros_like(global_total[g]))
        cur = lax.dynamic_slice_in_dim(own, start, BLK, axis=1)
        own = lax.dynamic_update_slice_in_dim(own, cur + add, start, axis=1)
    own = own.astype(jnp.bfloat16)
    grad_query = jnp.concatenate(dq_rows, axis=0)
    return (layer_out, grad_query, own[0], own[1], grad_weight)


def solution(mesh):
    groups, seq = mesh.devices.shape
    split = Mesh(mesh.devices.reshape(groups, seq // 2, 2), ("groups",) + SEQ)
    rows = P(("groups",) + SEQ, None)
    placed = (rows, rows, rows, P(SEQ, None), rows, P("groups"), rows)
    return jax.shard_map(
        local,
        mesh=split,
        in_specs=placed,
        out_specs=(rows, rows, rows, rows, rows),
        check_vma=False,
    )
```

```python
import math

import jax
import jax.numpy as jnp
from jax import lax
from jax.experimental import pallas as pl
from jax.sharding import Mesh
from jax.sharding import PartitionSpec as P

H = 8
BLK = 128
SEQ = ("chip", "core")


NEG_FILL = -1e30


def flat_index():
    return lax.axis_index("chip") * lax.axis_size("core") + lax.axis_index("core")


def xor_swap(x, level):
    if level == 0:
        n = lax.axis_size("core")
        return lax.ppermute(x, "core", [(i, i ^ 1) for i in range(n)])
    n = lax.axis_size("chip")
    m = 1 << (level - 1)
    return lax.ppermute(x, "chip", [(i, i ^ m) for i in range(n)])


def butterfly_sum(x, wire=None):
    count = lax.axis_size("chip") * lax.axis_size("core")
    levels = count.bit_length() - 1
    shape = x.shape
    flat = x.reshape(count, -1)
    d = flat_index()
    parts = flat
    for k in range(levels):
        half = parts.shape[0] // 2
        lo, hi = parts[:half], parts[half:]
        upper = ((d >> k) & 1) == 1
        send = jnp.where(upper, lo, hi)
        keep = jnp.where(upper, hi, lo)
        if wire is not None:
            send = send.astype(wire)
        parts = keep + xor_swap(send, k).astype(keep.dtype)
    for k in reversed(range(levels)):
        upper = ((d >> k) & 1) == 1
        if wire is not None and k == levels - 1:
            parts = parts.astype(wire)
        other = xor_swap(parts, k)
        parts = jnp.where(
            upper, jnp.concatenate([other, parts]), jnp.concatenate([parts, other])
        )
    return parts.reshape(shape)


def halo(shard):
    count = lax.axis_size("chip") * lax.axis_size("core")
    up = [(i, i + 1) for i in range(count - 1)]
    down = [(j, i) for i, j in up]
    before = lax.ppermute(shard, SEQ, up)
    after = lax.ppermute(shard, SEQ, down)
    return before, after


def _attn_kernel(live_ref, q_ref, k_ref, v_ref, up_ref, attn_ref, dq_ref, dk_ref, dv_ref):
    scale = 1.0 / math.sqrt(q_ref.shape[-1])
    q = q_ref[...]
    k = k_ref[...]
    v = v_ref[...]
    up = up_ref[...]
    nt = (((1,), (1,)), ((), ()))
    tn = (((0,), (0,)), ((), ()))
    scores = lax.dot_general(q, k, nt, preferred_element_type=jnp.float32) * scale
    scores = jnp.where(live_ref[...] > 0, scores, NEG_FILL)
    top = jnp.max(scores, axis=-1, keepdims=True)
    raised = jnp.exp(scores - top)
    probs = raised / jnp.sum(raised, axis=-1, keepdims=True)
    probs_b = probs.astype(jnp.bfloat16)
    attn_ref[...] = jnp.dot(probs_b, v, preferred_element_type=jnp.float32).astype(attn_ref.dtype)
    dv_ref[...] = lax.dot_general(probs_b, up, tn, preferred_element_type=jnp.float32)
    dprobs = lax.dot_general(up, v, nt, preferred_element_type=jnp.float32)
    rowdot = jnp.sum(probs * dprobs, axis=-1, keepdims=True)
    dscores = (scale * probs * (dprobs - rowdot)).astype(jnp.bfloat16)
    dq_ref[...] = jnp.dot(dscores, k, preferred_element_type=jnp.float32).astype(dq_ref.dtype)
    dk_ref[...] = lax.dot_general(dscores, q, tn, preferred_element_type=jnp.float32)

def attention(live, q, k, v, up, heads):
    rows, features = q.shape
    keys_n = k.shape[0]
    hd = features // heads
    qspec = pl.BlockSpec((rows, hd), lambda h: (0, h))
    kspec = pl.BlockSpec((keys_n, hd), lambda h: (0, h))
    return pl.pallas_call(
        _attn_kernel,
        grid=(heads,),
        in_specs=[pl.BlockSpec((1, keys_n), lambda h: (0, 0)), qspec, kspec, kspec, qspec],
        out_specs=[qspec, qspec, kspec, kspec],
        out_shape=[
            jax.ShapeDtypeStruct((rows, features), jnp.bfloat16),
            jax.ShapeDtypeStruct((rows, features), jnp.bfloat16),
            jax.ShapeDtypeStruct((keys_n, features), jnp.float32),
            jax.ShapeDtypeStruct((keys_n, features), jnp.float32),
        ],
    )(live, q, k, v, up)


def local(query, keys, values, out_weight, grad_out, global_blocks, random_blocks):
    tok_rows, feature_count = query.shape
    hd = feature_count // H
    blocks_dev = tok_rows // BLK
    count = lax.axis_size("chip") * lax.axis_size("core")
    total_blocks = blocks_dev * count
    device = flat_index()

    grad_out_all = lax.all_gather(grad_out, SEQ, axis=0, tiled=True)
    weight_all = lax.all_gather(out_weight, SEQ, axis=0, tiled=True)

    paired = jnp.stack([keys, values])
    before, after = halo(paired)
    extended = jnp.concatenate([before, paired, after], axis=1)

    slots = global_blocks.shape[0]
    owners = global_blocks // blocks_dev
    masked = []
    for g in range(slots):
        start = (global_blocks[g] % blocks_dev) * BLK
        block = lax.dynamic_slice_in_dim(paired, start, BLK, axis=1)
        masked.append(jnp.where(owners[g] == device, block, jnp.zeros_like(block)))
    global_kv = butterfly_sum(jnp.stack(masked))

    local_ids = jnp.arange(blocks_dev, dtype=jnp.int32)
    global_ids = device * blocks_dev + local_ids
    offsets = jnp.array([-1, 0, 1], dtype=jnp.int32)
    neighbour_ids = global_ids[:, None] + offsets[None, :]
    window_index = local_ids[:, None] + blocks_dev + offsets[None, :]
    window_live = (neighbour_ids >= 0) & (neighbour_ids < total_blocks)
    random_index = random_blocks - (device - 1) * blocks_dev
    ext_index = jnp.concatenate([window_index, random_index], axis=1)
    n_local = ext_index.shape[1]
    live = jnp.concatenate(
        [window_live, jnp.ones(random_blocks.shape, jnp.bool_), jnp.ones((blocks_dev, slots), jnp.bool_)],
        axis=1,
    )

    w_rows = out_weight.shape[0]
    upstream_cols = lax.dot_general(
        grad_out_all, out_weight, (((1,), (1,)), ((), ())), preferred_element_type=jnp.float32
    ).astype(jnp.bfloat16)
    upstream = lax.all_to_all(
        upstream_cols.reshape(count, tok_rows, w_rows), SEQ, 0, 0, tiled=False
    )
    upstream = jnp.swapaxes(upstream, 0, 1).reshape(tok_rows, feature_count)

    attn_rows, dq_rows = [], []
    grad_ext = [jnp.zeros((3 * blocks_dev * BLK, feature_count), jnp.float32) for _ in range(2)]
    global_local = None
    for b in range(blocks_dev):
        chosen = []
        for side in range(2):
            parts = [
                lax.dynamic_slice_in_dim(extended[side], ext_index[b, j] * BLK, BLK, axis=0)
                for j in range(n_local)
            ]
            parts += [global_kv[g, side] for g in range(slots)]
            chosen.append(jnp.concatenate(parts, axis=0))
        live_rows = jnp.repeat(live[b], BLK).astype(jnp.float32)[None]
        q = query[b * BLK : (b + 1) * BLK]
        up = upstream[b * BLK : (b + 1) * BLK]
        attn, dq, dk, dv = attention(live_rows, q, chosen[0], chosen[1], up, H)
        attn_rows.append(attn)
        dq_rows.append(dq)
        for side, grad in enumerate((dk, dv)):
            for j in range(n_local):
                start = ext_index[b, j] * BLK
                cur = lax.dynamic_slice_in_dim(grad_ext[side], start, BLK, axis=0)
                term = grad[j * BLK : (j + 1) * BLK]
                grad_ext[side] = lax.dynamic_update_slice_in_dim(
                    grad_ext[side], cur + term, start, axis=0
                )
        terms = jnp.stack(
            [dk[n_local * BLK :].reshape(slots, BLK, feature_count),
             dv[n_local * BLK :].reshape(slots, BLK, feature_count)],
            axis=1,
        )
        global_local = terms if global_local is None else global_local + terms
    grad_ext = jnp.stack(grad_ext)
    global_total = butterfly_sum(global_local, jnp.bfloat16)

    attn_out = jnp.concatenate(attn_rows, axis=0)
    layer_out = jnp.dot(attn_out, weight_all, preferred_element_type=jnp.float32).astype(
        jnp.bfloat16
    )
    attn_cols = lax.all_to_all(
        attn_out.reshape(tok_rows, count, w_rows), SEQ, 1, 0, tiled=False
    ).reshape(count * tok_rows, w_rows)
    grad_weight = lax.dot_general(
        attn_cols, grad_out_all, (((0,), (0,)), ((), ())), preferred_element_type=jnp.float32
    )

    rims = jnp.concatenate(
        [grad_ext[:, : blocks_dev * BLK], grad_ext[:, 2 * blocks_dev * BLK :]], axis=1
    ).astype(jnp.bfloat16)
    from_prev, from_next = halo(rims)
    finished = []
    for side in range(2):
        own = grad_ext[side, blocks_dev * BLK : 2 * blocks_dev * BLK]
        own = own + from_prev[side, blocks_dev * BLK :].astype(jnp.float32)
        own = own + from_next[side, : blocks_dev * BLK].astype(jnp.float32)
        for g in range(slots):
            start = (global_blocks[g] % blocks_dev) * BLK
            total = global_total[g, side]
            add = jnp.where(owners[g] == device, total, jnp.zeros_like(total))
            cur = lax.dynamic_slice_in_dim(own, start, BLK, axis=0)
            own = lax.dynamic_update_slice_in_dim(own, cur + add, start, axis=0)
        finished.append(own.astype(jnp.bfloat16))
    grad_query = jnp.concatenate(dq_rows, axis=0)
    return (layer_out, grad_query, finished[0], finished[1], grad_weight)


def solution(mesh):
    groups, seq = mesh.devices.shape
    split = Mesh(mesh.devices.reshape(groups, seq // 2, 2), ("groups",) + SEQ)
    rows = P(("groups",) + SEQ, None)
    placed = (rows, rows, rows, P(SEQ, None), rows, P("groups"), rows)
    return jax.shard_map(
        local,
        mesh=split,
        in_specs=placed,
        out_specs=(rows, rows, rows, rows, rows),
        check_vma=False,
    )
```

```python
import math

import jax
import jax.numpy as jnp
from jax import lax
from jax.experimental import pallas as pl
from jax.sharding import Mesh
from jax.sharding import PartitionSpec as P

H = 8
BLK = 128
SEQ = ("chip", "core")


NEG_FILL = -1e30


def flat_index():
    return lax.axis_index("chip") * lax.axis_size("core") + lax.axis_index("core")


def xor_swap(x, level):
    if level == 0:
        n = lax.axis_size("core")
        return lax.ppermute(x, "core", [(i, i ^ 1) for i in range(n)])
    n = lax.axis_size("chip")
    m = 1 << (level - 1)
    return lax.ppermute(x, "chip", [(i, i ^ m) for i in range(n)])


def butterfly_halves(x, wire=None):
    count = lax.axis_size("chip") * lax.axis_size("core")
    levels = count.bit_length() - 1
    d = flat_index()
    parts = x.reshape(count, -1)
    for k in range(levels):
        half = parts.shape[0] // 2
        lo, hi = parts[:half], parts[half:]
        upper = ((d >> k) & 1) == 1
        send = jnp.where(upper, lo, hi)
        keep = jnp.where(upper, hi, lo)
        if wire is not None:
            send = send.astype(wire)
        parts = keep + xor_swap(send, k).astype(keep.dtype)
    if wire is not None:
        parts = parts.astype(wire)
    return parts


def butterfly_doubling(parts, shape):
    count = lax.axis_size("chip") * lax.axis_size("core")
    levels = count.bit_length() - 1
    d = flat_index()
    for k in reversed(range(levels)):
        upper = ((d >> k) & 1) == 1
        other = xor_swap(parts, k)
        parts = jnp.where(
            upper, jnp.concatenate([other, parts]), jnp.concatenate([parts, other])
        )
    return parts.reshape(shape)


def butterfly_sum(x, wire=None):
    return butterfly_doubling(butterfly_halves(x, wire), x.shape)


def halo(shard):
    count = lax.axis_size("chip") * lax.axis_size("core")
    up = [(i, i + 1) for i in range(count - 1)]
    down = [(j, i) for i, j in up]
    before = lax.ppermute(shard, SEQ, up)
    after = lax.ppermute(shard, SEQ, down)
    return before, after


def _attn_kernel(live_ref, q_ref, k_ref, v_ref, up_ref, attn_ref, dq_ref, dk_ref, dv_ref):
    scale = 1.0 / math.sqrt(q_ref.shape[-1])
    q = q_ref[...]
    k = k_ref[...]
    v = v_ref[...]
    up = up_ref[...]
    nt = (((1,), (1,)), ((), ()))
    tn = (((0,), (0,)), ((), ()))
    scores = lax.dot_general(q, k, nt, preferred_element_type=jnp.float32) * scale
    scores = jnp.where(live_ref[...] > 0, scores, NEG_FILL)
    top = jnp.max(scores, axis=-1, keepdims=True)
    raised = jnp.exp(scores - top)
    probs = raised / jnp.sum(raised, axis=-1, keepdims=True)
    probs_b = probs.astype(jnp.bfloat16)
    attn_ref[...] = jnp.dot(probs_b, v, preferred_element_type=jnp.float32).astype(attn_ref.dtype)
    dv_ref[...] = lax.dot_general(probs_b, up, tn, preferred_element_type=jnp.float32)
    dprobs = lax.dot_general(up, v, nt, preferred_element_type=jnp.float32)
    rowdot = jnp.sum(probs * dprobs, axis=-1, keepdims=True)
    dscores = (scale * probs * (dprobs - rowdot)).astype(jnp.bfloat16)
    dq_ref[...] = jnp.dot(dscores, k, preferred_element_type=jnp.float32).astype(dq_ref.dtype)
    dk_ref[...] = lax.dot_general(dscores, q, tn, preferred_element_type=jnp.float32)

def attention(live, q, k, v, up, heads):
    rows, features = q.shape
    keys_n = k.shape[0]
    hd = features // heads
    qspec = pl.BlockSpec((rows, hd), lambda h: (0, h))
    kspec = pl.BlockSpec((keys_n, hd), lambda h: (0, h))
    return pl.pallas_call(
        _attn_kernel,
        grid=(heads,),
        in_specs=[pl.BlockSpec((1, keys_n), lambda h: (0, 0)), qspec, kspec, kspec, qspec],
        out_specs=[qspec, qspec, kspec, kspec],
        out_shape=[
            jax.ShapeDtypeStruct((rows, features), jnp.bfloat16),
            jax.ShapeDtypeStruct((rows, features), jnp.bfloat16),
            jax.ShapeDtypeStruct((keys_n, features), jnp.float32),
            jax.ShapeDtypeStruct((keys_n, features), jnp.float32),
        ],
    )(live, q, k, v, up)


def local(query, keys, values, out_weight, grad_out, global_blocks, random_blocks):
    tok_rows, feature_count = query.shape
    hd = feature_count // H
    blocks_dev = tok_rows // BLK
    count = lax.axis_size("chip") * lax.axis_size("core")
    total_blocks = blocks_dev * count
    device = flat_index()

    grad_out_all = lax.all_gather(grad_out, SEQ, axis=0, tiled=True)
    weight_all = lax.all_gather(out_weight, SEQ, axis=0, tiled=True)

    paired = jnp.stack([keys, values])
    before, after = halo(paired)
    extended = jnp.concatenate([before, paired, after], axis=1)

    slots = global_blocks.shape[0]
    owners = global_blocks // blocks_dev
    masked = []
    for g in range(slots):
        start = (global_blocks[g] % blocks_dev) * BLK
        block = lax.dynamic_slice_in_dim(paired, start, BLK, axis=1)
        masked.append(jnp.where(owners[g] == device, block, jnp.zeros_like(block)))
    global_kv = butterfly_sum(jnp.stack(masked))

    local_ids = jnp.arange(blocks_dev, dtype=jnp.int32)
    global_ids = device * blocks_dev + local_ids
    offsets = jnp.array([-1, 0, 1], dtype=jnp.int32)
    neighbour_ids = global_ids[:, None] + offsets[None, :]
    window_index = local_ids[:, None] + blocks_dev + offsets[None, :]
    window_live = (neighbour_ids >= 0) & (neighbour_ids < total_blocks)
    random_index = random_blocks - (device - 1) * blocks_dev
    ext_index = jnp.concatenate([window_index, random_index], axis=1)
    n_local = ext_index.shape[1]
    live = jnp.concatenate(
        [window_live, jnp.ones(random_blocks.shape, jnp.bool_), jnp.ones((blocks_dev, slots), jnp.bool_)],
        axis=1,
    )

    w_rows = out_weight.shape[0]
    upstream_cols = lax.dot_general(
        grad_out_all, out_weight, (((1,), (1,)), ((), ())), preferred_element_type=jnp.float32
    ).astype(jnp.bfloat16)
    upstream = lax.all_to_all(
        upstream_cols.reshape(count, tok_rows, w_rows), SEQ, 0, 0, tiled=False
    )
    upstream = jnp.swapaxes(upstream, 0, 1).reshape(tok_rows, feature_count)

    attn_rows, dq_rows = [], []
    grad_ext = [jnp.zeros((3 * blocks_dev * BLK, feature_count), jnp.float32) for _ in range(2)]
    global_local = None
    for b in range(blocks_dev):
        chosen = []
        for side in range(2):
            parts = [
                lax.dynamic_slice_in_dim(extended[side], ext_index[b, j] * BLK, BLK, axis=0)
                for j in range(n_local)
            ]
            parts += [global_kv[g, side] for g in range(slots)]
            chosen.append(jnp.concatenate(parts, axis=0))
        live_rows = jnp.repeat(live[b], BLK).astype(jnp.float32)[None]
        q = query[b * BLK : (b + 1) * BLK]
        up = upstream[b * BLK : (b + 1) * BLK]
        attn, dq, dk, dv = attention(live_rows, q, chosen[0], chosen[1], up, H)
        attn_rows.append(attn)
        dq_rows.append(dq)
        for side, grad in enumerate((dk, dv)):
            for j in range(n_local):
                start = ext_index[b, j] * BLK
                cur = lax.dynamic_slice_in_dim(grad_ext[side], start, BLK, axis=0)
                term = grad[j * BLK : (j + 1) * BLK]
                grad_ext[side] = lax.dynamic_update_slice_in_dim(
                    grad_ext[side], cur + term, start, axis=0
                )
        terms = jnp.stack(
            [dk[n_local * BLK :].reshape(slots, BLK, feature_count),
             dv[n_local * BLK :].reshape(slots, BLK, feature_count)],
            axis=1,
        )
        global_local = terms if global_local is None else global_local + terms
    grad_ext = jnp.stack(grad_ext)
    attn_out = jnp.concatenate(attn_rows, axis=0)
    attn_cols = lax.all_to_all(
        attn_out.reshape(tok_rows, count, w_rows), SEQ, 1, 0, tiled=False
    ).reshape(count * tok_rows, w_rows)
    halves = butterfly_halves(global_local, jnp.bfloat16)
    attn_cols, halves = lax.optimization_barrier((attn_cols, halves))
    global_total = butterfly_doubling(halves, global_local.shape)

    layer_out = jnp.dot(attn_out, weight_all, preferred_element_type=jnp.float32).astype(
        jnp.bfloat16
    )
    grad_weight = lax.dot_general(
        attn_cols, grad_out_all, (((0,), (0,)), ((), ())), preferred_element_type=jnp.float32
    )

    rims = jnp.concatenate(
        [grad_ext[:, : blocks_dev * BLK], grad_ext[:, 2 * blocks_dev * BLK :]], axis=1
    ).astype(jnp.bfloat16)
    from_prev, from_next = halo(rims)
    finished = []
    for side in range(2):
        own = grad_ext[side, blocks_dev * BLK : 2 * blocks_dev * BLK]
        own = own + from_prev[side, blocks_dev * BLK :].astype(jnp.float32)
        own = own + from_next[side, : blocks_dev * BLK].astype(jnp.float32)
        for g in range(slots):
            start = (global_blocks[g] % blocks_dev) * BLK
            total = global_total[g, side]
            add = jnp.where(owners[g] == device, total, jnp.zeros_like(total))
            cur = lax.dynamic_slice_in_dim(own, start, BLK, axis=0)
            own = lax.dynamic_update_slice_in_dim(own, cur + add, start, axis=0)
        finished.append(own.astype(jnp.bfloat16))
    grad_query = jnp.concatenate(dq_rows, axis=0)
    return (layer_out, grad_query, finished[0], finished[1], grad_weight)


def solution(mesh):
    groups, seq = mesh.devices.shape
    split = Mesh(mesh.devices.reshape(groups, seq // 2, 2), ("groups",) + SEQ)
    rows = P(("groups",) + SEQ, None)
    placed = (rows, rows, rows, P(SEQ, None), rows, P("groups"), rows)
    return jax.shard_map(
        local,
        mesh=split,
        in_specs=placed,
        out_specs=(rows, rows, rows, rows, rows),
        check_vma=False,
    )
```

```python
import math

import jax
import jax.numpy as jnp
from jax import lax
from jax.experimental import pallas as pl
from jax.sharding import Mesh
from jax.sharding import PartitionSpec as P

H = 8
BLK = 128
SEQ = ("chip", "core")


NEG_FILL = -1e30


def flat_index():
    return lax.axis_index("chip") * lax.axis_size("core") + lax.axis_index("core")


def xor_swap(x, level):
    if level == 0:
        n = lax.axis_size("core")
        return lax.ppermute(x, "core", [(i, i ^ 1) for i in range(n)])
    n = lax.axis_size("chip")
    m = 1 << (level - 1)
    return lax.ppermute(x, "chip", [(i, i ^ m) for i in range(n)])


def butterfly_halves(x, wire=None):
    count = lax.axis_size("chip") * lax.axis_size("core")
    levels = count.bit_length() - 1
    d = flat_index()
    parts = x.reshape(count, -1)
    for k in range(levels):
        half = parts.shape[0] // 2
        lo, hi = parts[:half], parts[half:]
        upper = ((d >> k) & 1) == 1
        send = jnp.where(upper, lo, hi)
        keep = jnp.where(upper, hi, lo)
        if wire is not None:
            send = send.astype(wire)
        parts = keep + xor_swap(send, k).astype(keep.dtype)
    if wire is not None:
        parts = parts.astype(wire)
    return parts


def butterfly_doubling(parts, shape):
    count = lax.axis_size("chip") * lax.axis_size("core")
    levels = count.bit_length() - 1
    d = flat_index()
    for k in reversed(range(levels)):
        upper = ((d >> k) & 1) == 1
        other = xor_swap(parts, k)
        parts = jnp.where(
            upper, jnp.concatenate([other, parts]), jnp.concatenate([parts, other])
        )
    return parts.reshape(shape)


def butterfly_sum(x, wire=None):
    return butterfly_doubling(butterfly_halves(x, wire), x.shape)


def halo(shard):
    count = lax.axis_size("chip") * lax.axis_size("core")
    up = [(i, i + 1) for i in range(count - 1)]
    down = [(j, i) for i, j in up]
    before = lax.ppermute(shard, SEQ, up)
    after = lax.ppermute(shard, SEQ, down)
    return before, after


def _attn_kernel(live_ref, q_ref, k_ref, v_ref, up_ref, attn_ref, dq_ref, dk_ref, dv_ref):
    scale = 1.0 / math.sqrt(q_ref.shape[-1])
    q = q_ref[...]
    k = k_ref[...]
    v = v_ref[...]
    up = up_ref[...]
    nt = (((1,), (1,)), ((), ()))
    tn = (((0,), (0,)), ((), ()))
    scores = lax.dot_general(q, k, nt, preferred_element_type=jnp.float32) * scale
    scores = jnp.where(live_ref[...] > 0, scores, NEG_FILL)
    top = jnp.max(scores, axis=-1, keepdims=True)
    raised = jnp.exp(scores - top)
    probs = raised / jnp.sum(raised, axis=-1, keepdims=True)
    probs_b = probs.astype(jnp.bfloat16)
    attn_ref[...] = jnp.dot(probs_b, v, preferred_element_type=jnp.float32).astype(attn_ref.dtype)
    dv_ref[...] = lax.dot_general(probs_b, up, tn, preferred_element_type=jnp.float32)
    dprobs = lax.dot_general(up, v, nt, preferred_element_type=jnp.float32)
    rowdot = jnp.sum(probs * dprobs, axis=-1, keepdims=True)
    dscores = (scale * probs * (dprobs - rowdot)).astype(jnp.bfloat16)
    dq_ref[...] = jnp.dot(dscores, k, preferred_element_type=jnp.float32).astype(dq_ref.dtype)
    dk_ref[...] = lax.dot_general(dscores, q, tn, preferred_element_type=jnp.float32)

def attention(live, q, k, v, up, heads):
    rows, features = q.shape
    keys_n = k.shape[0]
    hd = features // heads
    qspec = pl.BlockSpec((rows, hd), lambda h: (0, h))
    kspec = pl.BlockSpec((keys_n, hd), lambda h: (0, h))
    return pl.pallas_call(
        _attn_kernel,
        grid=(heads,),
        in_specs=[pl.BlockSpec((1, keys_n), lambda h: (0, 0)), qspec, kspec, kspec, qspec],
        out_specs=[qspec, qspec, kspec, kspec],
        out_shape=[
            jax.ShapeDtypeStruct((rows, features), jnp.bfloat16),
            jax.ShapeDtypeStruct((rows, features), jnp.bfloat16),
            jax.ShapeDtypeStruct((keys_n, features), jnp.float32),
            jax.ShapeDtypeStruct((keys_n, features), jnp.float32),
        ],
    )(live, q, k, v, up)


def local(query, keys, values, out_weight, grad_out, global_blocks, random_blocks):
    tok_rows, feature_count = query.shape
    hd = feature_count // H
    blocks_dev = tok_rows // BLK
    count = lax.axis_size("chip") * lax.axis_size("core")
    total_blocks = blocks_dev * count
    device = flat_index()

    grad_out_all = lax.all_gather(grad_out, SEQ, axis=0, tiled=True)
    weight_all = lax.all_gather(out_weight, SEQ, axis=0, tiled=True)

    paired = jnp.stack([keys, values])

    slots = global_blocks.shape[0]
    owners = global_blocks // blocks_dev
    masked = []
    for g in range(slots):
        start = (global_blocks[g] % blocks_dev) * BLK
        block = lax.dynamic_slice_in_dim(paired, start, BLK, axis=1)
        masked.append(jnp.where(owners[g] == device, block, jnp.zeros_like(block)))
    masked = jnp.stack(masked)
    halves = butterfly_halves(masked)
    halves, paired_late = lax.optimization_barrier((halves, paired))
    global_kv = butterfly_doubling(halves, masked.shape)
    before, after = halo(paired_late)
    extended = jnp.concatenate([before, paired, after], axis=1)

    local_ids = jnp.arange(blocks_dev, dtype=jnp.int32)
    global_ids = device * blocks_dev + local_ids
    offsets = jnp.array([-1, 0, 1], dtype=jnp.int32)
    neighbour_ids = global_ids[:, None] + offsets[None, :]
    window_index = local_ids[:, None] + blocks_dev + offsets[None, :]
    window_live = (neighbour_ids >= 0) & (neighbour_ids < total_blocks)
    random_index = random_blocks - (device - 1) * blocks_dev
    ext_index = jnp.concatenate([window_index, random_index], axis=1)
    n_local = ext_index.shape[1]
    live = jnp.concatenate(
        [window_live, jnp.ones(random_blocks.shape, jnp.bool_), jnp.ones((blocks_dev, slots), jnp.bool_)],
        axis=1,
    )

    w_rows = out_weight.shape[0]
    upstream_cols = lax.dot_general(
        grad_out_all, out_weight, (((1,), (1,)), ((), ())), preferred_element_type=jnp.float32
    ).astype(jnp.bfloat16)
    upstream = lax.all_to_all(
        upstream_cols.reshape(count, tok_rows, w_rows), SEQ, 0, 0, tiled=False
    )
    upstream = jnp.swapaxes(upstream, 0, 1).reshape(tok_rows, feature_count)

    attn_rows, dq_rows = [], []
    grad_ext = [jnp.zeros((3 * blocks_dev * BLK, feature_count), jnp.float32) for _ in range(2)]
    global_local = None
    for b in range(blocks_dev):
        chosen = []
        for side in range(2):
            parts = [
                lax.dynamic_slice_in_dim(extended[side], ext_index[b, j] * BLK, BLK, axis=0)
                for j in range(n_local)
            ]
            parts += [global_kv[g, side] for g in range(slots)]
            chosen.append(jnp.concatenate(parts, axis=0))
        live_rows = jnp.repeat(live[b], BLK).astype(jnp.float32)[None]
        q = query[b * BLK : (b + 1) * BLK]
        up = upstream[b * BLK : (b + 1) * BLK]
        attn, dq, dk, dv = attention(live_rows, q, chosen[0], chosen[1], up, H)
        attn_rows.append(attn)
        dq_rows.append(dq)
        for side, grad in enumerate((dk, dv)):
            for j in range(n_local):
                start = ext_index[b, j] * BLK
                cur = lax.dynamic_slice_in_dim(grad_ext[side], start, BLK, axis=0)
                term = grad[j * BLK : (j + 1) * BLK]
                grad_ext[side] = lax.dynamic_update_slice_in_dim(
                    grad_ext[side], cur + term, start, axis=0
                )
        terms = jnp.stack(
            [dk[n_local * BLK :].reshape(slots, BLK, feature_count),
             dv[n_local * BLK :].reshape(slots, BLK, feature_count)],
            axis=1,
        )
        global_local = terms if global_local is None else global_local + terms
    grad_ext = jnp.stack(grad_ext)
    global_total = butterfly_sum(global_local, jnp.bfloat16)

    attn_out = jnp.concatenate(attn_rows, axis=0)
    layer_out = jnp.dot(attn_out, weight_all, preferred_element_type=jnp.float32).astype(
        jnp.bfloat16
    )
    attn_cols = lax.all_to_all(
        attn_out.reshape(tok_rows, count, w_rows), SEQ, 1, 0, tiled=False
    ).reshape(count * tok_rows, w_rows)
    grad_weight = lax.dot_general(
        attn_cols, grad_out_all, (((0,), (0,)), ((), ())), preferred_element_type=jnp.float32
    )

    rims = jnp.concatenate(
        [grad_ext[:, : blocks_dev * BLK], grad_ext[:, 2 * blocks_dev * BLK :]], axis=1
    ).astype(jnp.bfloat16)
    from_prev, from_next = halo(rims)
    finished = []
    for side in range(2):
        own = grad_ext[side, blocks_dev * BLK : 2 * blocks_dev * BLK]
        own = own + from_prev[side, blocks_dev * BLK :].astype(jnp.float32)
        own = own + from_next[side, : blocks_dev * BLK].astype(jnp.float32)
        for g in range(slots):
            start = (global_blocks[g] % blocks_dev) * BLK
            total = global_total[g, side]
            add = jnp.where(owners[g] == device, total, jnp.zeros_like(total))
            cur = lax.dynamic_slice_in_dim(own, start, BLK, axis=0)
            own = lax.dynamic_update_slice_in_dim(own, cur + add, start, axis=0)
        finished.append(own.astype(jnp.bfloat16))
    grad_query = jnp.concatenate(dq_rows, axis=0)
    return (layer_out, grad_query, finished[0], finished[1], grad_weight)


def solution(mesh):
    groups, seq = mesh.devices.shape
    split = Mesh(mesh.devices.reshape(groups, seq // 2, 2), ("groups",) + SEQ)
    rows = P(("groups",) + SEQ, None)
    placed = (rows, rows, rows, P(SEQ, None), rows, P("groups"), rows)
    return jax.shard_map(
        local,
        mesh=split,
        in_specs=placed,
        out_specs=(rows, rows, rows, rows, rows),
        check_vma=False,
    )
```

```python
import math

import jax
import jax.numpy as jnp
from jax import lax
from jax.experimental import pallas as pl
from jax.sharding import Mesh
from jax.sharding import PartitionSpec as P

H = 8
BLK = 128
SEQ = ("chip", "core")


NEG_FILL = -1e30


def flat_index():
    return lax.axis_index("chip") * lax.axis_size("core") + lax.axis_index("core")


def xor_swap(x, level):
    if level == 0:
        n = lax.axis_size("core")
        return lax.ppermute(x, "core", [(i, i ^ 1) for i in range(n)])
    n = lax.axis_size("chip")
    m = 1 << (level - 1)
    return lax.ppermute(x, "chip", [(i, i ^ m) for i in range(n)])


def butterfly_sum(x, wire=None):
    count = lax.axis_size("chip") * lax.axis_size("core")
    levels = count.bit_length() - 1
    shape = x.shape
    flat = x.reshape(count, -1)
    d = flat_index()
    parts = flat
    for k in range(levels):
        half = parts.shape[0] // 2
        lo, hi = parts[:half], parts[half:]
        upper = ((d >> k) & 1) == 1
        send = jnp.where(upper, lo, hi)
        keep = jnp.where(upper, hi, lo)
        if wire is not None:
            send = send.astype(wire)
        parts = keep + xor_swap(send, k).astype(keep.dtype)
    for k in reversed(range(levels)):
        upper = ((d >> k) & 1) == 1
        if wire is not None and k == levels - 1:
            parts = parts.astype(wire)
        other = xor_swap(parts, k)
        parts = jnp.where(
            upper, jnp.concatenate([other, parts]), jnp.concatenate([parts, other])
        )
    return parts.reshape(shape)


def halo(shard):
    count = lax.axis_size("chip") * lax.axis_size("core")
    up = [(i, i + 1) for i in range(count - 1)]
    down = [(j, i) for i, j in up]
    before = lax.ppermute(shard, SEQ, up)
    after = lax.ppermute(shard, SEQ, down)
    return before, after


def _attn_kernel(live_ref, q_ref, k_ref, v_ref, up_ref, attn_ref, dq_ref, dk_ref, dv_ref, dg_ref):
    scale = 1.0 / math.sqrt(q_ref.shape[-1])
    q = q_ref[...]
    k = k_ref[...]
    v = v_ref[...]
    up = up_ref[...]
    nt = (((1,), (1,)), ((), ()))
    tn = (((0,), (0,)), ((), ()))
    scores = lax.dot_general(q, k, nt, preferred_element_type=jnp.float32) * scale
    scores = jnp.where(live_ref[...] > 0, scores, NEG_FILL)
    top = jnp.max(scores, axis=-1, keepdims=True)
    raised = jnp.exp(scores - top)
    probs = raised / jnp.sum(raised, axis=-1, keepdims=True)
    probs_b = probs.astype(jnp.bfloat16)
    attn_ref[...] = jnp.dot(probs_b, v, preferred_element_type=jnp.float32).astype(attn_ref.dtype)
    n_local = dk_ref.shape[0]
    dv = lax.dot_general(probs_b, up, tn, preferred_element_type=jnp.float32)
    dv_ref[...] = dv[:n_local]
    dg_ref[1] = dv[n_local:]
    dprobs = lax.dot_general(up, v, nt, preferred_element_type=jnp.float32)
    rowdot = jnp.sum(probs * dprobs, axis=-1, keepdims=True)
    dscores = (scale * probs * (dprobs - rowdot)).astype(jnp.bfloat16)
    dq_ref[...] = jnp.dot(dscores, k, preferred_element_type=jnp.float32).astype(dq_ref.dtype)
    dk = lax.dot_general(dscores, q, tn, preferred_element_type=jnp.float32)
    dk_ref[...] = dk[:n_local]
    dg_ref[0] = dk[n_local:]

def attention(live, q, k, v, up, heads, local_n):
    rows, features = q.shape
    keys_n = k.shape[0]
    hd = features // heads
    qspec = pl.BlockSpec((rows, hd), lambda h: (0, h))
    kspec = pl.BlockSpec((keys_n, hd), lambda h: (0, h))
    lspec = pl.BlockSpec((local_n, hd), lambda h: (0, h))
    gspec = pl.BlockSpec((2, keys_n - local_n, hd), lambda h: (0, 0, h))
    return pl.pallas_call(
        _attn_kernel,
        grid=(heads,),
        in_specs=[pl.BlockSpec((1, keys_n), lambda h: (0, 0)), qspec, kspec, kspec, qspec],
        out_specs=[qspec, qspec, lspec, lspec, gspec],
        out_shape=[
            jax.ShapeDtypeStruct((rows, features), jnp.bfloat16),
            jax.ShapeDtypeStruct((rows, features), jnp.bfloat16),
            jax.ShapeDtypeStruct((local_n, features), jnp.float32),
            jax.ShapeDtypeStruct((local_n, features), jnp.float32),
            jax.ShapeDtypeStruct((2, keys_n - local_n, features), jnp.float32),
        ],
    )(live, q, k, v, up)


def local(query, keys, values, out_weight, grad_out, global_blocks, random_blocks):
    tok_rows, feature_count = query.shape
    hd = feature_count // H
    blocks_dev = tok_rows // BLK
    count = lax.axis_size("chip") * lax.axis_size("core")
    total_blocks = blocks_dev * count
    device = flat_index()

    grad_out_all = lax.all_gather(grad_out, SEQ, axis=0, tiled=True)
    weight_all = lax.all_gather(out_weight, SEQ, axis=0, tiled=True)

    paired = jnp.stack([keys, values])
    before, after = halo(paired)
    extended = jnp.concatenate([before, paired, after], axis=1)

    slots = global_blocks.shape[0]
    owners = global_blocks // blocks_dev
    masked = []
    for g in range(slots):
        start = (global_blocks[g] % blocks_dev) * BLK
        block = lax.dynamic_slice_in_dim(paired, start, BLK, axis=1)
        masked.append(jnp.where(owners[g] == device, block, jnp.zeros_like(block)))
    global_kv = butterfly_sum(jnp.stack(masked))

    local_ids = jnp.arange(blocks_dev, dtype=jnp.int32)
    global_ids = device * blocks_dev + local_ids
    offsets = jnp.array([-1, 0, 1], dtype=jnp.int32)
    neighbour_ids = global_ids[:, None] + offsets[None, :]
    window_index = local_ids[:, None] + blocks_dev + offsets[None, :]
    window_live = (neighbour_ids >= 0) & (neighbour_ids < total_blocks)
    random_index = random_blocks - (device - 1) * blocks_dev
    ext_index = jnp.concatenate([window_index, random_index], axis=1)
    n_local = ext_index.shape[1]
    live = jnp.concatenate(
        [window_live, jnp.ones(random_blocks.shape, jnp.bool_), jnp.ones((blocks_dev, slots), jnp.bool_)],
        axis=1,
    )

    w_rows = out_weight.shape[0]
    upstream_cols = lax.dot_general(
        grad_out_all, out_weight, (((1,), (1,)), ((), ())), preferred_element_type=jnp.float32
    ).astype(jnp.bfloat16)
    upstream = lax.all_to_all(
        upstream_cols.reshape(count, tok_rows, w_rows), SEQ, 0, 0, tiled=False
    )
    upstream = jnp.swapaxes(upstream, 0, 1).reshape(tok_rows, feature_count)

    attn_rows, dq_rows = [], []
    grad_ext = [jnp.zeros((3 * blocks_dev * BLK, feature_count), jnp.float32) for _ in range(2)]
    global_local = None
    for b in range(blocks_dev):
        chosen = []
        for side in range(2):
            parts = [
                lax.dynamic_slice_in_dim(extended[side], ext_index[b, j] * BLK, BLK, axis=0)
                for j in range(n_local)
            ]
            parts += [global_kv[g, side] for g in range(slots)]
            chosen.append(jnp.concatenate(parts, axis=0))
        live_rows = jnp.repeat(live[b], BLK).astype(jnp.float32)[None]
        q = query[b * BLK : (b + 1) * BLK]
        up = upstream[b * BLK : (b + 1) * BLK]
        attn, dq, dk, dv, dg = attention(live_rows, q, chosen[0], chosen[1], up, H, n_local * BLK)
        attn_rows.append(attn)
        dq_rows.append(dq)
        for side, grad in enumerate((dk, dv)):
            for j in range(n_local):
                start = ext_index[b, j] * BLK
                cur = lax.dynamic_slice_in_dim(grad_ext[side], start, BLK, axis=0)
                term = grad[j * BLK : (j + 1) * BLK]
                grad_ext[side] = lax.dynamic_update_slice_in_dim(
                    grad_ext[side], cur + term, start, axis=0
                )
        terms = dg
        global_local = terms if global_local is None else global_local + terms
    grad_ext = jnp.stack(grad_ext)
    global_total = butterfly_sum(global_local, jnp.bfloat16)

    attn_out = jnp.concatenate(attn_rows, axis=0)
    layer_out = jnp.dot(attn_out, weight_all, preferred_element_type=jnp.float32).astype(
        jnp.bfloat16
    )
    attn_cols = lax.all_to_all(
        attn_out.reshape(tok_rows, count, w_rows), SEQ, 1, 0, tiled=False
    ).reshape(count * tok_rows, w_rows)
    grad_weight = lax.dot_general(
        attn_cols, grad_out_all, (((0,), (0,)), ((), ())), preferred_element_type=jnp.float32
    )

    rims = jnp.concatenate(
        [grad_ext[:, : blocks_dev * BLK], grad_ext[:, 2 * blocks_dev * BLK :]], axis=1
    ).astype(jnp.bfloat16)
    from_prev, from_next = halo(rims)
    finished = []
    for side in range(2):
        own = grad_ext[side, blocks_dev * BLK : 2 * blocks_dev * BLK]
        own = own + from_prev[side, blocks_dev * BLK :].astype(jnp.float32)
        own = own + from_next[side, : blocks_dev * BLK].astype(jnp.float32)
        for g in range(slots):
            start = (global_blocks[g] % blocks_dev) * BLK
            total = global_total[side, g * BLK : (g + 1) * BLK]
            add = jnp.where(owners[g] == device, total, jnp.zeros_like(total))
            cur = lax.dynamic_slice_in_dim(own, start, BLK, axis=0)
            own = lax.dynamic_update_slice_in_dim(own, cur + add, start, axis=0)
        finished.append(own.astype(jnp.bfloat16))
    grad_query = jnp.concatenate(dq_rows, axis=0)
    return (layer_out, grad_query, finished[0], finished[1], grad_weight)


def solution(mesh):
    groups, seq = mesh.devices.shape
    split = Mesh(mesh.devices.reshape(groups, seq // 2, 2), ("groups",) + SEQ)
    rows = P(("groups",) + SEQ, None)
    placed = (rows, rows, rows, P(SEQ, None), rows, P("groups"), rows)
    return jax.shard_map(
        local,
        mesh=split,
        in_specs=placed,
        out_specs=(rows, rows, rows, rows, rows),
        check_vma=False,
    )
```

```python
import math

import jax
import jax.numpy as jnp
from jax import lax
from jax.experimental import pallas as pl
from jax.sharding import Mesh
from jax.sharding import PartitionSpec as P

H = 8
BLK = 128
SEQ = ("chip", "core")


NEG_FILL = -1e30


def flat_index():
    return lax.axis_index("chip") * lax.axis_size("core") + lax.axis_index("core")


def xor_swap(x, level):
    if level == 0:
        n = lax.axis_size("core")
        return lax.ppermute(x, "core", [(i, i ^ 1) for i in range(n)])
    n = lax.axis_size("chip")
    m = 1 << (level - 1)
    return lax.ppermute(x, "chip", [(i, i ^ m) for i in range(n)])


def butterfly_sum(x, wire=None):
    count = lax.axis_size("chip") * lax.axis_size("core")
    levels = count.bit_length() - 1
    shape = x.shape
    flat = x.reshape(count, -1)
    d = flat_index()
    parts = flat
    for k in range(levels):
        half = parts.shape[0] // 2
        bit = (d >> k) & 1
        send = lax.dynamic_slice_in_dim(parts, (1 - bit) * half, half, axis=0)
        keep = lax.dynamic_slice_in_dim(parts, bit * half, half, axis=0)
        if wire is not None:
            send = send.astype(wire)
        parts = keep + xor_swap(send, k).astype(keep.dtype)
    for k in reversed(range(levels)):
        upper = ((d >> k) & 1) == 1
        if wire is not None and k == levels - 1:
            parts = parts.astype(wire)
        other = xor_swap(parts, k)
        parts = jnp.where(
            upper, jnp.concatenate([other, parts]), jnp.concatenate([parts, other])
        )
    return parts.reshape(shape)


def halo(shard):
    count = lax.axis_size("chip") * lax.axis_size("core")
    up = [(i, i + 1) for i in range(count - 1)]
    down = [(j, i) for i, j in up]
    before = lax.ppermute(shard, SEQ, up)
    after = lax.ppermute(shard, SEQ, down)
    return before, after


def _attn_kernel(live_ref, q_ref, k_ref, v_ref, up_ref, attn_ref, dq_ref, dk_ref, dv_ref, dg_ref):
    scale = 1.0 / math.sqrt(q_ref.shape[-1])
    q = q_ref[...]
    k = k_ref[...]
    v = v_ref[...]
    up = up_ref[...]
    nt = (((1,), (1,)), ((), ()))
    tn = (((0,), (0,)), ((), ()))
    scores = lax.dot_general(q, k, nt, preferred_element_type=jnp.float32) * scale
    scores = jnp.where(live_ref[...] > 0, scores, NEG_FILL)
    top = jnp.max(scores, axis=-1, keepdims=True)
    raised = jnp.exp(scores - top)
    probs = raised / jnp.sum(raised, axis=-1, keepdims=True)
    probs_b = probs.astype(jnp.bfloat16)
    attn_ref[...] = jnp.dot(probs_b, v, preferred_element_type=jnp.float32).astype(attn_ref.dtype)
    n_local = dk_ref.shape[0]
    dv = lax.dot_general(probs_b, up, tn, preferred_element_type=jnp.float32)
    dv_ref[...] = dv[:n_local]
    dg_ref[1] = dv[n_local:]
    dprobs = lax.dot_general(up, v, nt, preferred_element_type=jnp.float32)
    rowdot = jnp.sum(probs * dprobs, axis=-1, keepdims=True)
    dscores = (scale * probs * (dprobs - rowdot)).astype(jnp.bfloat16)
    dq_ref[...] = jnp.dot(dscores, k, preferred_element_type=jnp.float32).astype(dq_ref.dtype)
    dk = lax.dot_general(dscores, q, tn, preferred_element_type=jnp.float32)
    dk_ref[...] = dk[:n_local]
    dg_ref[0] = dk[n_local:]

def attention(live, q, k, v, up, heads, local_n):
    rows, features = q.shape
    keys_n = k.shape[0]
    hd = features // heads
    qspec = pl.BlockSpec((rows, hd), lambda h: (0, h))
    kspec = pl.BlockSpec((keys_n, hd), lambda h: (0, h))
    lspec = pl.BlockSpec((local_n, hd), lambda h: (0, h))
    gspec = pl.BlockSpec((2, keys_n - local_n, hd), lambda h: (0, 0, h))
    return pl.pallas_call(
        _attn_kernel,
        grid=(heads,),
        in_specs=[pl.BlockSpec((1, keys_n), lambda h: (0, 0)), qspec, kspec, kspec, qspec],
        out_specs=[qspec, qspec, lspec, lspec, gspec],
        out_shape=[
            jax.ShapeDtypeStruct((rows, features), jnp.bfloat16),
            jax.ShapeDtypeStruct((rows, features), jnp.bfloat16),
            jax.ShapeDtypeStruct((local_n, features), jnp.float32),
            jax.ShapeDtypeStruct((local_n, features), jnp.float32),
            jax.ShapeDtypeStruct((2, keys_n - local_n, features), jnp.float32),
        ],
    )(live, q, k, v, up)


def local(query, keys, values, out_weight, grad_out, global_blocks, random_blocks):
    tok_rows, feature_count = query.shape
    hd = feature_count // H
    blocks_dev = tok_rows // BLK
    count = lax.axis_size("chip") * lax.axis_size("core")
    total_blocks = blocks_dev * count
    device = flat_index()

    grad_out_all = lax.all_gather(grad_out, SEQ, axis=0, tiled=True)
    weight_all = lax.all_gather(out_weight, SEQ, axis=0, tiled=True)

    paired = jnp.stack([keys, values])
    before, after = halo(paired)
    extended = jnp.concatenate([before, paired, after], axis=1)

    slots = global_blocks.shape[0]
    owners = global_blocks // blocks_dev
    masked = []
    for g in range(slots):
        start = (global_blocks[g] % blocks_dev) * BLK
        block = lax.dynamic_slice_in_dim(paired, start, BLK, axis=1)
        masked.append(jnp.where(owners[g] == device, block, jnp.zeros_like(block)))
    global_kv = butterfly_sum(jnp.stack(masked))

    local_ids = jnp.arange(blocks_dev, dtype=jnp.int32)
    global_ids = device * blocks_dev + local_ids
    offsets = jnp.array([-1, 0, 1], dtype=jnp.int32)
    neighbour_ids = global_ids[:, None] + offsets[None, :]
    window_index = local_ids[:, None] + blocks_dev + offsets[None, :]
    window_live = (neighbour_ids >= 0) & (neighbour_ids < total_blocks)
    random_index = random_blocks - (device - 1) * blocks_dev
    ext_index = jnp.concatenate([window_index, random_index], axis=1)
    n_local = ext_index.shape[1]
    live = jnp.concatenate(
        [window_live, jnp.ones(random_blocks.shape, jnp.bool_), jnp.ones((blocks_dev, slots), jnp.bool_)],
        axis=1,
    )

    w_rows = out_weight.shape[0]
    upstream_cols = lax.dot_general(
        grad_out_all, out_weight, (((1,), (1,)), ((), ())), preferred_element_type=jnp.float32
    ).astype(jnp.bfloat16)
    upstream = lax.all_to_all(
        upstream_cols.reshape(count, tok_rows, w_rows), SEQ, 0, 0, tiled=False
    )
    upstream = jnp.swapaxes(upstream, 0, 1).reshape(tok_rows, feature_count)

    attn_rows, dq_rows = [], []
    grad_ext = [jnp.zeros((3 * blocks_dev * BLK, feature_count), jnp.float32) for _ in range(2)]
    global_local = None
    for b in range(blocks_dev):
        chosen = []
        for side in range(2):
            parts = [
                lax.dynamic_slice_in_dim(extended[side], ext_index[b, j] * BLK, BLK, axis=0)
                for j in range(n_local)
            ]
            parts += [global_kv[g, side] for g in range(slots)]
            chosen.append(jnp.concatenate(parts, axis=0))
        live_rows = jnp.repeat(live[b], BLK).astype(jnp.float32)[None]
        q = query[b * BLK : (b + 1) * BLK]
        up = upstream[b * BLK : (b + 1) * BLK]
        attn, dq, dk, dv, dg = attention(live_rows, q, chosen[0], chosen[1], up, H, n_local * BLK)
        attn_rows.append(attn)
        dq_rows.append(dq)
        for side, grad in enumerate((dk, dv)):
            for j in range(n_local):
                start = ext_index[b, j] * BLK
                cur = lax.dynamic_slice_in_dim(grad_ext[side], start, BLK, axis=0)
                term = grad[j * BLK : (j + 1) * BLK]
                grad_ext[side] = lax.dynamic_update_slice_in_dim(
                    grad_ext[side], cur + term, start, axis=0
                )
        terms = dg
        global_local = terms if global_local is None else global_local + terms
    grad_ext = jnp.stack(grad_ext)
    global_total = butterfly_sum(global_local, jnp.bfloat16)

    attn_out = jnp.concatenate(attn_rows, axis=0)
    layer_out = jnp.dot(attn_out, weight_all, preferred_element_type=jnp.float32).astype(
        jnp.bfloat16
    )
    attn_cols = lax.all_to_all(
        attn_out.reshape(tok_rows, count, w_rows), SEQ, 1, 0, tiled=False
    ).reshape(count * tok_rows, w_rows)
    grad_weight = lax.dot_general(
        attn_cols, grad_out_all, (((0,), (0,)), ((), ())), preferred_element_type=jnp.float32
    )

    rims = jnp.concatenate(
        [grad_ext[:, : blocks_dev * BLK], grad_ext[:, 2 * blocks_dev * BLK :]], axis=1
    ).astype(jnp.bfloat16)
    from_prev, from_next = halo(rims)
    finished = []
    for side in range(2):
        own = grad_ext[side, blocks_dev * BLK : 2 * blocks_dev * BLK]
        own = own + from_prev[side, blocks_dev * BLK :].astype(jnp.float32)
        own = own + from_next[side, : blocks_dev * BLK].astype(jnp.float32)
        for g in range(slots):
            start = (global_blocks[g] % blocks_dev) * BLK
            total = global_total[side, g * BLK : (g + 1) * BLK]
            add = jnp.where(owners[g] == device, total, jnp.zeros_like(total))
            cur = lax.dynamic_slice_in_dim(own, start, BLK, axis=0)
            own = lax.dynamic_update_slice_in_dim(own, cur + add, start, axis=0)
        finished.append(own.astype(jnp.bfloat16))
    grad_query = jnp.concatenate(dq_rows, axis=0)
    return (layer_out, grad_query, finished[0], finished[1], grad_weight)


def solution(mesh):
    groups, seq = mesh.devices.shape
    split = Mesh(mesh.devices.reshape(groups, seq // 2, 2), ("groups",) + SEQ)
    rows = P(("groups",) + SEQ, None)
    placed = (rows, rows, rows, P(SEQ, None), rows, P("groups"), rows)
    return jax.shard_map(
        local,
        mesh=split,
        in_specs=placed,
        out_specs=(rows, rows, rows, rows, rows),
        check_vma=False,
    )
```

```python
import math

import jax
import jax.numpy as jnp
from jax import lax
from jax.experimental import pallas as pl
from jax.experimental.pallas import tpu as pltpu
from jax.sharding import Mesh
from jax.sharding import PartitionSpec as P

H = 8
BLK = 128
SEQ = ("chip", "core")


NEG_FILL = -1e30


def flat_index():
    return lax.axis_index("chip") * lax.axis_size("core") + lax.axis_index("core")


def xor_swap(x, level):
    if level == 0:
        n = lax.axis_size("core")
        return lax.ppermute(x, "core", [(i, i ^ 1) for i in range(n)])
    n = lax.axis_size("chip")
    m = 1 << (level - 1)
    return lax.ppermute(x, "chip", [(i, i ^ m) for i in range(n)])


def butterfly_sum(x, wire=None):
    count = lax.axis_size("chip") * lax.axis_size("core")
    levels = count.bit_length() - 1
    shape = x.shape
    flat = x.reshape(count, -1)
    d = flat_index()
    parts = flat
    for k in range(levels):
        half = parts.shape[0] // 2
        bit = (d >> k) & 1
        send = lax.dynamic_slice_in_dim(parts, (1 - bit) * half, half, axis=0)
        keep = lax.dynamic_slice_in_dim(parts, bit * half, half, axis=0)
        if wire is not None:
            send = send.astype(wire)
        parts = keep + xor_swap(send, k).astype(keep.dtype)
    for k in reversed(range(levels)):
        upper = ((d >> k) & 1) == 1
        if wire is not None and k == levels - 1:
            parts = parts.astype(wire)
        other = xor_swap(parts, k)
        parts = jnp.where(
            upper, jnp.concatenate([other, parts]), jnp.concatenate([parts, other])
        )
    return parts.reshape(shape)


def halo(shard):
    count = lax.axis_size("chip") * lax.axis_size("core")
    up = [(i, i + 1) for i in range(count - 1)]
    down = [(j, i) for i, j in up]
    before = lax.ppermute(shard, SEQ, up)
    after = lax.ppermute(shard, SEQ, down)
    return before, after


def _attn_kernel(ext_ref, live_ref, q_ref, k_ref, v_ref, up_ref, attn_ref, dq_ref, gk_ref, gv_ref, dg_ref):
    scale = 1.0 / math.sqrt(q_ref.shape[-1])
    q = q_ref[...]
    k = k_ref[...]
    v = v_ref[...]
    up = up_ref[...]
    nt = (((1,), (1,)), ((), ()))
    tn = (((0,), (0,)), ((), ()))
    scores = lax.dot_general(q, k, nt, preferred_element_type=jnp.float32) * scale
    scores = jnp.where(live_ref[...] > 0, scores, NEG_FILL)
    top = jnp.max(scores, axis=-1, keepdims=True)
    raised = jnp.exp(scores - top)
    probs = raised / jnp.sum(raised, axis=-1, keepdims=True)
    probs_b = probs.astype(jnp.bfloat16)
    attn_ref[...] = jnp.dot(probs_b, v, preferred_element_type=jnp.float32).astype(attn_ref.dtype)
    n_local = k.shape[0] - dg_ref.shape[1]
    blk = dg_ref.shape[1] // 2
    dv = lax.dot_general(probs_b, up, tn, preferred_element_type=jnp.float32)
    dg_ref[1] = dv[n_local:]
    dprobs = lax.dot_general(up, v, nt, preferred_element_type=jnp.float32)
    rowdot = jnp.sum(probs * dprobs, axis=-1, keepdims=True)
    dscores = (scale * probs * (dprobs - rowdot)).astype(jnp.bfloat16)
    dq_ref[...] = jnp.dot(dscores, k, preferred_element_type=jnp.float32).astype(dq_ref.dtype)
    dk = lax.dot_general(dscores, q, tn, preferred_element_type=jnp.float32)
    dg_ref[0] = dk[n_local:]
    gk_ref[...] = jnp.zeros_like(gk_ref)
    gv_ref[...] = jnp.zeros_like(gv_ref)
    for j in range(n_local // blk):
        at = pl.ds(pl.multiple_of(ext_ref[j] * blk, blk), blk)
        gk_ref[at, :] += dk[j * blk : (j + 1) * blk]
        gv_ref[at, :] += dv[j * blk : (j + 1) * blk]

def attention(ext, live, q, k, v, up, heads, local_n, ext_n):
    rows, features = q.shape
    keys_n = k.shape[0]
    hd = features // heads
    qspec = pl.BlockSpec((rows, hd), lambda h, e: (0, h))
    kspec = pl.BlockSpec((keys_n, hd), lambda h, e: (0, h))
    espec = pl.BlockSpec((ext_n, hd), lambda h, e: (0, h))
    gspec = pl.BlockSpec((2, keys_n - local_n, hd), lambda h, e: (0, 0, h))
    grid_spec = pltpu.PrefetchScalarGridSpec(
        num_scalar_prefetch=1,
        grid=(heads,),
        in_specs=[pl.BlockSpec((1, keys_n), lambda h, e: (0, 0)), qspec, kspec, kspec, qspec],
        out_specs=[qspec, qspec, espec, espec, gspec],
    )
    return pl.pallas_call(
        _attn_kernel,
        grid_spec=grid_spec,
        out_shape=[
            jax.ShapeDtypeStruct((rows, features), jnp.bfloat16),
            jax.ShapeDtypeStruct((rows, features), jnp.bfloat16),
            jax.ShapeDtypeStruct((ext_n, features), jnp.float32),
            jax.ShapeDtypeStruct((ext_n, features), jnp.float32),
            jax.ShapeDtypeStruct((2, keys_n - local_n, features), jnp.float32),
        ],
    )(ext, live, q, k, v, up)


def local(query, keys, values, out_weight, grad_out, global_blocks, random_blocks):
    tok_rows, feature_count = query.shape
    hd = feature_count // H
    blocks_dev = tok_rows // BLK
    count = lax.axis_size("chip") * lax.axis_size("core")
    total_blocks = blocks_dev * count
    device = flat_index()

    grad_out_all = lax.all_gather(grad_out, SEQ, axis=0, tiled=True)
    weight_all = lax.all_gather(out_weight, SEQ, axis=0, tiled=True)

    paired = jnp.stack([keys, values])
    before, after = halo(paired)
    extended = jnp.concatenate([before, paired, after], axis=1)

    slots = global_blocks.shape[0]
    owners = global_blocks // blocks_dev
    masked = []
    for g in range(slots):
        start = (global_blocks[g] % blocks_dev) * BLK
        block = lax.dynamic_slice_in_dim(paired, start, BLK, axis=1)
        masked.append(jnp.where(owners[g] == device, block, jnp.zeros_like(block)))
    global_kv = butterfly_sum(jnp.stack(masked))

    local_ids = jnp.arange(blocks_dev, dtype=jnp.int32)
    global_ids = device * blocks_dev + local_ids
    offsets = jnp.array([-1, 0, 1], dtype=jnp.int32)
    neighbour_ids = global_ids[:, None] + offsets[None, :]
    window_index = local_ids[:, None] + blocks_dev + offsets[None, :]
    window_live = (neighbour_ids >= 0) & (neighbour_ids < total_blocks)
    random_index = random_blocks - (device - 1) * blocks_dev
    ext_index = jnp.concatenate([window_index, random_index], axis=1)
    n_local = ext_index.shape[1]
    live = jnp.concatenate(
        [window_live, jnp.ones(random_blocks.shape, jnp.bool_), jnp.ones((blocks_dev, slots), jnp.bool_)],
        axis=1,
    )

    w_rows = out_weight.shape[0]
    upstream_cols = lax.dot_general(
        grad_out_all, out_weight, (((1,), (1,)), ((), ())), preferred_element_type=jnp.float32
    ).astype(jnp.bfloat16)
    upstream = lax.all_to_all(
        upstream_cols.reshape(count, tok_rows, w_rows), SEQ, 0, 0, tiled=False
    )
    upstream = jnp.swapaxes(upstream, 0, 1).reshape(tok_rows, feature_count)

    attn_rows, dq_rows = [], []
    grad_ext = [jnp.zeros((3 * blocks_dev * BLK, feature_count), jnp.float32) for _ in range(2)]
    global_local = None
    for b in range(blocks_dev):
        chosen = []
        for side in range(2):
            parts = [
                lax.dynamic_slice_in_dim(extended[side], ext_index[b, j] * BLK, BLK, axis=0)
                for j in range(n_local)
            ]
            parts += [global_kv[g, side] for g in range(slots)]
            chosen.append(jnp.concatenate(parts, axis=0))
        live_rows = jnp.repeat(live[b], BLK).astype(jnp.float32)[None]
        q = query[b * BLK : (b + 1) * BLK]
        up = upstream[b * BLK : (b + 1) * BLK]
        attn, dq, gk, gv, dg = attention(
            ext_index[b], live_rows, q, chosen[0], chosen[1], up, H, n_local * BLK, 3 * blocks_dev * BLK
        )
        attn_rows.append(attn)
        dq_rows.append(dq)
        grad_ext = [grad_ext[0] + gk, grad_ext[1] + gv]
        terms = dg
        global_local = terms if global_local is None else global_local + terms
    grad_ext = jnp.stack(grad_ext)
    global_total = butterfly_sum(global_local, jnp.bfloat16)

    attn_out = jnp.concatenate(attn_rows, axis=0)
    layer_out = jnp.dot(attn_out, weight_all, preferred_element_type=jnp.float32).astype(
        jnp.bfloat16
    )
    attn_cols = lax.all_to_all(
        attn_out.reshape(tok_rows, count, w_rows), SEQ, 1, 0, tiled=False
    ).reshape(count * tok_rows, w_rows)
    grad_weight = lax.dot_general(
        attn_cols, grad_out_all, (((0,), (0,)), ((), ())), preferred_element_type=jnp.float32
    )

    rims = jnp.concatenate(
        [grad_ext[:, : blocks_dev * BLK], grad_ext[:, 2 * blocks_dev * BLK :]], axis=1
    ).astype(jnp.bfloat16)
    from_prev, from_next = halo(rims)
    finished = []
    for side in range(2):
        own = grad_ext[side, blocks_dev * BLK : 2 * blocks_dev * BLK]
        own = own + from_prev[side, blocks_dev * BLK :].astype(jnp.float32)
        own = own + from_next[side, : blocks_dev * BLK].astype(jnp.float32)
        for g in range(slots):
            start = (global_blocks[g] % blocks_dev) * BLK
            total = global_total[side, g * BLK : (g + 1) * BLK]
            add = jnp.where(owners[g] == device, total, jnp.zeros_like(total))
            cur = lax.dynamic_slice_in_dim(own, start, BLK, axis=0)
            own = lax.dynamic_update_slice_in_dim(own, cur + add, start, axis=0)
        finished.append(own.astype(jnp.bfloat16))
    grad_query = jnp.concatenate(dq_rows, axis=0)
    return (layer_out, grad_query, finished[0], finished[1], grad_weight)


def solution(mesh):
    groups, seq = mesh.devices.shape
    split = Mesh(mesh.devices.reshape(groups, seq // 2, 2), ("groups",) + SEQ)
    rows = P(("groups",) + SEQ, None)
    placed = (rows, rows, rows, P(SEQ, None), rows, P("groups"), rows)
    return jax.shard_map(
        local,
        mesh=split,
        in_specs=placed,
        out_specs=(rows, rows, rows, rows, rows),
        check_vma=False,
    )
```

```python
import math

import jax
import jax.numpy as jnp
from jax import lax
from jax.experimental import pallas as pl
from jax.experimental.pallas import tpu as pltpu
from jax.sharding import Mesh
from jax.sharding import PartitionSpec as P

H = 8
BLK = 128
SEQ = ("chip", "core")


NEG_FILL = -1e30


def flat_index():
    return lax.axis_index("chip") * lax.axis_size("core") + lax.axis_index("core")


def xor_swap(x, level):
    if level == 0:
        n = lax.axis_size("core")
        return lax.ppermute(x, "core", [(i, i ^ 1) for i in range(n)])
    n = lax.axis_size("chip")
    m = 1 << (level - 1)
    return lax.ppermute(x, "chip", [(i, i ^ m) for i in range(n)])


def butterfly_sum(x, wire=None):
    count = lax.axis_size("chip") * lax.axis_size("core")
    levels = count.bit_length() - 1
    shape = x.shape
    flat = x.reshape(count, -1)
    d = flat_index()
    parts = flat
    for k in range(levels):
        half = parts.shape[0] // 2
        bit = (d >> k) & 1
        send = lax.dynamic_slice_in_dim(parts, (1 - bit) * half, half, axis=0)
        keep = lax.dynamic_slice_in_dim(parts, bit * half, half, axis=0)
        if wire is not None:
            send = send.astype(wire)
        parts = keep + xor_swap(send, k).astype(keep.dtype)
    for k in reversed(range(levels)):
        upper = ((d >> k) & 1) == 1
        if wire is not None and k == levels - 1:
            parts = parts.astype(wire)
        other = xor_swap(parts, k)
        parts = jnp.where(
            upper, jnp.concatenate([other, parts]), jnp.concatenate([parts, other])
        )
    return parts.reshape(shape)


def halo(shard):
    count = lax.axis_size("chip") * lax.axis_size("core")
    up = [(i, i + 1) for i in range(count - 1)]
    down = [(j, i) for i, j in up]
    before = lax.ppermute(shard, SEQ, up)
    after = lax.ppermute(shard, SEQ, down)
    return before, after


def _attn_kernel(ext_ref, live_ref, q_ref, k_ref, v_ref, up_ref, attn_ref, dq_ref, gk_ref, gv_ref, dg_ref):
    scale = 1.0 / math.sqrt(q_ref.shape[-1])
    q = q_ref[...]
    k = k_ref[...]
    v = v_ref[...]
    up = up_ref[...]
    nt = (((1,), (1,)), ((), ()))
    tn = (((0,), (0,)), ((), ()))
    scores = lax.dot_general(q, k, nt, preferred_element_type=jnp.float32) * scale
    scores = jnp.where(live_ref[...] > 0, scores, NEG_FILL)
    top = jnp.max(scores, axis=-1, keepdims=True)
    raised = jnp.exp(scores - top)
    probs = raised / jnp.sum(raised, axis=-1, keepdims=True)
    probs_b = probs.astype(jnp.bfloat16)
    attn_ref[...] = jnp.dot(probs_b, v, preferred_element_type=jnp.float32).astype(attn_ref.dtype)
    n_local = k.shape[0] - dg_ref.shape[1]
    blk = dg_ref.shape[1] // 2
    dv = lax.dot_general(probs_b, up, tn, preferred_element_type=jnp.float32)
    dg_ref[1] = dv[n_local:]
    dprobs = lax.dot_general(up, v, nt, preferred_element_type=jnp.float32)
    rowdot = jnp.sum(probs * dprobs, axis=-1, keepdims=True)
    dscores = (scale * probs * (dprobs - rowdot)).astype(jnp.bfloat16)
    dq_ref[...] = jnp.dot(dscores, k, preferred_element_type=jnp.float32).astype(dq_ref.dtype)
    dk = lax.dot_general(dscores, q, tn, preferred_element_type=jnp.float32)
    dg_ref[0] = dk[n_local:]
    gk_ref[...] = jnp.zeros_like(gk_ref)
    gv_ref[...] = jnp.zeros_like(gv_ref)
    for j in range(n_local // blk):
        at = pl.ds(pl.multiple_of(ext_ref[j] * blk, blk), blk)
        gk_ref[at, :] += dk[j * blk : (j + 1) * blk]
        gv_ref[at, :] += dv[j * blk : (j + 1) * blk]

def attention(ext, live, q, k, v, up, heads, local_n, ext_n):
    rows, features = q.shape
    keys_n = k.shape[0]
    hd = features // heads
    qspec = pl.BlockSpec((rows, hd), lambda h, e: (0, h))
    kspec = pl.BlockSpec((keys_n, hd), lambda h, e: (0, h))
    espec = pl.BlockSpec((ext_n, hd), lambda h, e: (0, h))
    gspec = pl.BlockSpec((2, keys_n - local_n, hd), lambda h, e: (0, 0, h))
    grid_spec = pltpu.PrefetchScalarGridSpec(
        num_scalar_prefetch=1,
        grid=(heads,),
        in_specs=[pl.BlockSpec((1, keys_n), lambda h, e: (0, 0)), qspec, kspec, kspec, qspec],
        out_specs=[qspec, qspec, espec, espec, gspec],
    )
    return pl.pallas_call(
        _attn_kernel,
        grid_spec=grid_spec,
        out_shape=[
            jax.ShapeDtypeStruct((rows, features), jnp.bfloat16),
            jax.ShapeDtypeStruct((rows, features), jnp.bfloat16),
            jax.ShapeDtypeStruct((ext_n, features), jnp.float32),
            jax.ShapeDtypeStruct((ext_n, features), jnp.float32),
            jax.ShapeDtypeStruct((2, keys_n - local_n, features), jnp.float32),
        ],
    )(ext, live, q, k, v, up)


def local(query, keys, values, out_weight, grad_out, global_blocks, random_blocks):
    tok_rows, feature_count = query.shape
    hd = feature_count // H
    blocks_dev = tok_rows // BLK
    count = lax.axis_size("chip") * lax.axis_size("core")
    total_blocks = blocks_dev * count
    device = flat_index()

    both = lax.all_gather(jnp.concatenate([grad_out, out_weight]), SEQ, axis=0, tiled=False)
    grad_out_all = both[:, : grad_out.shape[0]]
    weight_all = both[:, grad_out.shape[0] :]

    paired = jnp.stack([keys, values])
    before, after = halo(paired)
    extended = jnp.concatenate([before, paired, after], axis=1)

    slots = global_blocks.shape[0]
    owners = global_blocks // blocks_dev
    masked = []
    for g in range(slots):
        start = (global_blocks[g] % blocks_dev) * BLK
        block = lax.dynamic_slice_in_dim(paired, start, BLK, axis=1)
        masked.append(jnp.where(owners[g] == device, block, jnp.zeros_like(block)))
    global_kv = butterfly_sum(jnp.stack(masked))

    local_ids = jnp.arange(blocks_dev, dtype=jnp.int32)
    global_ids = device * blocks_dev + local_ids
    offsets = jnp.array([-1, 0, 1], dtype=jnp.int32)
    neighbour_ids = global_ids[:, None] + offsets[None, :]
    window_index = local_ids[:, None] + blocks_dev + offsets[None, :]
    window_live = (neighbour_ids >= 0) & (neighbour_ids < total_blocks)
    random_index = random_blocks - (device - 1) * blocks_dev
    ext_index = jnp.concatenate([window_index, random_index], axis=1)
    n_local = ext_index.shape[1]
    live = jnp.concatenate(
        [window_live, jnp.ones(random_blocks.shape, jnp.bool_), jnp.ones((blocks_dev, slots), jnp.bool_)],
        axis=1,
    )

    w_rows = out_weight.shape[0]
    upstream_cols = lax.dot_general(
        grad_out_all, out_weight, (((2,), (1,)), ((), ())), preferred_element_type=jnp.float32
    ).astype(jnp.bfloat16)
    upstream = lax.all_to_all(upstream_cols, SEQ, 0, 0, tiled=False)
    upstream = jnp.swapaxes(upstream, 0, 1).reshape(tok_rows, feature_count)

    attn_rows, dq_rows = [], []
    grad_ext = [jnp.zeros((3 * blocks_dev * BLK, feature_count), jnp.float32) for _ in range(2)]
    global_local = None
    for b in range(blocks_dev):
        chosen = []
        for side in range(2):
            parts = [
                lax.dynamic_slice_in_dim(extended[side], ext_index[b, j] * BLK, BLK, axis=0)
                for j in range(n_local)
            ]
            parts += [global_kv[g, side] for g in range(slots)]
            chosen.append(jnp.concatenate(parts, axis=0))
        live_rows = jnp.repeat(live[b], BLK).astype(jnp.float32)[None]
        q = query[b * BLK : (b + 1) * BLK]
        up = upstream[b * BLK : (b + 1) * BLK]
        attn, dq, gk, gv, dg = attention(
            ext_index[b], live_rows, q, chosen[0], chosen[1], up, H, n_local * BLK, 3 * blocks_dev * BLK
        )
        attn_rows.append(attn)
        dq_rows.append(dq)
        grad_ext = [grad_ext[0] + gk, grad_ext[1] + gv]
        terms = dg
        global_local = terms if global_local is None else global_local + terms
    grad_ext = jnp.stack(grad_ext)
    global_total = butterfly_sum(global_local, jnp.bfloat16)

    attn_out = jnp.concatenate(attn_rows, axis=0)
    layer_out = lax.dot_general(
        attn_out.reshape(tok_rows, count, w_rows), weight_all, (((1, 2), (0, 1)), ((), ())),
        preferred_element_type=jnp.float32,
    ).astype(jnp.bfloat16)
    attn_cols = lax.all_to_all(
        attn_out.reshape(tok_rows, count, w_rows), SEQ, 1, 0, tiled=False
    )
    grad_weight = lax.dot_general(
        attn_cols, grad_out_all, (((0, 1), (0, 1)), ((), ())), preferred_element_type=jnp.float32
    )

    rims = jnp.concatenate(
        [grad_ext[:, : blocks_dev * BLK], grad_ext[:, 2 * blocks_dev * BLK :]], axis=1
    ).astype(jnp.bfloat16)
    from_prev, from_next = halo(rims)
    finished = []
    for side in range(2):
        own = grad_ext[side, blocks_dev * BLK : 2 * blocks_dev * BLK]
        own = own + from_prev[side, blocks_dev * BLK :].astype(jnp.float32)
        own = own + from_next[side, : blocks_dev * BLK].astype(jnp.float32)
        for g in range(slots):
            start = (global_blocks[g] % blocks_dev) * BLK
            total = global_total[side, g * BLK : (g + 1) * BLK]
            add = jnp.where(owners[g] == device, total, jnp.zeros_like(total))
            cur = lax.dynamic_slice_in_dim(own, start, BLK, axis=0)
            own = lax.dynamic_update_slice_in_dim(own, cur + add, start, axis=0)
        finished.append(own.astype(jnp.bfloat16))
    grad_query = jnp.concatenate(dq_rows, axis=0)
    return (layer_out, grad_query, finished[0], finished[1], grad_weight)


def solution(mesh):
    groups, seq = mesh.devices.shape
    split = Mesh(mesh.devices.reshape(groups, seq // 2, 2), ("groups",) + SEQ)
    rows = P(("groups",) + SEQ, None)
    placed = (rows, rows, rows, P(SEQ, None), rows, P("groups"), rows)
    return jax.shard_map(
        local,
        mesh=split,
        in_specs=placed,
        out_specs=(rows, rows, rows, rows, rows),
        check_vma=False,
    )
```

```python
import math

import jax
import jax.numpy as jnp
from jax import lax
from jax.experimental import pallas as pl
from jax.experimental.pallas import tpu as pltpu
from jax.sharding import Mesh
from jax.sharding import PartitionSpec as P

H = 8
BLK = 128
SEQ = ("chip", "core")


NEG_FILL = -1e30


def flat_index():
    return lax.axis_index("chip") * lax.axis_size("core") + lax.axis_index("core")


def xor_swap(x, level):
    if level == 0:
        n = lax.axis_size("core")
        return lax.ppermute(x, "core", [(i, i ^ 1) for i in range(n)])
    n = lax.axis_size("chip")
    m = 1 << (level - 1)
    return lax.ppermute(x, "chip", [(i, i ^ m) for i in range(n)])


def butterfly_sum(x, wire=None):
    count = lax.axis_size("chip") * lax.axis_size("core")
    levels = count.bit_length() - 1
    shape = x.shape
    flat = x.reshape(count, -1)
    d = flat_index()
    parts = flat
    for k in range(levels):
        half = parts.shape[0] // 2
        bit = (d >> k) & 1
        send = lax.dynamic_slice_in_dim(parts, (1 - bit) * half, half, axis=0)
        keep = lax.dynamic_slice_in_dim(parts, bit * half, half, axis=0)
        if wire is not None:
            send = send.astype(wire)
        parts = keep + xor_swap(send, k).astype(keep.dtype)
    for k in reversed(range(levels)):
        upper = ((d >> k) & 1) == 1
        if wire is not None and k == levels - 1:
            parts = parts.astype(wire)
        other = xor_swap(parts, k)
        parts = jnp.where(
            upper, jnp.concatenate([other, parts]), jnp.concatenate([parts, other])
        )
    return parts.reshape(shape)


def halo(shard):
    count = lax.axis_size("chip") * lax.axis_size("core")
    up = [(i, i + 1) for i in range(count - 1)]
    down = [(j, i) for i, j in up]
    before = lax.ppermute(shard, SEQ, up)
    after = lax.ppermute(shard, SEQ, down)
    return before, after


def _attn_kernel(ext_ref, live_ref, q_ref, k_ref, v_ref, up_ref, attn_ref, dq_ref, gk_ref, gv_ref, dg_ref):
    scale = 1.0 / math.sqrt(q_ref.shape[-1])
    q = q_ref[...]
    k = k_ref[...]
    v = v_ref[...]
    up = up_ref[...]
    nt = (((1,), (1,)), ((), ()))
    tn = (((0,), (0,)), ((), ()))
    scores = lax.dot_general(q, k, nt, preferred_element_type=jnp.float32) * scale
    scores = jnp.where(live_ref[...] > 0, scores, NEG_FILL)
    top = jnp.max(scores, axis=-1, keepdims=True)
    raised = jnp.exp(scores - top)
    probs = raised / jnp.sum(raised, axis=-1, keepdims=True)
    probs_b = probs.astype(jnp.bfloat16)
    attn_ref[...] = jnp.dot(probs_b, v, preferred_element_type=jnp.float32).astype(attn_ref.dtype)
    n_local = k.shape[0] - dg_ref.shape[1]
    blk = dg_ref.shape[1] // 2
    dv = lax.dot_general(probs_b, up, tn, preferred_element_type=jnp.float32)
    dg_ref[1] = dv[n_local:]
    dprobs = lax.dot_general(up, v, nt, preferred_element_type=jnp.float32)
    rowdot = jnp.sum(probs * dprobs, axis=-1, keepdims=True)
    dscores = (scale * probs * (dprobs - rowdot)).astype(jnp.bfloat16)
    dq_ref[...] = jnp.dot(dscores, k, preferred_element_type=jnp.float32).astype(dq_ref.dtype)
    dk = lax.dot_general(dscores, q, tn, preferred_element_type=jnp.float32)
    dg_ref[0] = dk[n_local:]
    gk_ref[...] = jnp.zeros_like(gk_ref)
    gv_ref[...] = jnp.zeros_like(gv_ref)
    for j in range(n_local // blk):
        at = pl.ds(pl.multiple_of(ext_ref[j] * blk, blk), blk)
        gk_ref[at, :] += dk[j * blk : (j + 1) * blk]
        gv_ref[at, :] += dv[j * blk : (j + 1) * blk]

def attention(ext, live, q, k, v, up, heads, local_n, ext_n):
    rows, features = q.shape
    keys_n = k.shape[0]
    hd = features // heads
    qspec = pl.BlockSpec((rows, hd), lambda h, e: (0, h))
    kspec = pl.BlockSpec((keys_n, hd), lambda h, e: (0, h))
    espec = pl.BlockSpec((ext_n, hd), lambda h, e: (0, h))
    gspec = pl.BlockSpec((2, keys_n - local_n, hd), lambda h, e: (0, 0, h))
    grid_spec = pltpu.PrefetchScalarGridSpec(
        num_scalar_prefetch=1,
        grid=(heads,),
        in_specs=[pl.BlockSpec((1, keys_n), lambda h, e: (0, 0)), qspec, kspec, kspec, qspec],
        out_specs=[qspec, qspec, espec, espec, gspec],
    )
    return pl.pallas_call(
        _attn_kernel,
        grid_spec=grid_spec,
        out_shape=[
            jax.ShapeDtypeStruct((rows, features), jnp.bfloat16),
            jax.ShapeDtypeStruct((rows, features), jnp.bfloat16),
            jax.ShapeDtypeStruct((ext_n, features), jnp.float32),
            jax.ShapeDtypeStruct((ext_n, features), jnp.float32),
            jax.ShapeDtypeStruct((2, keys_n - local_n, features), jnp.float32),
        ],
    )(ext, live, q, k, v, up)


def local(query, keys, values, out_weight, grad_out, global_blocks, random_blocks):
    tok_rows, feature_count = query.shape
    hd = feature_count // H
    blocks_dev = tok_rows // BLK
    count = lax.axis_size("chip") * lax.axis_size("core")
    total_blocks = blocks_dev * count
    device = flat_index()

    grad_out_all = lax.all_gather(grad_out, SEQ, axis=0, tiled=True)
    weight_all = lax.all_gather(out_weight, SEQ, axis=0, tiled=True)

    paired = jnp.stack([keys, values])
    before, after = halo(paired)
    extended = jnp.concatenate([before, paired, after], axis=1)

    slots = global_blocks.shape[0]
    owners = global_blocks // blocks_dev
    masked = []
    for g in range(slots):
        start = (global_blocks[g] % blocks_dev) * BLK
        block = lax.dynamic_slice_in_dim(paired, start, BLK, axis=1)
        masked.append(jnp.where(owners[g] == device, block, jnp.zeros_like(block)))
    global_kv = butterfly_sum(jnp.stack(masked))

    local_ids = jnp.arange(blocks_dev, dtype=jnp.int32)
    global_ids = device * blocks_dev + local_ids
    offsets = jnp.array([-1, 0, 1], dtype=jnp.int32)
    neighbour_ids = global_ids[:, None] + offsets[None, :]
    window_index = local_ids[:, None] + blocks_dev + offsets[None, :]
    window_live = (neighbour_ids >= 0) & (neighbour_ids < total_blocks)
    random_index = random_blocks - (device - 1) * blocks_dev
    ext_index = jnp.concatenate([window_index, random_index], axis=1)
    n_local = ext_index.shape[1]
    live = jnp.concatenate(
        [window_live, jnp.ones(random_blocks.shape, jnp.bool_), jnp.ones((blocks_dev, slots), jnp.bool_)],
        axis=1,
    )

    w_rows = out_weight.shape[0]
    upstream_cols = lax.dot_general(
        grad_out_all, out_weight, (((1,), (1,)), ((), ())), preferred_element_type=jnp.float32
    ).astype(jnp.bfloat16)
    upstream = lax.all_to_all(
        upstream_cols.reshape(count, tok_rows, w_rows), SEQ, 0, 0, tiled=False
    )
    upstream = jnp.swapaxes(upstream, 0, 1).reshape(tok_rows, feature_count)

    attn_rows, dq_rows = [], []
    grad_ext = [jnp.zeros((3 * blocks_dev * BLK, feature_count), jnp.float32) for _ in range(2)]
    global_local = None
    for b in range(blocks_dev):
        chosen = []
        for side in range(2):
            parts = [
                lax.dynamic_slice_in_dim(extended[side], ext_index[b, j] * BLK, BLK, axis=0)
                for j in range(n_local)
            ]
            parts += [global_kv[g, side] for g in range(slots)]
            chosen.append(jnp.concatenate(parts, axis=0))
        live_rows = jnp.repeat(live[b], BLK).astype(jnp.float32)[None]
        q = query[b * BLK : (b + 1) * BLK]
        up = upstream[b * BLK : (b + 1) * BLK]
        attn, dq, gk, gv, dg = attention(
            ext_index[b], live_rows, q, chosen[0], chosen[1], up, H, n_local * BLK, 3 * blocks_dev * BLK
        )
        attn_rows.append(attn)
        dq_rows.append(dq)
        grad_ext = [grad_ext[0] + gk, grad_ext[1] + gv]
        terms = dg
        global_local = terms if global_local is None else global_local + terms
    grad_ext = jnp.stack(grad_ext)
    attn_out = jnp.concatenate(attn_rows, axis=0)
    layer_out = jnp.dot(attn_out, weight_all, preferred_element_type=jnp.float32).astype(
        jnp.bfloat16
    )
    layer_out, global_local = lax.optimization_barrier((layer_out, global_local))
    global_total = butterfly_sum(global_local, jnp.bfloat16)

    attn_cols = lax.all_to_all(
        attn_out.reshape(tok_rows, count, w_rows), SEQ, 1, 0, tiled=False
    ).reshape(count * tok_rows, w_rows)
    grad_weight = lax.dot_general(
        attn_cols, grad_out_all, (((0,), (0,)), ((), ())), preferred_element_type=jnp.float32
    )

    rims = jnp.concatenate(
        [grad_ext[:, : blocks_dev * BLK], grad_ext[:, 2 * blocks_dev * BLK :]], axis=1
    ).astype(jnp.bfloat16)
    from_prev, from_next = halo(rims)
    finished = []
    for side in range(2):
        own = grad_ext[side, blocks_dev * BLK : 2 * blocks_dev * BLK]
        own = own + from_prev[side, blocks_dev * BLK :].astype(jnp.float32)
        own = own + from_next[side, : blocks_dev * BLK].astype(jnp.float32)
        for g in range(slots):
            start = (global_blocks[g] % blocks_dev) * BLK
            total = global_total[side, g * BLK : (g + 1) * BLK]
            add = jnp.where(owners[g] == device, total, jnp.zeros_like(total))
            cur = lax.dynamic_slice_in_dim(own, start, BLK, axis=0)
            own = lax.dynamic_update_slice_in_dim(own, cur + add, start, axis=0)
        finished.append(own.astype(jnp.bfloat16))
    grad_query = jnp.concatenate(dq_rows, axis=0)
    return (layer_out, grad_query, finished[0], finished[1], grad_weight)


def solution(mesh):
    groups, seq = mesh.devices.shape
    split = Mesh(mesh.devices.reshape(groups, seq // 2, 2), ("groups",) + SEQ)
    rows = P(("groups",) + SEQ, None)
    placed = (rows, rows, rows, P(SEQ, None), rows, P("groups"), rows)
    return jax.shard_map(
        local,
        mesh=split,
        in_specs=placed,
        out_specs=(rows, rows, rows, rows, rows),
        check_vma=False,
    )
```

```python
import math

import jax
import jax.numpy as jnp
from jax import lax
from jax.experimental import pallas as pl
from jax.sharding import Mesh
from jax.sharding import PartitionSpec as P

H = 8
BLK = 128
SEQ = ("chip", "core")


NEG_FILL = -1e30


def flat_index():
    return lax.axis_index("chip") * lax.axis_size("core") + lax.axis_index("core")


def xor_swap(x, level):
    if level == 0:
        n = lax.axis_size("core")
        return lax.ppermute(x, "core", [(i, i ^ 1) for i in range(n)])
    n = lax.axis_size("chip")
    m = 1 << (level - 1)
    return lax.ppermute(x, "chip", [(i, i ^ m) for i in range(n)])


def butterfly_sum(x, wire=None):
    count = lax.axis_size("chip") * lax.axis_size("core")
    levels = count.bit_length() - 1
    shape = x.shape
    flat = x.reshape(count, -1)
    d = flat_index()
    parts = flat
    for k in range(levels):
        half = parts.shape[0] // 2
        bit = (d >> k) & 1
        send = lax.dynamic_slice_in_dim(parts, (1 - bit) * half, half, axis=0)
        keep = lax.dynamic_slice_in_dim(parts, bit * half, half, axis=0)
        if wire is not None:
            send = send.astype(wire)
        parts = keep + xor_swap(send, k).astype(keep.dtype)
    for k in reversed(range(levels)):
        upper = ((d >> k) & 1) == 1
        if wire is not None and k == levels - 1:
            parts = parts.astype(wire)
        other = xor_swap(parts, k)
        parts = jnp.where(
            upper, jnp.concatenate([other, parts]), jnp.concatenate([parts, other])
        )
    return parts.reshape(shape)


def halo(shard):
    count = lax.axis_size("chip") * lax.axis_size("core")
    up = [(i, i + 1) for i in range(count - 1)]
    down = [(j, i) for i, j in up]
    before = lax.ppermute(shard, SEQ, up)
    after = lax.ppermute(shard, SEQ, down)
    return before, after


def _attn_kernel(live_ref, q_ref, k_ref, v_ref, up_ref, attn_ref, dq_ref, dk_ref, dv_ref, dg_ref):
    scale = 1.0 / math.sqrt(q_ref.shape[-1])
    q = q_ref[...]
    k = k_ref[...]
    v = v_ref[...]
    up = up_ref[...]
    nt = (((1,), (1,)), ((), ()))
    tn = (((0,), (0,)), ((), ()))
    scores = lax.dot_general(q, k, nt, preferred_element_type=jnp.float32) * scale
    scores = jnp.where(live_ref[...] > 0, scores, NEG_FILL)
    top = jnp.max(scores, axis=-1, keepdims=True)
    raised = jnp.exp(scores - top)
    probs = raised / jnp.sum(raised, axis=-1, keepdims=True)
    probs_b = probs.astype(jnp.bfloat16)
    attn_ref[...] = jnp.dot(probs_b, v, preferred_element_type=jnp.float32).astype(attn_ref.dtype)
    n_local = dk_ref.shape[0]
    dv = lax.dot_general(probs_b, up, tn, preferred_element_type=jnp.float32)
    dv_ref[...] = dv[:n_local]
    dg_ref[1] = dv[n_local:]
    dprobs = lax.dot_general(up, v, nt, preferred_element_type=jnp.float32)
    rowdot = jnp.sum(probs * dprobs, axis=-1, keepdims=True)
    dscores = (scale * probs * (dprobs - rowdot)).astype(jnp.bfloat16)
    dq_ref[...] = jnp.dot(dscores, k, preferred_element_type=jnp.float32).astype(dq_ref.dtype)
    dk = lax.dot_general(dscores, q, tn, preferred_element_type=jnp.float32)
    dk_ref[...] = dk[:n_local]
    dg_ref[0] = dk[n_local:]

def attention(live, q, k, v, up, heads, local_n):
    rows, features = q.shape
    keys_n = k.shape[0]
    hd = features // heads
    qspec = pl.BlockSpec((rows, hd), lambda h: (0, h))
    kspec = pl.BlockSpec((keys_n, hd), lambda h: (0, h))
    lspec = pl.BlockSpec((local_n, hd), lambda h: (0, h))
    gspec = pl.BlockSpec((2, keys_n - local_n, hd), lambda h: (0, 0, h))
    return pl.pallas_call(
        _attn_kernel,
        grid=(heads,),
        in_specs=[pl.BlockSpec((1, keys_n), lambda h: (0, 0)), qspec, kspec, kspec, qspec],
        out_specs=[qspec, qspec, lspec, lspec, gspec],
        out_shape=[
            jax.ShapeDtypeStruct((rows, features), jnp.bfloat16),
            jax.ShapeDtypeStruct((rows, features), jnp.bfloat16),
            jax.ShapeDtypeStruct((local_n, features), jnp.float32),
            jax.ShapeDtypeStruct((local_n, features), jnp.float32),
            jax.ShapeDtypeStruct((2, keys_n - local_n, features), jnp.float32),
        ],
    )(live, q, k, v, up)


def local(query, keys, values, out_weight, grad_out, global_blocks, random_blocks):
    tok_rows, feature_count = query.shape
    hd = feature_count // H
    blocks_dev = tok_rows // BLK
    count = lax.axis_size("chip") * lax.axis_size("core")
    total_blocks = blocks_dev * count
    device = flat_index()

    grad_out_all = lax.all_gather(grad_out, SEQ, axis=0, tiled=True)
    weight_all = lax.all_gather(out_weight, SEQ, axis=0, tiled=True)

    paired = jnp.stack([keys, values])
    before, after = halo(paired)
    extended = jnp.concatenate([before, paired, after], axis=1)

    slots = global_blocks.shape[0]
    owners = global_blocks // blocks_dev
    masked = []
    for g in range(slots):
        start = (global_blocks[g] % blocks_dev) * BLK
        block = lax.dynamic_slice_in_dim(paired, start, BLK, axis=1)
        masked.append(jnp.where(owners[g] == device, block, jnp.zeros_like(block)))
    global_kv = butterfly_sum(jnp.stack(masked))

    local_ids = jnp.arange(blocks_dev, dtype=jnp.int32)
    global_ids = device * blocks_dev + local_ids
    offsets = jnp.array([-1, 0, 1], dtype=jnp.int32)
    neighbour_ids = global_ids[:, None] + offsets[None, :]
    window_index = local_ids[:, None] + blocks_dev + offsets[None, :]
    window_live = (neighbour_ids >= 0) & (neighbour_ids < total_blocks)
    random_index = random_blocks - (device - 1) * blocks_dev
    ext_index = jnp.concatenate([window_index, random_index], axis=1)
    n_local = ext_index.shape[1]
    live = jnp.concatenate(
        [window_live, jnp.ones(random_blocks.shape, jnp.bool_), jnp.ones((blocks_dev, slots), jnp.bool_)],
        axis=1,
    )

    w_rows = out_weight.shape[0]
    upstream_cols = lax.dot_general(
        grad_out_all, out_weight, (((1,), (1,)), ((), ())), preferred_element_type=jnp.float32
    ).astype(jnp.bfloat16)
    upstream = lax.all_to_all(
        upstream_cols.reshape(count, tok_rows, w_rows), SEQ, 0, 0, tiled=False
    )
    upstream = jnp.swapaxes(upstream, 0, 1).reshape(tok_rows, feature_count)

    attn_rows, dq_rows = [], []
    grad_ext = [jnp.zeros((3 * blocks_dev * BLK, feature_count), jnp.float32) for _ in range(2)]
    global_local = None
    for b in range(blocks_dev):
        chosen = []
        for side in range(2):
            parts = [
                lax.dynamic_slice_in_dim(extended[side], ext_index[b, j] * BLK, BLK, axis=0)
                for j in range(n_local)
            ]
            parts += [global_kv[g, side] for g in range(slots)]
            chosen.append(jnp.concatenate(parts, axis=0))
        live_rows = jnp.repeat(live[b], BLK).astype(jnp.float32)[None]
        q = query[b * BLK : (b + 1) * BLK]
        up = upstream[b * BLK : (b + 1) * BLK]
        attn, dq, dk, dv, dg = attention(live_rows, q, chosen[0], chosen[1], up, H, n_local * BLK)
        attn_rows.append(attn)
        dq_rows.append(dq)
        for side, grad in enumerate((dk, dv)):
            for j in range(n_local):
                start = ext_index[b, j] * BLK
                cur = lax.dynamic_slice_in_dim(grad_ext[side], start, BLK, axis=0)
                term = grad[j * BLK : (j + 1) * BLK]
                grad_ext[side] = lax.dynamic_update_slice_in_dim(
                    grad_ext[side], cur + term, start, axis=0
                )
        terms = dg
        global_local = terms if global_local is None else global_local + terms
    grad_ext = jnp.stack(grad_ext)
    attn_out = jnp.concatenate(attn_rows, axis=0)
    attn_cols = lax.all_to_all(
        attn_out.reshape(tok_rows, count, w_rows), SEQ, 1, 0, tiled=False
    ).reshape(count * tok_rows, w_rows)
    attn_cols, global_local = lax.optimization_barrier((attn_cols, global_local))
    global_total = butterfly_sum(global_local, jnp.bfloat16)

    layer_out = jnp.dot(attn_out, weight_all, preferred_element_type=jnp.float32).astype(
        jnp.bfloat16
    )
    grad_weight = lax.dot_general(
        attn_cols, grad_out_all, (((0,), (0,)), ((), ())), preferred_element_type=jnp.float32
    )

    rims = jnp.concatenate(
        [grad_ext[:, : blocks_dev * BLK], grad_ext[:, 2 * blocks_dev * BLK :]], axis=1
    ).astype(jnp.bfloat16)
    from_prev, from_next = halo(rims)
    finished = []
    for side in range(2):
        own = grad_ext[side, blocks_dev * BLK : 2 * blocks_dev * BLK]
        own = own + from_prev[side, blocks_dev * BLK :].astype(jnp.float32)
        own = own + from_next[side, : blocks_dev * BLK].astype(jnp.float32)
        for g in range(slots):
            start = (global_blocks[g] % blocks_dev) * BLK
            total = global_total[side, g * BLK : (g + 1) * BLK]
            add = jnp.where(owners[g] == device, total, jnp.zeros_like(total))
            cur = lax.dynamic_slice_in_dim(own, start, BLK, axis=0)
            own = lax.dynamic_update_slice_in_dim(own, cur + add, start, axis=0)
        finished.append(own.astype(jnp.bfloat16))
    grad_query = jnp.concatenate(dq_rows, axis=0)
    return (layer_out, grad_query, finished[0], finished[1], grad_weight)


def solution(mesh):
    groups, seq = mesh.devices.shape
    split = Mesh(mesh.devices.reshape(groups, seq // 2, 2), ("groups",) + SEQ)
    rows = P(("groups",) + SEQ, None)
    placed = (rows, rows, rows, P(SEQ, None), rows, P("groups"), rows)
    return jax.shard_map(
        local,
        mesh=split,
        in_specs=placed,
        out_specs=(rows, rows, rows, rows, rows),
        check_vma=False,
    )
```

```python
import math

import jax
import jax.numpy as jnp
from jax import lax
from jax.experimental import pallas as pl
from jax.sharding import Mesh
from jax.sharding import PartitionSpec as P

H = 8
BLK = 128
SEQ = ("chip", "core")


NEG_FILL = -1e30


def flat_index():
    return lax.axis_index("chip") * lax.axis_size("core") + lax.axis_index("core")


def xor_swap(x, level):
    if level == 0:
        n = lax.axis_size("core")
        return lax.ppermute(x, "core", [(i, i ^ 1) for i in range(n)])
    n = lax.axis_size("chip")
    m = 1 << (level - 1)
    return lax.ppermute(x, "chip", [(i, i ^ m) for i in range(n)])


def butterfly_sum(x, wire=None):
    count = lax.axis_size("chip") * lax.axis_size("core")
    levels = count.bit_length() - 1
    shape = x.shape
    flat = x.reshape(count, -1)
    d = flat_index()
    parts = flat
    for k in range(levels):
        half = parts.shape[0] // 2
        bit = (d >> k) & 1
        send = lax.dynamic_slice_in_dim(parts, (1 - bit) * half, half, axis=0)
        keep = lax.dynamic_slice_in_dim(parts, bit * half, half, axis=0)
        if wire is not None:
            send = send.astype(wire)
        parts = keep + xor_swap(send, k).astype(keep.dtype)
    for k in reversed(range(levels)):
        upper = ((d >> k) & 1) == 1
        if wire is not None and k == levels - 1:
            parts = parts.astype(wire)
        other = xor_swap(parts, k)
        parts = jnp.where(
            upper, jnp.concatenate([other, parts]), jnp.concatenate([parts, other])
        )
    return parts.reshape(shape)


def halo(shard):
    count = lax.axis_size("chip") * lax.axis_size("core")
    up = [(i, i + 1) for i in range(count - 1)]
    down = [(j, i) for i, j in up]
    before = lax.ppermute(shard, SEQ, up)
    after = lax.ppermute(shard, SEQ, down)
    return before, after


def _attn_kernel(live_ref, q_ref, k_ref, v_ref, up_ref, attn_ref, dq_ref, dk_ref, dv_ref, dg_ref):
    width = q_ref.shape[-1] // 2
    for i in range(2):
        cols = slice(i * width, (i + 1) * width)
        _one_head(live_ref, q_ref, k_ref, v_ref, up_ref, attn_ref, dq_ref, dk_ref, dv_ref, dg_ref, cols)


def _one_head(live_ref, q_ref, k_ref, v_ref, up_ref, attn_ref, dq_ref, dk_ref, dv_ref, dg_ref, cols):
    q = q_ref[:, cols]
    k = k_ref[:, cols]
    v = v_ref[:, cols]
    up = up_ref[:, cols]
    scale = 1.0 / math.sqrt(q.shape[-1])
    nt = (((1,), (1,)), ((), ()))
    tn = (((0,), (0,)), ((), ()))
    scores = lax.dot_general(q, k, nt, preferred_element_type=jnp.float32) * scale
    scores = jnp.where(live_ref[...] > 0, scores, NEG_FILL)
    top = jnp.max(scores, axis=-1, keepdims=True)
    raised = jnp.exp(scores - top)
    probs = raised / jnp.sum(raised, axis=-1, keepdims=True)
    probs_b = probs.astype(jnp.bfloat16)
    attn_ref[:, cols] = jnp.dot(probs_b, v, preferred_element_type=jnp.float32).astype(attn_ref.dtype)
    n_local = dk_ref.shape[0]
    dv = lax.dot_general(probs_b, up, tn, preferred_element_type=jnp.float32)
    dv_ref[:, cols] = dv[:n_local]
    dg_ref[1, :, cols] = dv[n_local:]
    dprobs = lax.dot_general(up, v, nt, preferred_element_type=jnp.float32)
    rowdot = jnp.sum(probs * dprobs, axis=-1, keepdims=True)
    dscores = (scale * probs * (dprobs - rowdot)).astype(jnp.bfloat16)
    dq_ref[:, cols] = jnp.dot(dscores, k, preferred_element_type=jnp.float32).astype(dq_ref.dtype)
    dk = lax.dot_general(dscores, q, tn, preferred_element_type=jnp.float32)
    dk_ref[:, cols] = dk[:n_local]
    dg_ref[0, :, cols] = dk[n_local:]

def attention(live, q, k, v, up, heads, local_n):
    rows, features = q.shape
    keys_n = k.shape[0]
    hd = 2 * features // heads
    qspec = pl.BlockSpec((rows, hd), lambda h: (0, h))
    kspec = pl.BlockSpec((keys_n, hd), lambda h: (0, h))
    lspec = pl.BlockSpec((local_n, hd), lambda h: (0, h))
    gspec = pl.BlockSpec((2, keys_n - local_n, hd), lambda h: (0, 0, h))
    return pl.pallas_call(
        _attn_kernel,
        grid=(heads // 2,),
        in_specs=[pl.BlockSpec((1, keys_n), lambda h: (0, 0)), qspec, kspec, kspec, qspec],
        out_specs=[qspec, qspec, lspec, lspec, gspec],
        out_shape=[
            jax.ShapeDtypeStruct((rows, features), jnp.bfloat16),
            jax.ShapeDtypeStruct((rows, features), jnp.bfloat16),
            jax.ShapeDtypeStruct((local_n, features), jnp.float32),
            jax.ShapeDtypeStruct((local_n, features), jnp.float32),
            jax.ShapeDtypeStruct((2, keys_n - local_n, features), jnp.float32),
        ],
    )(live, q, k, v, up)


def local(query, keys, values, out_weight, grad_out, global_blocks, random_blocks):
    tok_rows, feature_count = query.shape
    hd = feature_count // H
    blocks_dev = tok_rows // BLK
    count = lax.axis_size("chip") * lax.axis_size("core")
    total_blocks = blocks_dev * count
    device = flat_index()

    grad_out_all = lax.all_gather(grad_out, SEQ, axis=0, tiled=True)
    weight_all = lax.all_gather(out_weight, SEQ, axis=0, tiled=True)

    paired = jnp.stack([keys, values])
    before, after = halo(paired)
    extended = jnp.concatenate([before, paired, after], axis=1)

    slots = global_blocks.shape[0]
    owners = global_blocks // blocks_dev
    masked = []
    for g in range(slots):
        start = (global_blocks[g] % blocks_dev) * BLK
        block = lax.dynamic_slice_in_dim(paired, start, BLK, axis=1)
        masked.append(jnp.where(owners[g] == device, block, jnp.zeros_like(block)))
    global_kv = butterfly_sum(jnp.stack(masked))

    local_ids = jnp.arange(blocks_dev, dtype=jnp.int32)
    global_ids = device * blocks_dev + local_ids
    offsets = jnp.array([-1, 0, 1], dtype=jnp.int32)
    neighbour_ids = global_ids[:, None] + offsets[None, :]
    window_index = local_ids[:, None] + blocks_dev + offsets[None, :]
    window_live = (neighbour_ids >= 0) & (neighbour_ids < total_blocks)
    random_index = random_blocks - (device - 1) * blocks_dev
    ext_index = jnp.concatenate([window_index, random_index], axis=1)
    n_local = ext_index.shape[1]
    live = jnp.concatenate(
        [window_live, jnp.ones(random_blocks.shape, jnp.bool_), jnp.ones((blocks_dev, slots), jnp.bool_)],
        axis=1,
    )

    w_rows = out_weight.shape[0]
    upstream_cols = lax.dot_general(
        grad_out_all, out_weight, (((1,), (1,)), ((), ())), preferred_element_type=jnp.float32
    ).astype(jnp.bfloat16)
    upstream = lax.all_to_all(
        upstream_cols.reshape(count, tok_rows, w_rows), SEQ, 0, 0, tiled=False
    )
    upstream = jnp.swapaxes(upstream, 0, 1).reshape(tok_rows, feature_count)

    attn_rows, dq_rows = [], []
    grad_ext = [jnp.zeros((3 * blocks_dev * BLK, feature_count), jnp.float32) for _ in range(2)]
    global_local = None
    for b in range(blocks_dev):
        chosen = []
        for side in range(2):
            parts = [
                lax.dynamic_slice_in_dim(extended[side], ext_index[b, j] * BLK, BLK, axis=0)
                for j in range(n_local)
            ]
            parts += [global_kv[g, side] for g in range(slots)]
            chosen.append(jnp.concatenate(parts, axis=0))
        live_rows = jnp.repeat(live[b], BLK).astype(jnp.float32)[None]
        q = query[b * BLK : (b + 1) * BLK]
        up = upstream[b * BLK : (b + 1) * BLK]
        attn, dq, dk, dv, dg = attention(live_rows, q, chosen[0], chosen[1], up, H, n_local * BLK)
        attn_rows.append(attn)
        dq_rows.append(dq)
        for side, grad in enumerate((dk, dv)):
            for j in range(n_local):
                start = ext_index[b, j] * BLK
                cur = lax.dynamic_slice_in_dim(grad_ext[side], start, BLK, axis=0)
                term = grad[j * BLK : (j + 1) * BLK]
                grad_ext[side] = lax.dynamic_update_slice_in_dim(
                    grad_ext[side], cur + term, start, axis=0
                )
        terms = dg
        global_local = terms if global_local is None else global_local + terms
    grad_ext = jnp.stack(grad_ext)
    global_total = butterfly_sum(global_local, jnp.bfloat16)

    attn_out = jnp.concatenate(attn_rows, axis=0)
    layer_out = jnp.dot(attn_out, weight_all, preferred_element_type=jnp.float32).astype(
        jnp.bfloat16
    )
    attn_cols = lax.all_to_all(
        attn_out.reshape(tok_rows, count, w_rows), SEQ, 1, 0, tiled=False
    ).reshape(count * tok_rows, w_rows)
    grad_weight = lax.dot_general(
        attn_cols, grad_out_all, (((0,), (0,)), ((), ())), preferred_element_type=jnp.float32
    )

    rims = jnp.concatenate(
        [grad_ext[:, : blocks_dev * BLK], grad_ext[:, 2 * blocks_dev * BLK :]], axis=1
    ).astype(jnp.bfloat16)
    from_prev, from_next = halo(rims)
    finished = []
    for side in range(2):
        own = grad_ext[side, blocks_dev * BLK : 2 * blocks_dev * BLK]
        own = own + from_prev[side, blocks_dev * BLK :].astype(jnp.float32)
        own = own + from_next[side, : blocks_dev * BLK].astype(jnp.float32)
        for g in range(slots):
            start = (global_blocks[g] % blocks_dev) * BLK
            total = global_total[side, g * BLK : (g + 1) * BLK]
            add = jnp.where(owners[g] == device, total, jnp.zeros_like(total))
            cur = lax.dynamic_slice_in_dim(own, start, BLK, axis=0)
            own = lax.dynamic_update_slice_in_dim(own, cur + add, start, axis=0)
        finished.append(own.astype(jnp.bfloat16))
    grad_query = jnp.concatenate(dq_rows, axis=0)
    return (layer_out, grad_query, finished[0], finished[1], grad_weight)


def solution(mesh):
    groups, seq = mesh.devices.shape
    split = Mesh(mesh.devices.reshape(groups, seq // 2, 2), ("groups",) + SEQ)
    rows = P(("groups",) + SEQ, None)
    placed = (rows, rows, rows, P(SEQ, None), rows, P("groups"), rows)
    return jax.shard_map(
        local,
        mesh=split,
        in_specs=placed,
        out_specs=(rows, rows, rows, rows, rows),
        check_vma=False,
    )
```

```python
import math

import jax
import jax.numpy as jnp
from jax import lax
from jax.experimental import pallas as pl
from jax.sharding import Mesh
from jax.sharding import PartitionSpec as P

H = 8
BLK = 128
SEQ = ("chip", "core")


NEG_FILL = -1e30


def flat_index():
    return lax.axis_index("chip") * lax.axis_size("core") + lax.axis_index("core")


def xor_swap(x, level):
    if level == 0:
        n = lax.axis_size("core")
        return lax.ppermute(x, "core", [(i, i ^ 1) for i in range(n)])
    n = lax.axis_size("chip")
    m = 1 << (level - 1)
    return lax.ppermute(x, "chip", [(i, i ^ m) for i in range(n)])


def butterfly_sum(x, wire=None):
    count = lax.axis_size("chip") * lax.axis_size("core")
    levels = count.bit_length() - 1
    shape = x.shape
    flat = x.reshape(count, -1)
    d = flat_index()
    parts = flat
    for k in range(levels):
        half = parts.shape[0] // 2
        bit = (d >> k) & 1
        send = lax.dynamic_slice_in_dim(parts, (1 - bit) * half, half, axis=0)
        keep = lax.dynamic_slice_in_dim(parts, bit * half, half, axis=0)
        if wire is not None:
            send = send.astype(wire)
        parts = keep + xor_swap(send, k).astype(keep.dtype)
    for k in reversed(range(levels)):
        upper = ((d >> k) & 1) == 1
        if wire is not None and k == levels - 1:
            parts = parts.astype(wire)
        other = xor_swap(parts, k)
        parts = jnp.where(
            upper, jnp.concatenate([other, parts]), jnp.concatenate([parts, other])
        )
    return parts.reshape(shape)


def halo(shard):
    count = lax.axis_size("chip") * lax.axis_size("core")
    up = [(i, i + 1) for i in range(count - 1)]
    down = [(j, i) for i, j in up]
    before = lax.ppermute(shard, SEQ, up)
    after = lax.ppermute(shard, SEQ, down)
    return before, after


def _attn_kernel(live_ref, q_ref, k_ref, v_ref, up_ref, attn_ref, dq_ref, dk_ref, dv_ref, dg_ref):
    width = q_ref.shape[-1] // 4
    for i in range(4):
        cols = slice(i * width, (i + 1) * width)
        _one_head(live_ref, q_ref, k_ref, v_ref, up_ref, attn_ref, dq_ref, dk_ref, dv_ref, dg_ref, cols)


def _one_head(live_ref, q_ref, k_ref, v_ref, up_ref, attn_ref, dq_ref, dk_ref, dv_ref, dg_ref, cols):
    q = q_ref[:, cols]
    k = k_ref[:, cols]
    v = v_ref[:, cols]
    up = up_ref[:, cols]
    scale = 1.0 / math.sqrt(q.shape[-1])
    nt = (((1,), (1,)), ((), ()))
    tn = (((0,), (0,)), ((), ()))
    scores = lax.dot_general(q, k, nt, preferred_element_type=jnp.float32) * scale
    scores = jnp.where(live_ref[...] > 0, scores, NEG_FILL)
    top = jnp.max(scores, axis=-1, keepdims=True)
    raised = jnp.exp(scores - top)
    probs = raised / jnp.sum(raised, axis=-1, keepdims=True)
    probs_b = probs.astype(jnp.bfloat16)
    attn_ref[:, cols] = jnp.dot(probs_b, v, preferred_element_type=jnp.float32).astype(attn_ref.dtype)
    n_local = dk_ref.shape[0]
    dv = lax.dot_general(probs_b, up, tn, preferred_element_type=jnp.float32)
    dv_ref[:, cols] = dv[:n_local]
    dg_ref[1, :, cols] = dv[n_local:]
    dprobs = lax.dot_general(up, v, nt, preferred_element_type=jnp.float32)
    rowdot = jnp.sum(probs * dprobs, axis=-1, keepdims=True)
    dscores = (scale * probs * (dprobs - rowdot)).astype(jnp.bfloat16)
    dq_ref[:, cols] = jnp.dot(dscores, k, preferred_element_type=jnp.float32).astype(dq_ref.dtype)
    dk = lax.dot_general(dscores, q, tn, preferred_element_type=jnp.float32)
    dk_ref[:, cols] = dk[:n_local]
    dg_ref[0, :, cols] = dk[n_local:]

def attention(live, q, k, v, up, heads, local_n):
    rows, features = q.shape
    keys_n = k.shape[0]
    hd = 4 * features // heads
    qspec = pl.BlockSpec((rows, hd), lambda h: (0, h))
    kspec = pl.BlockSpec((keys_n, hd), lambda h: (0, h))
    lspec = pl.BlockSpec((local_n, hd), lambda h: (0, h))
    gspec = pl.BlockSpec((2, keys_n - local_n, hd), lambda h: (0, 0, h))
    return pl.pallas_call(
        _attn_kernel,
        grid=(heads // 4,),
        in_specs=[pl.BlockSpec((1, keys_n), lambda h: (0, 0)), qspec, kspec, kspec, qspec],
        out_specs=[qspec, qspec, lspec, lspec, gspec],
        out_shape=[
            jax.ShapeDtypeStruct((rows, features), jnp.bfloat16),
            jax.ShapeDtypeStruct((rows, features), jnp.bfloat16),
            jax.ShapeDtypeStruct((local_n, features), jnp.float32),
            jax.ShapeDtypeStruct((local_n, features), jnp.float32),
            jax.ShapeDtypeStruct((2, keys_n - local_n, features), jnp.float32),
        ],
    )(live, q, k, v, up)


def local(query, keys, values, out_weight, grad_out, global_blocks, random_blocks):
    tok_rows, feature_count = query.shape
    hd = feature_count // H
    blocks_dev = tok_rows // BLK
    count = lax.axis_size("chip") * lax.axis_size("core")
    total_blocks = blocks_dev * count
    device = flat_index()

    grad_out_all = lax.all_gather(grad_out, SEQ, axis=0, tiled=True)
    weight_all = lax.all_gather(out_weight, SEQ, axis=0, tiled=True)

    paired = jnp.stack([keys, values])
    before, after = halo(paired)
    extended = jnp.concatenate([before, paired, after], axis=1)

    slots = global_blocks.shape[0]
    owners = global_blocks // blocks_dev
    masked = []
    for g in range(slots):
        start = (global_blocks[g] % blocks_dev) * BLK
        block = lax.dynamic_slice_in_dim(paired, start, BLK, axis=1)
        masked.append(jnp.where(owners[g] == device, block, jnp.zeros_like(block)))
    global_kv = butterfly_sum(jnp.stack(masked))

    local_ids = jnp.arange(blocks_dev, dtype=jnp.int32)
    global_ids = device * blocks_dev + local_ids
    offsets = jnp.array([-1, 0, 1], dtype=jnp.int32)
    neighbour_ids = global_ids[:, None] + offsets[None, :]
    window_index = local_ids[:, None] + blocks_dev + offsets[None, :]
    window_live = (neighbour_ids >= 0) & (neighbour_ids < total_blocks)
    random_index = random_blocks - (device - 1) * blocks_dev
    ext_index = jnp.concatenate([window_index, random_index], axis=1)
    n_local = ext_index.shape[1]
    live = jnp.concatenate(
        [window_live, jnp.ones(random_blocks.shape, jnp.bool_), jnp.ones((blocks_dev, slots), jnp.bool_)],
        axis=1,
    )

    w_rows = out_weight.shape[0]
    upstream_cols = lax.dot_general(
        grad_out_all, out_weight, (((1,), (1,)), ((), ())), preferred_element_type=jnp.float32
    ).astype(jnp.bfloat16)
    upstream = lax.all_to_all(
        upstream_cols.reshape(count, tok_rows, w_rows), SEQ, 0, 0, tiled=False
    )
    upstream = jnp.swapaxes(upstream, 0, 1).reshape(tok_rows, feature_count)

    attn_rows, dq_rows = [], []
    grad_ext = [jnp.zeros((3 * blocks_dev * BLK, feature_count), jnp.float32) for _ in range(2)]
    global_local = None
    for b in range(blocks_dev):
        chosen = []
        for side in range(2):
            parts = [
                lax.dynamic_slice_in_dim(extended[side], ext_index[b, j] * BLK, BLK, axis=0)
                for j in range(n_local)
            ]
            parts += [global_kv[g, side] for g in range(slots)]
            chosen.append(jnp.concatenate(parts, axis=0))
        live_rows = jnp.repeat(live[b], BLK).astype(jnp.float32)[None]
        q = query[b * BLK : (b + 1) * BLK]
        up = upstream[b * BLK : (b + 1) * BLK]
        attn, dq, dk, dv, dg = attention(live_rows, q, chosen[0], chosen[1], up, H, n_local * BLK)
        attn_rows.append(attn)
        dq_rows.append(dq)
        for side, grad in enumerate((dk, dv)):
            for j in range(n_local):
                start = ext_index[b, j] * BLK
                cur = lax.dynamic_slice_in_dim(grad_ext[side], start, BLK, axis=0)
                term = grad[j * BLK : (j + 1) * BLK]
                grad_ext[side] = lax.dynamic_update_slice_in_dim(
                    grad_ext[side], cur + term, start, axis=0
                )
        terms = dg
        global_local = terms if global_local is None else global_local + terms
    grad_ext = jnp.stack(grad_ext)
    global_total = butterfly_sum(global_local, jnp.bfloat16)

    attn_out = jnp.concatenate(attn_rows, axis=0)
    layer_out = jnp.dot(attn_out, weight_all, preferred_element_type=jnp.float32).astype(
        jnp.bfloat16
    )
    attn_cols = lax.all_to_all(
        attn_out.reshape(tok_rows, count, w_rows), SEQ, 1, 0, tiled=False
    ).reshape(count * tok_rows, w_rows)
    grad_weight = lax.dot_general(
        attn_cols, grad_out_all, (((0,), (0,)), ((), ())), preferred_element_type=jnp.float32
    )

    rims = jnp.concatenate(
        [grad_ext[:, : blocks_dev * BLK], grad_ext[:, 2 * blocks_dev * BLK :]], axis=1
    ).astype(jnp.bfloat16)
    from_prev, from_next = halo(rims)
    finished = []
    for side in range(2):
        own = grad_ext[side, blocks_dev * BLK : 2 * blocks_dev * BLK]
        own = own + from_prev[side, blocks_dev * BLK :].astype(jnp.float32)
        own = own + from_next[side, : blocks_dev * BLK].astype(jnp.float32)
        for g in range(slots):
            start = (global_blocks[g] % blocks_dev) * BLK
            total = global_total[side, g * BLK : (g + 1) * BLK]
            add = jnp.where(owners[g] == device, total, jnp.zeros_like(total))
            cur = lax.dynamic_slice_in_dim(own, start, BLK, axis=0)
            own = lax.dynamic_update_slice_in_dim(own, cur + add, start, axis=0)
        finished.append(own.astype(jnp.bfloat16))
    grad_query = jnp.concatenate(dq_rows, axis=0)
    return (layer_out, grad_query, finished[0], finished[1], grad_weight)


def solution(mesh):
    groups, seq = mesh.devices.shape
    split = Mesh(mesh.devices.reshape(groups, seq // 2, 2), ("groups",) + SEQ)
    rows = P(("groups",) + SEQ, None)
    placed = (rows, rows, rows, P(SEQ, None), rows, P("groups"), rows)
    return jax.shard_map(
        local,
        mesh=split,
        in_specs=placed,
        out_specs=(rows, rows, rows, rows, rows),
        check_vma=False,
    )
```
